128 devices in a mesh: seq: 32 (over x, y_hi, z), mp: 4 (over y_lo, core).
Axes of the slice: x: 4, y: 4 (y_hi: 2, y_lo: 2; y = y_hi * 2 + y_lo), z: 4, core: 2. Of those that a mesh axis runs over, the one named last changes fastest.
Arguments:
- hidden_in: bfloat16 [8192, 1536], P('seq', 'mp'), may hold values from -6 to 6
- wq: bfloat16 [1536, 1536], P('seq', 'mp'), may hold values from -1 to 1
- wkv: bfloat16 [1536, 512], P('seq'), may hold values from -0.15625 to 0.15625
- wo: bfloat16 [1536, 1536], P('mp', 'seq'), may hold values from -0.15625 to 0.15625
- lengths: int32 [3], replicated, may hold values from 1 to 6144, 8192 in all
- routes: int32 [8192, 4], P('seq'), may hold values from 0 to 31, all different within a row; in each aligned block of 256 rows (0 to 255, 256 to 511, ...) at most 64 rows name the same one
- gate_logits: float32 [8192, 4], P('seq'), may hold values from -6 to 6
- expert_gate: bfloat16 [32, 768, 1536], P('seq', 'mp'), may hold values from -0.15625 to 0.15625
- expert_up: bfloat16 [32, 768, 1536], P('seq', 'mp'), may hold values from -0.15625 to 0.15625
- expert_down: bfloat16 [32, 768, 1536], P('seq', 'mp'), may hold values from -0.21875 to 0.21875
Outputs:
- layer_out: bfloat16 [8192, 1536], P('seq', 'mp')
The draws below stay inside these ranges and needn't reach their ends.
Inputs may be any that keep to these rules, and one draw needn't show every extreme that they name: `lengths`: sum to 8192; the longest is exactly 6144. `routes`: a token's 4 experts differ; among the rows of one device no expert is named more than 64 times, a bound that some block reaches.
All inputs are finite; a program needn't handle non-finite values.
Results may differ from the reference program's by a relative error of at most 0.018.
Values may be sent and summed in bfloat16 or wider, within the bound.
No kernel may reach another device: no remote copies, remote signals or barrier semaphores. Data moves between devices by JAX's collectives and lax.ppermute only.
A program may use at most 128 MiB of HBM per device.

```python
import math
import jax
import jax.numpy as jnp
import numpy as np
from jax import lax

D = 1536
HQ = 12
KVH = 2
HD = 128
FFE = 768
TOP = 4
WINDOW = 4096
TOK_DEV = 256
TOKENS = 8192
EXPERTS = 32
CAP = 64
N_SEQ = 32


def draw_wq(key, part):
    base = jax.random.truncated_normal(key, -4.0, 4.0, (D, HQ * HD), jnp.float32) * D ** (-0.5)
    return jnp.clip(base, -1.0, 1.0).astype(jnp.bfloat16)


def block_scale(stream_key, shape, split, least, high):
    factor_of, own = 1.0, jax.random.fold_in(stream_key, 6)
    for dim, parts in split:
        draws = jnp.exp(jax.random.uniform(jax.random.fold_in(own, dim), (parts,), jnp.float32, least / len(split), high / len(split)))
        factor_of = factor_of * jnp.repeat(draws, shape[dim] // parts).reshape([-1 if axis == dim else 1 for axis in range(len(shape))])
    return factor_of


def split_up(count, total, reach, slope):
    loads = [(1 << 20) // math.isqrt(grade ** slope) + 1 for grade in range(2, count + 1)]
    surplus, given = total - reach - (count - 1), [1] * (count - 1)
    while surplus > 0:
        movable = [i for i in range(count - 1) if given[i] < reach]
        mass, budget = sum([loads[i] for i in movable]), surplus
        for i in movable:
            addition = min(reach - given[i], max(1, budget * loads[i] // mass), surplus)
            given[i] = given[i] + addition
            surplus = surplus - addition
    return np.array([reach] + given)


def ragged_sizes(key, amount, total, bound, skew):
    if amount == 2:
        one = jax.random.randint(key, (), max(1, total - bound), min(bound, total - 1) + 1)
        return jnp.stack([one, total - one])
    sizes = jnp.asarray(split_up(amount, total, bound, skew), jnp.int32)
    pairs = (amount - 1) // 2
    source_of, taker = sizes[1:1 + 2 * pairs:2], sizes[2:2 + 2 * pairs:2]
    margin = jnp.minimum(source_of - 1, bound - taker)
    shifted = jax.random.randint(jax.random.fold_in(key, 1), (pairs,), 0, 1 << 20) % (margin + 1)
    sizes = sizes.at[1:1 + 2 * pairs:2].set(source_of - shifted).at[2:2 + 2 * pairs:2].set(taker + shifted)
    return sizes[jax.random.permutation(jax.random.fold_in(key, 2), amount)]


def routed_block(stream_key, own, number, rows, number_of, top, most, skew):
    sequence = jax.random.permutation(stream_key, number_of)
    packed, common = portions_of(number_of, rows * top, most, skew, True), portions_of(number_of, rows * top, most, skew, False)
    places = jnp.arange(number_of)

    def named(sizes, rotation):
        used = int((sizes > 0).sum())
        fixed = max(1, used // 4)
        moved = fixed + (places - fixed + rotation * (used - fixed)) % max(1, number_of - fixed)
        return jnp.zeros((number_of,), jnp.int32).at[sequence[jnp.where(places < fixed, places, moved)]].set(jnp.asarray(sizes, jnp.int32))

    sizes = jnp.where(number % 4 == 0, named(packed, number // 4), named(common, number - number // 4 - 1))
    mixed = jax.random.permutation(jax.random.fold_in(own, 3), number_of)
    source_of, taker = mixed[0:number_of // 2 * 2:2], mixed[1:number_of // 2 * 2:2]
    room = jnp.minimum(sizes[source_of] - 1, most - sizes[taker]) // 2
    room = jnp.where((source_of == sequence[0]) | (taker == sequence[0]) | (sizes[taker] == 0), 0, jnp.maximum(room, 0))
    moved = jax.random.randint(jax.random.fold_in(own, 4), (number_of // 2,), 0, 1 << 20) % (room + 1)
    sizes = sizes.at[source_of].add(-moved).at[taker].add(moved)
    items = jnp.searchsorted(jnp.cumsum(sizes), jnp.arange(rows * top), side="right").astype(jnp.int32)
    grid = items.reshape(top, rows).T
    grid = grid[jax.random.permutation(jax.random.fold_in(own, 1), rows)]
    rotation = jax.random.randint(jax.random.fold_in(own, 2), (rows, 1), 0, top)
    return jnp.take_along_axis(grid, (jnp.arange(top)[None, :] + rotation) % top, axis=1)


def portions_of(amount, total, limit, slope, full):
    loads = [(1 << 20) // math.isqrt(grade ** slope) + 1 for grade in range(1, amount + 1)]
    largest = limit if full else min(limit, max(-(-total // amount), total * loads[0] // sum(loads)))
    least = 1 if total - largest >= amount - 1 else 0
    given, rest = [largest] + [least] * (amount - 1), total - largest - least * (amount - 1)
    while rest > 0:
        free = [i for i in range(1, amount) if given[i] < largest] or [i for i in range(1, amount) if given[i] < limit]
        whole, remaining = sum([loads[i] for i in free]), rest
        for i in free:
            more = min(limit - given[i], max(1, remaining * loads[i] // whole), rest)
            given[i] = given[i] + more
            rest = rest - more
    return np.array(given)


def noise(stream_key, extent, scale, limit, shards=(), held_as=jnp.bfloat16):
    factor_of = block_scale(stream_key, extent, shards, -0.22, 0.18) if shards else 1.0
    array = jax.random.normal(stream_key, extent, jnp.float32) * scale * factor_of
    return jnp.minimum(jnp.maximum(array, -limit), limit).astype(held_as)


def setup_inputs(seed: int = 0) -> dict:
    arg_keys = jax.random.split(jax.random.key(seed), 11)
    hidden_in = noise(arg_keys[0], (TOKENS, D), 1.0, 6.0, ((0, 32), (1, 4)))
    wq = draw_wq(jax.random.fold_in(arg_keys[10], 71), 0)
    wkv = noise(arg_keys[2], (D, 2 * KVH * HD), D ** -0.5, 0.15625, ((0, 32),))
    wo = noise(arg_keys[3], (HQ * HD, D), (HQ * HD) ** -0.5, 0.15625, ((0, 4), (1, 32)))
    lengths = ragged_sizes(arg_keys[4], 3, TOKENS, 3 * TOKENS // 4, 2).astype(jnp.int32)
    routes_keys = jax.random.split(jax.random.fold_in(arg_keys[5], 1), TOKENS // TOK_DEV)
    routes_turns = jax.random.permutation(jax.random.fold_in(arg_keys[5], 3), TOKENS // TOK_DEV)
    routes = jax.vmap(lambda own, number: routed_block(jax.random.fold_in(arg_keys[5], 2), own, number, TOK_DEV, EXPERTS, TOP, CAP, 2))(routes_keys, routes_turns).reshape((TOKENS, TOP))
    gate_logits = noise(arg_keys[6], (TOKENS, TOP), 1.5, 6.0, ((0, 32),), jnp.float32)
    expert_gate = noise(arg_keys[7], (EXPERTS, FFE, D), D ** -0.5, 0.15625, ((0, 32), (1, 4)))
    expert_up = noise(arg_keys[8], (EXPERTS, FFE, D), D ** -0.5, 0.15625, ((0, 32), (1, 4)))
    expert_down = noise(arg_keys[9], (EXPERTS, FFE, D), FFE ** -0.5, 0.21875, ((0, 32), (1, 4)))
    return {"hidden_in": hidden_in, "wq": wq, "wkv": wkv, "wo": wo, "lengths": lengths, "routes": routes, "gate_logits": gate_logits, "expert_gate": expert_gate, "expert_up": expert_up, "expert_down": expert_down}


ROPE_BASE = 1500000.0
EPSILON = 1e-06

def prompt_ids(index, lengths):
    first_end = lengths[0]
    second_end = lengths[0] + lengths[1]
    prompt = (index >= first_end).astype(jnp.int32) + (index >= second_end).astype(jnp.int32)
    begin = jnp.where(index >= second_end, second_end, jnp.where(index >= first_end, first_end, 0))
    return (prompt, index - begin)

def rotary(values, position):
    half_dim = values.shape[-1] // 2
    freqs = jnp.exp(jnp.arange(half_dim, dtype=jnp.float32) * (-2.0 * math.log(ROPE_BASE) / values.shape[-1]))
    angles = position.astype(jnp.float32)[:, None] * freqs[None, :]
    cosine = jnp.cos(angles)[:, None, :]
    sine = jnp.sin(angles)[:, None, :]
    front = values[..., :half_dim]
    latter = values[..., half_dim:]
    return jnp.concatenate([front * cosine - latter * sine, latter * cosine + front * sine], axis=-1)

def rms_norm(values):
    return values * lax.rsqrt(lax.optimization_barrier(jnp.sum(values * values, axis=-1, keepdims=True)) / values.shape[-1] + EPSILON)

def window_mask(query_index, key_index, lengths):
    query_prompt, _ = prompt_ids(query_index, lengths)
    key_prompt, _ = prompt_ids(key_index, lengths)
    spacing = query_index[:, None] - key_index[None, :]
    return (query_prompt[:, None] == key_prompt[None, :]) & (spacing >= 0) & (spacing < WINDOW) & (key_index[None, :] >= 0)

def reference(hidden_in, wq, wkv, wo, lengths, routes, gate_logits, expert_gate, expert_up, expert_down):
    token_count = hidden_in.shape[0]
    index_all = jnp.arange(token_count, dtype=jnp.int32)
    _, position = prompt_ids(index_all, lengths)
    normed = rms_norm(hidden_in.astype(jnp.float32)).astype(jnp.bfloat16)
    query_lin = jnp.dot(normed, wq, preferred_element_type=jnp.float32)
    kv_lin = jnp.dot(normed, wkv, preferred_element_type=jnp.float32)
    queries = rotary(query_lin.reshape(token_count, HQ, HD), position).astype(jnp.bfloat16)
    keys = rotary(kv_lin[:, :KVH * HD].reshape(token_count, KVH, HD), position).astype(jnp.bfloat16)
    values = kv_lin[:, KVH * HD:].reshape(token_count, KVH, HD).astype(jnp.bfloat16)
    keys_wide = jnp.repeat(keys, HQ // KVH, axis=1).astype(jnp.float32)
    values_wide = jnp.repeat(values, HQ // KVH, axis=1).astype(jnp.float32)
    block_rows = min(512, token_count)
    scale = HD ** (-0.5)

    def attend_block(block):
        start = block * block_rows
        query_block = lax.dynamic_slice_in_dim(queries, start, block_rows, 0).astype(jnp.float32)
        scores = jnp.einsum('qhd,khd->hqk', query_block, keys_wide) * scale
        query_index = start + jnp.arange(block_rows, dtype=jnp.int32)
        allowed = window_mask(query_index, index_all, lengths)[None]
        masked = jnp.where(allowed, scores, -1e+30)
        peak = lax.optimization_barrier(jnp.max(masked, axis=-1, keepdims=True))
        weights = jnp.where(allowed, jnp.exp(masked - peak), 0.0)
        total = lax.optimization_barrier(jnp.sum(weights, axis=-1))
        mixed = jnp.einsum('hqk,khd->hqd', weights, values_wide) / total[..., None]
        return mixed.transpose(1, 0, 2).reshape(block_rows, HQ * HD)
    attended = lax.map(attend_block, jnp.arange(token_count // block_rows, dtype=jnp.int32))
    attended = attended.reshape(token_count, HQ * HD).astype(jnp.bfloat16)
    attn_out = jnp.dot(attended, wo, preferred_element_type=jnp.float32)
    residual = (hidden_in.astype(jnp.float32) + attn_out).astype(jnp.bfloat16)
    moe_in = rms_norm(residual.astype(jnp.float32)).astype(jnp.bfloat16)
    gate_weights = jax.nn.softmax(gate_logits.astype(jnp.float32), axis=-1)
    capacity = N_SEQ * CAP

    def expert_step(accum, inputs):
        w_gate, w_up, w_down, expert = inputs
        chosen = routes == expert
        share = lax.optimization_barrier(jnp.sum(jnp.where(chosen, gate_weights, 0.0), axis=1))
        picked = jnp.any(chosen, axis=1)
        row_index = jnp.nonzero(picked, size=capacity, fill_value=0)[0].astype(jnp.int32)
        counted = jnp.sum(picked.astype(jnp.int32))
        usable = jnp.arange(capacity, dtype=jnp.int32) < counted
        selected = moe_in[row_index]
        gate_act = jnp.dot(selected, w_gate.T, preferred_element_type=jnp.float32)
        up_act = jnp.dot(selected, w_up.T, preferred_element_type=jnp.float32)
        active = (jnp.maximum(gate_act, 0.0) * up_act).astype(jnp.bfloat16)
        result = jnp.dot(active, w_down, preferred_element_type=jnp.float32).astype(jnp.bfloat16)
        contrib = jnp.where(usable[:, None], share[row_index][:, None] * result.astype(jnp.float32), 0.0)
        return (accum.at[row_index].add(contrib), None)
    moe_total, _ = lax.scan(expert_step, jnp.zeros((token_count, D), jnp.float32), (expert_gate, expert_up, expert_down, jnp.arange(EXPERTS, dtype=jnp.int32)))
    return (residual.astype(jnp.float32) + moe_total).astype(jnp.bfloat16)
```

```python
import math

import jax
import jax.numpy as jnp
from jax import lax
from jax.sharding import PartitionSpec as P

D = 1536
HQ = 12
KVH = 2
HD = 128
WINDOW = 4096


ROPE_BASE = 1500000.0
EPSILON = 1e-06


def prompt_ids(index, lengths):
    first_end = lengths[0]
    second_end = lengths[0] + lengths[1]
    prompt = (index >= first_end).astype(jnp.int32) + (index >= second_end).astype(jnp.int32)
    begin = jnp.where(index >= second_end, second_end, jnp.where(index >= first_end, first_end, 0))
    return (prompt, index - begin)


def rotary(values, position):
    half_dim = values.shape[-1] // 2
    freqs = jnp.exp(
        jnp.arange(half_dim, dtype=jnp.float32) * (-2.0 * math.log(ROPE_BASE) / values.shape[-1])
    )
    angles = position.astype(jnp.float32)[:, None] * freqs[None, :]
    cosine = jnp.cos(angles)[:, None, :]
    sine = jnp.sin(angles)[:, None, :]
    front = values[..., :half_dim]
    latter = values[..., half_dim:]
    return jnp.concatenate(
        [front * cosine - latter * sine, latter * cosine + front * sine], axis=-1
    )


def gather_seq(piece, count):
    rows = piece.shape[0]
    spread = jnp.broadcast_to(piece[None], (count,) + piece.shape).reshape(
        count * rows, piece.shape[1]
    )
    return lax.all_to_all(spread, "seq", 0, 0, tiled=True)


def local(
    hidden_in, wq, wkv, wo, lengths, routes, gate_logits, expert_gate, expert_up, expert_down
):
    tok_rows = hidden_in.shape[0]
    seq_index = lax.axis_index("seq")
    mp_index = lax.axis_index("mp")
    seq_count = lax.axis_size("seq")
    mp_count = lax.axis_size("mp")
    heads_here = wq.shape[1] // HD
    q_cols = heads_here * HD
    kv_group = mp_index * heads_here // (HQ // KVH)

    expert_all = lax.all_gather(
        jnp.concatenate([expert_gate, expert_up, expert_down], axis=0), "mp", axis=1, tiled=True
    )

    key_cols = lax.dynamic_slice_in_dim(wkv, kv_group * HD, HD, 1)
    value_cols = lax.dynamic_slice_in_dim(wkv, KVH * HD + kv_group * HD, HD, 1)
    piece = jnp.concatenate([wq, key_cols, value_cols, wo.T], axis=1)
    weights = gather_seq(piece, seq_count)
    w_qkv = weights[:, : q_cols + 2 * HD]
    wo_rows = weights[:, q_cols + 2 * HD :]

    whole = lax.all_gather(hidden_in, "mp", axis=1, tiled=True)
    whole_f = whole.astype(jnp.float32)
    normed = (
        whole_f * lax.rsqrt(jnp.sum(whole_f * whole_f, axis=-1, keepdims=True) / D + EPSILON)
    ).astype(jnp.bfloat16)
    lin = jnp.dot(normed, w_qkv, preferred_element_type=jnp.float32)
    own_index = seq_index * tok_rows + jnp.arange(tok_rows, dtype=jnp.int32)
    _, own_pos = prompt_ids(own_index, lengths)
    queries = (
        rotary(lin[:, :q_cols].reshape(tok_rows, heads_here, HD), own_pos)
        .astype(jnp.bfloat16)
        .transpose(1, 0, 2)
    )
    key_own = rotary(lin[:, q_cols : q_cols + HD].reshape(tok_rows, 1, HD), own_pos)[:, 0, :]
    value_own = lin[:, q_cols + HD :]
    kv_own = jnp.concatenate([key_own.astype(jnp.bfloat16), value_own.astype(jnp.bfloat16)], axis=1)

    back = min((WINDOW - 1 + tok_rows - 1) // tok_rows, seq_count - 1)
    blocks = []
    for k in range(back, 0, -1):
        blocks.append(lax.ppermute(kv_own, "seq", [(i, i + k) for i in range(seq_count - k)]))
    blocks.append(kv_own)
    kv_win = jnp.concatenate(blocks, axis=0)
    key_rows = kv_win[:, :HD]
    value_rows = kv_win[:, HD:].astype(jnp.float32)
    key_index = (seq_index - back) * tok_rows + jnp.arange((back + 1) * tok_rows, dtype=jnp.int32)

    scores = jnp.einsum(
        "hqd,kd->hqk", queries, key_rows, preferred_element_type=jnp.float32
    ) * HD ** (-0.5)
    query_prompt, _ = prompt_ids(own_index, lengths)
    key_prompt, _ = prompt_ids(key_index, lengths)
    spacing = own_index[:, None] - key_index[None, :]
    allowed = (
        (query_prompt[:, None] == key_prompt[None, :])
        & (spacing >= 0)
        & (spacing < WINDOW)
        & (key_index[None, :] >= 0)
    )[None]
    masked = jnp.where(allowed, scores, -1e30)
    peak = jnp.max(masked, axis=-1)
    probs = jnp.where(allowed, jnp.exp(masked - peak[..., None]), 0.0)
    total = jnp.sum(probs, axis=-1)
    accum = jnp.einsum("hqk,kd->hqd", probs, value_rows)
    attended = (
        (accum / total[..., None])
        .transpose(1, 0, 2)
        .reshape(tok_rows, q_cols)
        .astype(jnp.bfloat16)
    )
    partial_out = lax.dot_general(
        attended, wo_rows, (((1,), (1,)), ((), ())), preferred_element_type=jnp.float32
    )
    attn_mine = lax.psum_scatter(
        partial_out.astype(jnp.bfloat16), "mp", scatter_dimension=1, tiled=True
    ).astype(jnp.float32)
    residual = (hidden_in.astype(jnp.float32) + attn_mine).astype(jnp.bfloat16)
    residual_f = residual.astype(jnp.float32)
    square_sum = lax.psum(jnp.sum(residual_f * residual_f, axis=-1), "mp")
    moe_local = (residual_f * lax.rsqrt(square_sum / D + EPSILON)[:, None]).astype(jnp.bfloat16)

    local_experts = expert_gate.shape[0]
    experts = seq_count * local_experts
    top_count = routes.shape[1]
    capacity = 2 * tok_rows * top_count // experts
    part_cap = capacity // mp_count
    flat_ids = routes.reshape(-1)
    one_hot = (flat_ids[:, None] == jnp.arange(experts, dtype=jnp.int32)[None, :]).astype(jnp.int32)
    earlier_count = jnp.sum((jnp.cumsum(one_hot, axis=0) - one_hot) * one_hot, axis=1)
    mine = (earlier_count // part_cap) == mp_index
    slot_index = flat_ids * part_cap + earlier_count % part_cap
    send_index = jnp.where(mine, slot_index, experts * part_cap)
    source_row = jnp.arange(tok_rows * top_count, dtype=jnp.int32) // top_count
    full_rows = lax.all_gather(moe_local, "mp", axis=1, tiled=True)
    buffer = (
        jnp.zeros((experts * part_cap, D), jnp.bfloat16)
        .at[send_index]
        .set(full_rows[source_row], mode="drop")
    )
    arrived = lax.all_to_all(buffer, "seq", 0, 0, tiled=True)
    hidden_units = expert_all.shape[1]
    w_gate = expert_all[0]
    w_up = expert_all[1]
    w_down = expert_all[2]
    gate_act = lax.dot_general(
        arrived, w_gate, (((1,), (1,)), ((), ())), preferred_element_type=jnp.float32
    )
    up_act = lax.dot_general(
        arrived, w_up, (((1,), (1,)), ((), ())), preferred_element_type=jnp.float32
    )
    active = (jnp.maximum(gate_act, 0.0) * up_act).astype(jnp.bfloat16)
    result = jnp.dot(active, w_down, preferred_element_type=jnp.float32).astype(jnp.bfloat16)
    returned = lax.all_to_all(result, "seq", 0, 0, tiled=True)

    gate_weights = jax.nn.softmax(gate_logits, axis=-1)
    picked_back = returned[jnp.where(mine, slot_index, 0)].astype(jnp.float32)
    share = jnp.where(mine, gate_weights.reshape(-1), 0.0)
    weighted = picked_back * share[:, None]
    partial_moe = jnp.sum(weighted.reshape(tok_rows, top_count, D), axis=1)
    swapped = lax.all_to_all(partial_moe.astype(jnp.bfloat16), "mp", 1, 0, tiled=True)
    moe_total = jnp.sum(
        swapped.reshape(mp_count, tok_rows, D // mp_count).astype(jnp.float32), axis=0
    )
    del hidden_units
    return (residual_f + moe_total).astype(jnp.bfloat16)


def solution(mesh):
    return jax.shard_map(
        local,
        mesh=mesh,
        in_specs=(
            P("seq", "mp"),
            P("seq", "mp"),
            P("seq", None),
            P("mp", "seq"),
            P(),
            P("seq", None),
            P("seq", None),
            P("seq", "mp", None),
            P("seq", "mp", None),
            P("seq", "mp", None),
        ),
        out_specs=P("seq", "mp"),
        check_vma=False,
    )
```

```python
import math

import jax
import jax.numpy as jnp
from jax import lax
from jax.sharding import PartitionSpec as P

D = 1536
HQ = 12
KVH = 2
HD = 128
WINDOW = 4096


ROPE_BASE = 1500000.0
EPSILON = 1e-06


def prompt_ids(index, lengths):
    first_end = lengths[0]
    second_end = lengths[0] + lengths[1]
    prompt = (index >= first_end).astype(jnp.int32) + (index >= second_end).astype(jnp.int32)
    begin = jnp.where(index >= second_end, second_end, jnp.where(index >= first_end, first_end, 0))
    return (prompt, index - begin)


def rotary(values, position):
    half_dim = values.shape[-1] // 2
    freqs = jnp.exp(
        jnp.arange(half_dim, dtype=jnp.float32) * (-2.0 * math.log(ROPE_BASE) / values.shape[-1])
    )
    angles = position.astype(jnp.float32)[:, None] * freqs[None, :]
    cosine = jnp.cos(angles)[:, None, :]
    sine = jnp.sin(angles)[:, None, :]
    front = values[..., :half_dim]
    latter = values[..., half_dim:]
    return jnp.concatenate(
        [front * cosine - latter * sine, latter * cosine + front * sine], axis=-1
    )


def gather_seq(piece, count):
    rows = piece.shape[0]
    spread = jnp.broadcast_to(piece[None], (count,) + piece.shape).reshape(
        count * rows, piece.shape[1]
    )
    return lax.all_to_all(spread, "seq", 0, 0, tiled=True)


def local(
    hidden_in, wq, wkv, wo, lengths, routes, gate_logits, expert_gate, expert_up, expert_down
):
    tok_rows = hidden_in.shape[0]
    seq_index = lax.axis_index("seq")
    mp_index = lax.axis_index("mp")
    seq_count = lax.axis_size("seq")
    mp_count = lax.axis_size("mp")
    heads_here = wq.shape[1] // HD
    q_cols = heads_here * HD
    kv_group = mp_index * heads_here // (HQ // KVH)

    expert_all = lax.all_gather(
        jnp.concatenate([expert_gate, expert_up, expert_down], axis=0), "mp", axis=1, tiled=True
    )

    key_cols = lax.dynamic_slice_in_dim(wkv, kv_group * HD, HD, 1)
    value_cols = lax.dynamic_slice_in_dim(wkv, KVH * HD + kv_group * HD, HD, 1)
    piece = jnp.concatenate([wq, key_cols, value_cols, wo.T], axis=1)
    weights = gather_seq(piece, seq_count)
    w_qkv = weights[:, : q_cols + 2 * HD]
    wo_rows = weights[:, q_cols + 2 * HD :]

    whole = lax.all_gather(hidden_in, "mp", axis=1, tiled=True)
    whole_f = whole.astype(jnp.float32)
    normed = (
        whole_f * lax.rsqrt(jnp.sum(whole_f * whole_f, axis=-1, keepdims=True) / D + EPSILON)
    ).astype(jnp.bfloat16)
    lin = jnp.dot(normed, w_qkv, preferred_element_type=jnp.float32)
    own_index = seq_index * tok_rows + jnp.arange(tok_rows, dtype=jnp.int32)
    _, own_pos = prompt_ids(own_index, lengths)
    queries = (
        rotary(lin[:, :q_cols].reshape(tok_rows, heads_here, HD), own_pos)
        .astype(jnp.bfloat16)
        .transpose(1, 0, 2)
    )
    key_own = rotary(lin[:, q_cols : q_cols + HD].reshape(tok_rows, 1, HD), own_pos)[:, 0, :]
    value_own = lin[:, q_cols + HD :]
    kv_own = jnp.concatenate([key_own.astype(jnp.bfloat16), value_own.astype(jnp.bfloat16)], axis=1)

    back = min((WINDOW - 1 + tok_rows - 1) // tok_rows, seq_count - 1)
    half = (back + 1) // 2
    core = mp_index % 2
    fetched = []
    for j in range(half):
        pairs = []
        for s in range(seq_count):
            for m in range(mp_count):
                k = 2 * j + 1 + m % 2
                if s + k < seq_count:
                    pairs.append((s * mp_count + m, (s + k) * mp_count + m))
        fetched.append(lax.ppermute(kv_own, ("seq", "mp"), pairs))
    fetched = jnp.stack(fetched)
    partner = lax.ppermute(
        fetched, "mp", [(m, m ^ 1) for m in range(mp_count)]
    )
    odd = jnp.where(core == 0, fetched, partner)
    even = jnp.where(core == 0, partner, fetched)
    offsets = jnp.concatenate(
        [
            2 * jnp.arange(half, dtype=jnp.int32) + 1,
            2 * jnp.arange(half, dtype=jnp.int32) + 2,
            jnp.zeros((1,), jnp.int32),
        ]
    )
    kv_win = jnp.concatenate(
        [odd.reshape(-1, 2 * HD), even.reshape(-1, 2 * HD), kv_own], axis=0
    )
    key_rows = kv_win[:, :HD]
    value_rows = kv_win[:, HD:].astype(jnp.float32)
    key_index = (
        (seq_index - offsets)[:, None] * tok_rows + jnp.arange(tok_rows, dtype=jnp.int32)[None, :]
    ).reshape(-1)
    key_index = jnp.where(
        jnp.repeat(offsets, tok_rows) <= back, key_index, -1
    )

    scores = jnp.einsum(
        "hqd,kd->hqk", queries, key_rows, preferred_element_type=jnp.float32
    ) * HD ** (-0.5)
    query_prompt, _ = prompt_ids(own_index, lengths)
    key_prompt, _ = prompt_ids(key_index, lengths)
    spacing = own_index[:, None] - key_index[None, :]
    allowed = (
        (query_prompt[:, None] == key_prompt[None, :])
        & (spacing >= 0)
        & (spacing < WINDOW)
        & (key_index[None, :] >= 0)
    )[None]
    masked = jnp.where(allowed, scores, -1e30)
    peak = jnp.max(masked, axis=-1)
    probs = jnp.where(allowed, jnp.exp(masked - peak[..., None]), 0.0)
    total = jnp.sum(probs, axis=-1)
    accum = jnp.einsum("hqk,kd->hqd", probs, value_rows)
    attended = (
        (accum / total[..., None])
        .transpose(1, 0, 2)
        .reshape(tok_rows, q_cols)
        .astype(jnp.bfloat16)
    )
    partial_out = lax.dot_general(
        attended, wo_rows, (((1,), (1,)), ((), ())), preferred_element_type=jnp.float32
    )
    swapped_out = lax.all_to_all(partial_out.astype(jnp.bfloat16), "mp", 1, 0, tiled=True)
    attn_mine = jnp.sum(
        swapped_out.reshape(mp_count, tok_rows, D // mp_count).astype(jnp.float32), axis=0
    )
    residual = (hidden_in.astype(jnp.float32) + attn_mine).astype(jnp.bfloat16)
    residual_f = residual.astype(jnp.float32)
    residual_rows = lax.all_gather(residual, "mp", axis=1, tiled=True).astype(jnp.float32)
    full_rows = (
        residual_rows
        * lax.rsqrt(jnp.sum(residual_rows * residual_rows, axis=-1, keepdims=True) / D + EPSILON)
    ).astype(jnp.bfloat16)

    local_experts = expert_gate.shape[0]
    experts = seq_count * local_experts
    top_count = routes.shape[1]
    capacity = 2 * tok_rows * top_count // experts
    part_cap = capacity // mp_count
    flat_ids = routes.reshape(-1)
    one_hot = (flat_ids[:, None] == jnp.arange(experts, dtype=jnp.int32)[None, :]).astype(jnp.int32)
    earlier_count = jnp.sum((jnp.cumsum(one_hot, axis=0) - one_hot) * one_hot, axis=1)
    mine = (earlier_count // part_cap) == mp_index
    slot_index = flat_ids * part_cap + earlier_count % part_cap
    send_index = jnp.where(mine, slot_index, experts * part_cap)
    slots = jnp.arange(experts * part_cap, dtype=jnp.int32)
    pick = (send_index[None, :] == slots[:, None]).reshape(experts * part_cap, tok_rows, top_count)
    select = jnp.sum(pick.astype(jnp.bfloat16), axis=2)
    buffer = jnp.dot(select, full_rows, preferred_element_type=jnp.float32).astype(jnp.bfloat16)
    arrived = lax.all_to_all(buffer, "seq", 0, 0, tiled=True)
    w_gate = expert_all[0]
    w_up = expert_all[1]
    w_down = expert_all[2]
    gate_act = lax.dot_general(
        arrived, w_gate, (((1,), (1,)), ((), ())), preferred_element_type=jnp.float32
    )
    up_act = lax.dot_general(
        arrived, w_up, (((1,), (1,)), ((), ())), preferred_element_type=jnp.float32
    )
    active = (jnp.maximum(gate_act, 0.0) * up_act).astype(jnp.bfloat16)
    result = jnp.dot(active, w_down, preferred_element_type=jnp.float32).astype(jnp.bfloat16)
    returned = lax.all_to_all(result, "seq", 0, 0, tiled=True)

    gate_weights = jax.nn.softmax(gate_logits, axis=-1)
    share = jnp.where(mine, gate_weights.reshape(-1), 0.0)
    combine = jnp.sum(
        jnp.where(
            send_index[:, None] == slots[None, :], share[:, None], 0.0
        ).reshape(tok_rows, top_count, experts * part_cap),
        axis=1,
    )
    partial_moe = jnp.dot(
        combine,
        returned.astype(jnp.float32),
        precision=lax.Precision.HIGHEST,
        preferred_element_type=jnp.float32,
    )
    swapped = lax.all_to_all(partial_moe.astype(jnp.bfloat16), "mp", 1, 0, tiled=True)
    moe_total = jnp.sum(
        swapped.reshape(mp_count, tok_rows, D // mp_count).astype(jnp.float32), axis=0
    )
    return (residual_f + moe_total).astype(jnp.bfloat16)


def solution(mesh):
    return jax.shard_map(
        local,
        mesh=mesh,
        in_specs=(
            P("seq", "mp"),
            P("seq", "mp"),
            P("seq", None),
            P("mp", "seq"),
            P(),
            P("seq", None),
            P("seq", None),
            P("seq", "mp", None),
            P("seq", "mp", None),
            P("seq", "mp", None),
        ),
        out_specs=P("seq", "mp"),
        check_vma=False,
    )
```

```python
import math

import jax
import jax.numpy as jnp
from jax import lax
from jax.sharding import PartitionSpec as P

D = 1536
HQ = 12
KVH = 2
HD = 128
WINDOW = 4096


ROPE_BASE = 1500000.0
EPSILON = 1e-06


def prompt_ids(index, lengths):
    first_end = lengths[0]
    second_end = lengths[0] + lengths[1]
    prompt = (index >= first_end).astype(jnp.int32) + (index >= second_end).astype(jnp.int32)
    begin = jnp.where(index >= second_end, second_end, jnp.where(index >= first_end, first_end, 0))
    return (prompt, index - begin)


def rotary(values, position):
    half_dim = values.shape[-1] // 2
    freqs = jnp.exp(
        jnp.arange(half_dim, dtype=jnp.float32) * (-2.0 * math.log(ROPE_BASE) / values.shape[-1])
    )
    angles = position.astype(jnp.float32)[:, None] * freqs[None, :]
    cosine = jnp.cos(angles)[:, None, :]
    sine = jnp.sin(angles)[:, None, :]
    front = values[..., :half_dim]
    latter = values[..., half_dim:]
    return jnp.concatenate(
        [front * cosine - latter * sine, latter * cosine + front * sine], axis=-1
    )


def gather_seq(piece, count):
    rows = piece.shape[0]
    spread = jnp.broadcast_to(piece[None], (count,) + piece.shape).reshape(
        count * rows, piece.shape[1]
    )
    return lax.all_to_all(spread, "seq", 0, 0, tiled=True)


def local(
    hidden_in, wq, wkv, wo, lengths, routes, gate_logits, expert_gate, expert_up, expert_down
):
    tok_rows = hidden_in.shape[0]
    seq_index = lax.axis_index("seq")
    mp_index = lax.axis_index("mp")
    seq_count = lax.axis_size("seq")
    mp_count = lax.axis_size("mp")
    heads_here = wq.shape[1] // HD
    q_cols = heads_here * HD
    kv_group = mp_index * heads_here // (HQ // KVH)

    whole = lax.all_gather(hidden_in, "mp", axis=1, tiled=True)
    expert_own, whole = lax.optimization_barrier(
        (jnp.concatenate([expert_gate, expert_up, expert_down], axis=0), whole)
    )
    mp_count_static = lax.axis_size("mp")
    across = lax.ppermute(expert_own, "mp", [(m, m ^ 2) for m in range(mp_count_static)])
    beside = lax.ppermute(
        jnp.concatenate([expert_own, across], axis=1),
        "mp",
        [(m, m ^ 1) for m in range(mp_count_static)],
    )
    expert_all = jnp.concatenate([expert_own, across, beside], axis=1)

    key_cols = lax.dynamic_slice_in_dim(wkv, kv_group * HD, HD, 1)
    value_cols = lax.dynamic_slice_in_dim(wkv, KVH * HD + kv_group * HD, HD, 1)
    piece = jnp.concatenate([wq, key_cols, value_cols, wo.T], axis=1)
    weights = gather_seq(piece, seq_count)
    w_qkv = weights[:, : q_cols + 2 * HD]
    wo_rows = weights[:, q_cols + 2 * HD :]

    whole_f = whole.astype(jnp.float32)
    normed = (
        whole_f * lax.rsqrt(jnp.sum(whole_f * whole_f, axis=-1, keepdims=True) / D + EPSILON)
    ).astype(jnp.bfloat16)
    lin = jnp.dot(normed, w_qkv, preferred_element_type=jnp.float32)
    own_index = seq_index * tok_rows + jnp.arange(tok_rows, dtype=jnp.int32)
    _, own_pos = prompt_ids(own_index, lengths)
    queries = (
        rotary(lin[:, :q_cols].reshape(tok_rows, heads_here, HD), own_pos)
        .astype(jnp.bfloat16)
        .transpose(1, 0, 2)
    )
    key_own = rotary(lin[:, q_cols : q_cols + HD].reshape(tok_rows, 1, HD), own_pos)[:, 0, :]
    value_own = lin[:, q_cols + HD :]
    kv_own = jnp.concatenate([key_own.astype(jnp.bfloat16), value_own.astype(jnp.bfloat16)], axis=1)

    back = min((WINDOW - 1 + tok_rows - 1) // tok_rows, seq_count - 1)
    half = (back + 1) // 2
    core = mp_index % 2
    fetched = []
    for j in range(half):
        pairs = []
        for s in range(seq_count):
            for m in range(mp_count):
                k = 2 * j + 1 + m % 2
                if s + k < seq_count:
                    pairs.append((s * mp_count + m, (s + k) * mp_count + m))
        fetched.append(lax.ppermute(kv_own, ("seq", "mp"), pairs))
    fetched = jnp.stack(fetched)
    partner = lax.ppermute(
        fetched, "mp", [(m, m ^ 1) for m in range(mp_count)]
    )
    odd = jnp.where(core == 0, fetched, partner)
    even = jnp.where(core == 0, partner, fetched)
    offsets = jnp.concatenate(
        [
            2 * jnp.arange(half, dtype=jnp.int32) + 1,
            2 * jnp.arange(half, dtype=jnp.int32) + 2,
            jnp.zeros((1,), jnp.int32),
        ]
    )
    kv_win = jnp.concatenate(
        [odd.reshape(-1, 2 * HD), even.reshape(-1, 2 * HD), kv_own], axis=0
    )
    key_rows = kv_win[:, :HD]
    value_rows = kv_win[:, HD:].astype(jnp.float32)
    key_index = (
        (seq_index - offsets)[:, None] * tok_rows + jnp.arange(tok_rows, dtype=jnp.int32)[None, :]
    ).reshape(-1)
    key_index = jnp.where(
        jnp.repeat(offsets, tok_rows) <= back, key_index, -1
    )

    scores = jnp.einsum(
        "hqd,kd->hqk", queries, key_rows, preferred_element_type=jnp.float32
    ) * HD ** (-0.5)
    query_prompt, _ = prompt_ids(own_index, lengths)
    key_prompt, _ = prompt_ids(key_index, lengths)
    spacing = own_index[:, None] - key_index[None, :]
    allowed = (
        (query_prompt[:, None] == key_prompt[None, :])
        & (spacing >= 0)
        & (spacing < WINDOW)
        & (key_index[None, :] >= 0)
    )[None]
    masked = jnp.where(allowed, scores, -1e30)
    peak = jnp.max(masked, axis=-1)
    probs = jnp.where(allowed, jnp.exp(masked - peak[..., None]), 0.0)
    total = jnp.sum(probs, axis=-1)
    accum = jnp.einsum("hqk,kd->hqd", probs, value_rows)
    attended = (
        (accum / total[..., None])
        .transpose(1, 0, 2)
        .reshape(tok_rows, q_cols)
        .astype(jnp.bfloat16)
    )
    partial_out = lax.dot_general(
        attended, wo_rows, (((1,), (1,)), ((), ())), preferred_element_type=jnp.float32
    )
    swapped_out = lax.all_to_all(partial_out.astype(jnp.bfloat16), "mp", 1, 0, tiled=True)
    attn_mine = jnp.sum(
        swapped_out.reshape(mp_count, tok_rows, D // mp_count).astype(jnp.float32), axis=0
    )
    residual = (hidden_in.astype(jnp.float32) + attn_mine).astype(jnp.bfloat16)
    residual_f = residual.astype(jnp.float32)
    residual_rows = lax.all_gather(residual, "mp", axis=1, tiled=True).astype(jnp.float32)
    full_rows = (
        residual_rows
        * lax.rsqrt(jnp.sum(residual_rows * residual_rows, axis=-1, keepdims=True) / D + EPSILON)
    ).astype(jnp.bfloat16)

    local_experts = expert_gate.shape[0]
    experts = seq_count * local_experts
    top_count = routes.shape[1]
    capacity = 2 * tok_rows * top_count // experts
    part_cap = capacity // mp_count
    flat_ids = routes.reshape(-1)
    one_hot = (flat_ids[:, None] == jnp.arange(experts, dtype=jnp.int32)[None, :]).astype(jnp.int32)
    pair_count = tok_rows * top_count
    before = (
        jnp.arange(pair_count, dtype=jnp.int32)[:, None] > jnp.arange(pair_count, dtype=jnp.int32)[None, :]
    ).astype(jnp.bfloat16)
    earlier_all = jnp.dot(before, one_hot.astype(jnp.bfloat16), preferred_element_type=jnp.float32)
    earlier_count = jnp.sum(earlier_all.astype(jnp.int32) * one_hot, axis=1)
    mine = (earlier_count // part_cap) == mp_index
    slot_index = flat_ids * part_cap + earlier_count % part_cap
    send_index = jnp.where(mine, slot_index, experts * part_cap)
    slots = jnp.arange(experts * part_cap, dtype=jnp.int32)
    pick = (send_index[None, :] == slots[:, None]).reshape(experts * part_cap, tok_rows, top_count)
    select = jnp.sum(pick.astype(jnp.bfloat16), axis=2)
    buffer = jnp.dot(select, full_rows, preferred_element_type=jnp.float32).astype(jnp.bfloat16)
    arrived = lax.all_to_all(buffer, "seq", 0, 0, tiled=True)
    w_gate = expert_all[0]
    w_up = expert_all[1]
    w_down = expert_all[2]
    gate_act = lax.dot_general(
        arrived, w_gate, (((1,), (1,)), ((), ())), preferred_element_type=jnp.float32
    )
    up_act = lax.dot_general(
        arrived, w_up, (((1,), (1,)), ((), ())), preferred_element_type=jnp.float32
    )
    active = (jnp.maximum(gate_act, 0.0) * up_act).astype(jnp.bfloat16)
    result = jnp.dot(active, w_down, preferred_element_type=jnp.float32).astype(jnp.bfloat16)
    returned = lax.all_to_all(result, "seq", 0, 0, tiled=True)

    gate_weights = jax.nn.softmax(gate_logits, axis=-1)
    share = jnp.where(mine, gate_weights.reshape(-1), 0.0)
    combine = jnp.sum(
        jnp.where(
            send_index[:, None] == slots[None, :], share[:, None], 0.0
        ).reshape(tok_rows, top_count, experts * part_cap),
        axis=1,
    )
    partial_moe = jnp.dot(
        combine,
        returned.astype(jnp.float32),
        precision=lax.Precision.HIGHEST,
        preferred_element_type=jnp.float32,
    )
    swapped = lax.all_to_all(partial_moe.astype(jnp.bfloat16), "mp", 1, 0, tiled=True)
    moe_total = jnp.sum(
        swapped.reshape(mp_count, tok_rows, D // mp_count).astype(jnp.float32), axis=0
    )
    return (residual_f + moe_total).astype(jnp.bfloat16)


def solution(mesh):
    return jax.shard_map(
        local,
        mesh=mesh,
        in_specs=(
            P("seq", "mp"),
            P("seq", "mp"),
            P("seq", None),
            P("mp", "seq"),
            P(),
            P("seq", None),
            P("seq", None),
            P("seq", "mp", None),
            P("seq", "mp", None),
            P("seq", "mp", None),
        ),
        out_specs=P("seq", "mp"),
        check_vma=False,
    )
```

```python
import math

import jax
import jax.numpy as jnp
from jax import lax
from jax.sharding import PartitionSpec as P

D = 1536
HQ = 12
KVH = 2
HD = 128
WINDOW = 4096


ROPE_BASE = 1500000.0
EPSILON = 1e-06


def prompt_ids(index, lengths):
    first_end = lengths[0]
    second_end = lengths[0] + lengths[1]
    prompt = (index >= first_end).astype(jnp.int32) + (index >= second_end).astype(jnp.int32)
    begin = jnp.where(index >= second_end, second_end, jnp.where(index >= first_end, first_end, 0))
    return (prompt, index - begin)


def rotary(values, position):
    half_dim = values.shape[-1] // 2
    freqs = jnp.exp(
        jnp.arange(half_dim, dtype=jnp.float32) * (-2.0 * math.log(ROPE_BASE) / values.shape[-1])
    )
    angles = position.astype(jnp.float32)[:, None] * freqs[None, :]
    cosine = jnp.cos(angles)[:, None, :]
    sine = jnp.sin(angles)[:, None, :]
    front = values[..., :half_dim]
    latter = values[..., half_dim:]
    return jnp.concatenate(
        [front * cosine - latter * sine, latter * cosine + front * sine], axis=-1
    )


def gather_seq(piece, count):
    rows = piece.shape[0]
    spread = jnp.broadcast_to(piece[None], (count,) + piece.shape).reshape(
        count * rows, piece.shape[1]
    )
    return lax.all_to_all(spread, "seq", 0, 0, tiled=True)


def local(
    hidden_in, wq, wkv, wo, lengths, routes, gate_logits, expert_gate, expert_up, expert_down
):
    tok_rows = hidden_in.shape[0]
    seq_index = lax.axis_index("seq")
    mp_index = lax.axis_index("mp")
    seq_count = lax.axis_size("seq")
    mp_count = lax.axis_size("mp")
    heads_here = wq.shape[1] // HD
    q_cols = heads_here * HD
    kv_group = mp_index * heads_here // (HQ // KVH)

    expert_all = lax.all_gather(
        jnp.concatenate([expert_gate, expert_up, expert_down], axis=0), "mp", axis=1, tiled=True
    )

    key_cols = lax.dynamic_slice_in_dim(wkv, kv_group * HD, HD, 1)
    value_cols = lax.dynamic_slice_in_dim(wkv, KVH * HD + kv_group * HD, HD, 1)
    piece = jnp.concatenate([wq, key_cols, value_cols, wo.T], axis=1)
    weights = gather_seq(piece, seq_count)
    w_qkv = weights[:, : q_cols + 2 * HD]
    wo_rows = weights[:, q_cols + 2 * HD :]

    whole = lax.all_gather(hidden_in, "mp", axis=1, tiled=True)
    whole_f = whole.astype(jnp.float32)
    normed = (
        whole_f * lax.rsqrt(jnp.sum(whole_f * whole_f, axis=-1, keepdims=True) / D + EPSILON)
    ).astype(jnp.bfloat16)
    lin = jnp.dot(normed, w_qkv, preferred_element_type=jnp.float32)
    own_index = seq_index * tok_rows + jnp.arange(tok_rows, dtype=jnp.int32)
    _, own_pos = prompt_ids(own_index, lengths)
    queries = (
        rotary(lin[:, :q_cols].reshape(tok_rows, heads_here, HD), own_pos)
        .astype(jnp.bfloat16)
        .transpose(1, 0, 2)
    )
    key_own = rotary(lin[:, q_cols : q_cols + HD].reshape(tok_rows, 1, HD), own_pos)[:, 0, :]
    value_own = lin[:, q_cols + HD :]
    kv_own = jnp.concatenate([key_own.astype(jnp.bfloat16), value_own.astype(jnp.bfloat16)], axis=1)

    back = min((WINDOW - 1 + tok_rows - 1) // tok_rows, seq_count - 1)
    half = (back + 1) // 2
    core = mp_index % 2
    fetched = []
    for j in range(half):
        pairs = []
        for s in range(seq_count):
            for m in range(mp_count):
                k = 2 * j + 1 + m % 2
                if s + k < seq_count:
                    pairs.append((s * mp_count + m, (s + k) * mp_count + m))
        fetched.append(lax.ppermute(kv_own, ("seq", "mp"), pairs))
    fetched = jnp.stack(fetched)
    partner = lax.ppermute(
        fetched, "mp", [(m, m ^ 1) for m in range(mp_count)]
    )
    odd = jnp.where(core == 0, fetched, partner)
    even = jnp.where(core == 0, partner, fetched)
    offsets = jnp.concatenate(
        [
            2 * jnp.arange(half, dtype=jnp.int32) + 1,
            2 * jnp.arange(half, dtype=jnp.int32) + 2,
            jnp.zeros((1,), jnp.int32),
        ]
    )
    kv_win = jnp.concatenate(
        [odd.reshape(-1, 2 * HD), even.reshape(-1, 2 * HD), kv_own], axis=0
    )
    key_rows = kv_win[:, :HD]
    value_rows = kv_win[:, HD:].astype(jnp.float32)
    key_index = (
        (seq_index - offsets)[:, None] * tok_rows + jnp.arange(tok_rows, dtype=jnp.int32)[None, :]
    ).reshape(-1)
    key_index = jnp.where(
        jnp.repeat(offsets, tok_rows) <= back, key_index, -1
    )

    scores = jnp.einsum(
        "hqd,kd->hqk", queries, key_rows, preferred_element_type=jnp.float32
    ) * HD ** (-0.5)
    query_prompt, _ = prompt_ids(own_index, lengths)
    key_prompt, _ = prompt_ids(key_index, lengths)
    spacing = own_index[:, None] - key_index[None, :]
    allowed = (
        (query_prompt[:, None] == key_prompt[None, :])
        & (spacing >= 0)
        & (spacing < WINDOW)
        & (key_index[None, :] >= 0)
    )[None]
    masked = jnp.where(allowed, scores, -1e30)
    peak = jnp.max(masked, axis=-1)
    probs = jnp.where(allowed, jnp.exp(masked - peak[..., None]), 0.0)
    total = jnp.sum(probs, axis=-1)
    accum = jnp.einsum("hqk,kd->hqd", probs, value_rows)
    attended = (
        (accum / total[..., None])
        .transpose(1, 0, 2)
        .reshape(tok_rows, q_cols)
        .astype(jnp.bfloat16)
    )
    partial_out = lax.dot_general(
        attended, wo_rows, (((1,), (1,)), ((), ())), preferred_element_type=jnp.float32
    )
    swapped_out = lax.all_to_all(partial_out.astype(jnp.bfloat16), "mp", 1, 0, tiled=True)
    attn_mine = jnp.sum(
        swapped_out.reshape(mp_count, tok_rows, D // mp_count).astype(jnp.float32), axis=0
    )
    residual = (hidden_in.astype(jnp.float32) + attn_mine).astype(jnp.bfloat16)
    residual_f = residual.astype(jnp.float32)

    local_experts = expert_gate.shape[0]
    experts = seq_count * local_experts
    top_count = routes.shape[1]
    capacity = 2 * tok_rows * top_count // experts
    part_cap = capacity // mp_count
    pair_count = tok_rows * top_count
    flat_ids = routes.reshape(-1)
    one_hot = (flat_ids[:, None] == jnp.arange(experts, dtype=jnp.int32)[None, :]).astype(jnp.int32)
    before = (
        jnp.arange(pair_count, dtype=jnp.int32)[:, None]
        > jnp.arange(pair_count, dtype=jnp.int32)[None, :]
    ).astype(jnp.bfloat16)
    earlier_all = jnp.dot(before, one_hot.astype(jnp.bfloat16), preferred_element_type=jnp.float32)
    earlier_count = jnp.sum(earlier_all.astype(jnp.int32) * one_hot, axis=1)
    slot_index = flat_ids * capacity + earlier_count
    slots = jnp.arange(experts * capacity, dtype=jnp.int32)
    pick = (slot_index[None, :] == slots[:, None]).reshape(experts * capacity, tok_rows, top_count)
    select = jnp.sum(pick.astype(jnp.bfloat16), axis=2)
    buffer = jnp.dot(select, residual, preferred_element_type=jnp.float32).astype(jnp.bfloat16)
    arrived = lax.all_to_all(buffer, ("seq", "mp"), 0, 0, tiled=True)
    feat = D // mp_count
    arrived_rows = (
        arrived.reshape(seq_count, mp_count, part_cap, feat)
        .transpose(0, 2, 1, 3)
        .reshape(seq_count * part_cap, D)
        .astype(jnp.float32)
    )
    moe_in = (
        arrived_rows
        * lax.rsqrt(jnp.sum(arrived_rows * arrived_rows, axis=-1, keepdims=True) / D + EPSILON)
    ).astype(jnp.bfloat16)
    w_gate = expert_all[0]
    w_up = expert_all[1]
    w_down = expert_all[2]
    gate_act = lax.dot_general(
        moe_in, w_gate, (((1,), (1,)), ((), ())), preferred_element_type=jnp.float32
    )
    up_act = lax.dot_general(
        moe_in, w_up, (((1,), (1,)), ((), ())), preferred_element_type=jnp.float32
    )
    active = (jnp.maximum(gate_act, 0.0) * up_act).astype(jnp.bfloat16)
    result = jnp.dot(active, w_down, preferred_element_type=jnp.float32).astype(jnp.bfloat16)
    outgoing = (
        result.reshape(seq_count, part_cap, mp_count, feat)
        .transpose(0, 2, 1, 3)
        .reshape(seq_count * mp_count * part_cap, feat)
    )
    returned = lax.all_to_all(outgoing, ("seq", "mp"), 0, 0, tiled=True)

    gate_weights = jax.nn.softmax(gate_logits, axis=-1)
    combine = jnp.sum(
        jnp.where(
            slot_index[:, None] == slots[None, :], gate_weights.reshape(-1)[:, None], 0.0
        ).reshape(tok_rows, top_count, experts * capacity),
        axis=1,
    )
    moe_total = jnp.dot(
        combine,
        returned.astype(jnp.float32),
        precision=lax.Precision.HIGHEST,
        preferred_element_type=jnp.float32,
    )
    return (residual_f + moe_total).astype(jnp.bfloat16)


def solution(mesh):
    return jax.shard_map(
        local,
        mesh=mesh,
        in_specs=(
            P("seq", "mp"),
            P("seq", "mp"),
            P("seq", None),
            P("mp", "seq"),
            P(),
            P("seq", None),
            P("seq", None),
            P("seq", "mp", None),
            P("seq", "mp", None),
            P("seq", "mp", None),
        ),
        out_specs=P("seq", "mp"),
        check_vma=False,
    )
```

```python
import math

import jax
import jax.numpy as jnp
from jax import lax
from jax.sharding import PartitionSpec as P

D = 1536
HQ = 12
KVH = 2
HD = 128
WINDOW = 4096


ROPE_BASE = 1500000.0
EPSILON = 1e-06


def prompt_ids(index, lengths):
    first_end = lengths[0]
    second_end = lengths[0] + lengths[1]
    prompt = (index >= first_end).astype(jnp.int32) + (index >= second_end).astype(jnp.int32)
    begin = jnp.where(index >= second_end, second_end, jnp.where(index >= first_end, first_end, 0))
    return (prompt, index - begin)


def rotary(values, position):
    half_dim = values.shape[-1] // 2
    freqs = jnp.exp(
        jnp.arange(half_dim, dtype=jnp.float32) * (-2.0 * math.log(ROPE_BASE) / values.shape[-1])
    )
    angles = position.astype(jnp.float32)[:, None] * freqs[None, :]
    cosine = jnp.cos(angles)[:, None, :]
    sine = jnp.sin(angles)[:, None, :]
    front = values[..., :half_dim]
    latter = values[..., half_dim:]
    return jnp.concatenate(
        [front * cosine - latter * sine, latter * cosine + front * sine], axis=-1
    )


def gather_seq(piece, count):
    rows = piece.shape[0]
    spread = jnp.broadcast_to(piece[None], (count,) + piece.shape).reshape(
        count * rows, piece.shape[1]
    )
    return lax.all_to_all(spread, "seq", 0, 0, tiled=True)


def local(
    hidden_in, wq, wkv, wo, lengths, routes, gate_logits, expert_gate, expert_up, expert_down
):
    tok_rows = hidden_in.shape[0]
    seq_index = lax.axis_index("seq")
    mp_index = lax.axis_index("mp")
    seq_count = lax.axis_size("seq")
    mp_count = lax.axis_size("mp")
    heads_here = wq.shape[1] // HD
    q_cols = heads_here * HD
    kv_group = mp_index * heads_here // (HQ // KVH)

    expert_all = lax.all_gather(
        jnp.concatenate([expert_gate, expert_up, expert_down], axis=0), "mp", axis=1, tiled=True
    )

    core = mp_index % 2
    kv_col = jnp.where(core == 0, kv_group * HD, KVH * HD + kv_group * HD)
    kv_cols = lax.dynamic_slice_in_dim(wkv, kv_col, HD, 1)
    w_qkv = gather_seq(jnp.concatenate([wq, kv_cols], axis=1), seq_count)

    whole = lax.all_gather(hidden_in, "mp", axis=1, tiled=True)
    whole_f = whole.astype(jnp.float32)
    normed = (
        whole_f * lax.rsqrt(jnp.sum(whole_f * whole_f, axis=-1, keepdims=True) / D + EPSILON)
    ).astype(jnp.bfloat16)
    lin = jnp.dot(normed, w_qkv, preferred_element_type=jnp.float32)
    wo_piece, lin = lax.optimization_barrier((wo.T, lin))
    wo_rows = gather_seq(wo_piece, seq_count)
    own_index = seq_index * tok_rows + jnp.arange(tok_rows, dtype=jnp.int32)
    _, own_pos = prompt_ids(own_index, lengths)
    queries = (
        rotary(lin[:, :q_cols].reshape(tok_rows, heads_here, HD), own_pos)
        .astype(jnp.bfloat16)
        .transpose(1, 0, 2)
    )
    kv_lin = lin[:, q_cols:]
    kv_mine = jnp.where(
        core == 0, rotary(kv_lin.reshape(tok_rows, 1, HD), own_pos)[:, 0, :], kv_lin
    ).astype(jnp.bfloat16)
    kv_other = lax.ppermute(kv_mine, "mp", [(m, m ^ 1) for m in range(mp_count)])
    key_own = jnp.where(core == 0, kv_mine, kv_other)
    value_own = jnp.where(core == 0, kv_other, kv_mine)
    kv_own = jnp.concatenate([key_own, value_own], axis=1)

    back = min((WINDOW - 1 + tok_rows - 1) // tok_rows, seq_count - 1)
    half = (back + 1) // 2
    fetched = []
    for j in range(half):
        pairs = []
        for s in range(seq_count):
            for m in range(mp_count):
                k = 2 * j + 1 + m % 2
                if s + k < seq_count:
                    pairs.append((s * mp_count + m, (s + k) * mp_count + m))
        fetched.append(lax.ppermute(kv_own, ("seq", "mp"), pairs))
    fetched = jnp.stack(fetched)
    partner = lax.ppermute(
        fetched, "mp", [(m, m ^ 1) for m in range(mp_count)]
    )
    odd = jnp.where(core == 0, fetched, partner)
    even = jnp.where(core == 0, partner, fetched)
    offsets = jnp.concatenate(
        [
            2 * jnp.arange(half, dtype=jnp.int32) + 1,
            2 * jnp.arange(half, dtype=jnp.int32) + 2,
            jnp.zeros((1,), jnp.int32),
        ]
    )
    kv_win = jnp.concatenate(
        [odd.reshape(-1, 2 * HD), even.reshape(-1, 2 * HD), kv_own], axis=0
    )
    key_rows = kv_win[:, :HD]
    value_rows = kv_win[:, HD:].astype(jnp.float32)
    key_index = (
        (seq_index - offsets)[:, None] * tok_rows + jnp.arange(tok_rows, dtype=jnp.int32)[None, :]
    ).reshape(-1)
    key_index = jnp.where(
        jnp.repeat(offsets, tok_rows) <= back, key_index, -1
    )

    scores = jnp.einsum(
        "hqd,kd->hqk", queries, key_rows, preferred_element_type=jnp.float32
    ) * HD ** (-0.5)
    query_prompt, _ = prompt_ids(own_index, lengths)
    key_prompt, _ = prompt_ids(key_index, lengths)
    spacing = own_index[:, None] - key_index[None, :]
    allowed = (
        (query_prompt[:, None] == key_prompt[None, :])
        & (spacing >= 0)
        & (spacing < WINDOW)
        & (key_index[None, :] >= 0)
    )[None]
    masked = jnp.where(allowed, scores, -1e30)
    peak = jnp.max(masked, axis=-1)
    probs = jnp.where(allowed, jnp.exp(masked - peak[..., None]), 0.0)
    total = jnp.sum(probs, axis=-1)
    accum = jnp.einsum("hqk,kd->hqd", probs, value_rows)
    attended = (
        (accum / total[..., None])
        .transpose(1, 0, 2)
        .reshape(tok_rows, q_cols)
        .astype(jnp.bfloat16)
    )
    partial_out = lax.dot_general(
        attended, wo_rows, (((1,), (1,)), ((), ())), preferred_element_type=jnp.float32
    )
    swapped_out = lax.all_to_all(partial_out.astype(jnp.bfloat16), "mp", 1, 0, tiled=True)
    attn_mine = jnp.sum(
        swapped_out.reshape(mp_count, tok_rows, D // mp_count).astype(jnp.float32), axis=0
    )
    residual = (hidden_in.astype(jnp.float32) + attn_mine).astype(jnp.bfloat16)
    residual_f = residual.astype(jnp.float32)

    local_experts = expert_gate.shape[0]
    experts = seq_count * local_experts
    top_count = routes.shape[1]
    capacity = 2 * tok_rows * top_count // experts
    part_cap = capacity // mp_count
    pair_count = tok_rows * top_count
    flat_ids = routes.reshape(-1)
    one_hot = (flat_ids[:, None] == jnp.arange(experts, dtype=jnp.int32)[None, :]).astype(jnp.int32)
    before = (
        jnp.arange(pair_count, dtype=jnp.int32)[:, None]
        > jnp.arange(pair_count, dtype=jnp.int32)[None, :]
    ).astype(jnp.bfloat16)
    earlier_all = jnp.dot(before, one_hot.astype(jnp.bfloat16), preferred_element_type=jnp.float32)
    earlier_count = jnp.sum(earlier_all.astype(jnp.int32) * one_hot, axis=1)
    slot_index = flat_ids * capacity + earlier_count
    slots = jnp.arange(experts * capacity, dtype=jnp.int32)
    pick = (slot_index[None, :] == slots[:, None]).reshape(experts * capacity, tok_rows, top_count)
    select = jnp.sum(pick.astype(jnp.bfloat16), axis=2)
    buffer = jnp.dot(select, residual, preferred_element_type=jnp.float32).astype(jnp.bfloat16)
    arrived = lax.all_to_all(buffer, ("seq", "mp"), 0, 0, tiled=True)
    feat = D // mp_count
    arrived_rows = (
        arrived.reshape(seq_count, mp_count, part_cap, feat)
        .transpose(0, 2, 1, 3)
        .reshape(seq_count * part_cap, D)
        .astype(jnp.float32)
    )
    moe_in = (
        arrived_rows
        * lax.rsqrt(jnp.sum(arrived_rows * arrived_rows, axis=-1, keepdims=True) / D + EPSILON)
    ).astype(jnp.bfloat16)
    w_gate = expert_all[0]
    w_up = expert_all[1]
    w_down = expert_all[2]
    gate_act = lax.dot_general(
        moe_in, w_gate, (((1,), (1,)), ((), ())), preferred_element_type=jnp.float32
    )
    up_act = lax.dot_general(
        moe_in, w_up, (((1,), (1,)), ((), ())), preferred_element_type=jnp.float32
    )
    active = (jnp.maximum(gate_act, 0.0) * up_act).astype(jnp.bfloat16)
    result = jnp.dot(active, w_down, preferred_element_type=jnp.float32).astype(jnp.bfloat16)
    outgoing = (
        result.reshape(seq_count, part_cap, mp_count, feat)
        .transpose(0, 2, 1, 3)
        .reshape(seq_count * mp_count * part_cap, feat)
    )
    returned = lax.all_to_all(outgoing, ("seq", "mp"), 0, 0, tiled=True)

    gate_weights = jax.nn.softmax(gate_logits, axis=-1)
    combine = jnp.sum(
        jnp.where(
            slot_index[:, None] == slots[None, :], gate_weights.reshape(-1)[:, None], 0.0
        ).reshape(tok_rows, top_count, experts * capacity),
        axis=1,
    )
    moe_total = jnp.dot(
        combine,
        returned.astype(jnp.float32),
        precision=lax.Precision.HIGHEST,
        preferred_element_type=jnp.float32,
    )
    return (residual_f + moe_total).astype(jnp.bfloat16)


def solution(mesh):
    return jax.shard_map(
        local,
        mesh=mesh,
        in_specs=(
            P("seq", "mp"),
            P("seq", "mp"),
            P("seq", None),
            P("mp", "seq"),
            P(),
            P("seq", None),
            P("seq", None),
            P("seq", "mp", None),
            P("seq", "mp", None),
            P("seq", "mp", None),
        ),
        out_specs=P("seq", "mp"),
        check_vma=False,
    )
```

```python
import math

import jax
import jax.numpy as jnp
from jax import lax
from jax.sharding import PartitionSpec as P

D = 1536
HQ = 12
KVH = 2
HD = 128
WINDOW = 4096


ROPE_BASE = 1500000.0
EPSILON = 1e-06


def prompt_ids(index, lengths):
    first_end = lengths[0]
    second_end = lengths[0] + lengths[1]
    prompt = (index >= first_end).astype(jnp.int32) + (index >= second_end).astype(jnp.int32)
    begin = jnp.where(index >= second_end, second_end, jnp.where(index >= first_end, first_end, 0))
    return (prompt, index - begin)


def rotary(values, position):
    half_dim = values.shape[-1] // 2
    freqs = jnp.exp(
        jnp.arange(half_dim, dtype=jnp.float32) * (-2.0 * math.log(ROPE_BASE) / values.shape[-1])
    )
    angles = position.astype(jnp.float32)[:, None] * freqs[None, :]
    cosine = jnp.cos(angles)[:, None, :]
    sine = jnp.sin(angles)[:, None, :]
    front = values[..., :half_dim]
    latter = values[..., half_dim:]
    return jnp.concatenate(
        [front * cosine - latter * sine, latter * cosine + front * sine], axis=-1
    )


def gather_seq(piece, count):
    rows = piece.shape[0]
    spread = jnp.broadcast_to(piece[None], (count,) + piece.shape).reshape(
        count * rows, piece.shape[1]
    )
    return lax.all_to_all(spread, "seq", 0, 0, tiled=True)


def local(
    hidden_in, wq, wkv, wo, lengths, routes, gate_logits, expert_gate, expert_up, expert_down
):
    tok_rows = hidden_in.shape[0]
    seq_index = lax.axis_index("seq")
    mp_index = lax.axis_index("mp")
    seq_count = lax.axis_size("seq")
    mp_count = lax.axis_size("mp")
    heads_here = wq.shape[1] // HD
    q_cols = heads_here * HD
    kv_group = mp_index * heads_here // (HQ // KVH)

    expert_all = lax.all_gather(
        jnp.concatenate([expert_gate, expert_up, expert_down], axis=0), "mp", axis=1, tiled=True
    )

    core = mp_index % 2
    kv_col = jnp.where(core == 0, kv_group * HD, KVH * HD + kv_group * HD)
    kv_cols = lax.dynamic_slice_in_dim(wkv, kv_col, HD, 1)
    w_qkv = gather_seq(jnp.concatenate([wq, kv_cols], axis=1), seq_count)

    whole = lax.all_gather(hidden_in, "mp", axis=1, tiled=True)
    whole_f = whole.astype(jnp.float32)
    normed = (
        whole_f * lax.rsqrt(jnp.sum(whole_f * whole_f, axis=-1, keepdims=True) / D + EPSILON)
    ).astype(jnp.bfloat16)
    lin = jnp.dot(normed, w_qkv, preferred_element_type=jnp.float32)
    wo_piece, lin = lax.optimization_barrier((wo.T, lin))
    wo_cols = lax.all_to_all(gather_seq(wo_piece, seq_count), "mp", 0, 1, tiled=True)
    own_index = seq_index * tok_rows + jnp.arange(tok_rows, dtype=jnp.int32)
    _, own_pos = prompt_ids(own_index, lengths)
    queries = (
        rotary(lin[:, :q_cols].reshape(tok_rows, heads_here, HD), own_pos)
        .astype(jnp.bfloat16)
        .transpose(1, 0, 2)
    )
    kv_lin = lin[:, q_cols:]
    kv_mine = jnp.where(
        core == 0, rotary(kv_lin.reshape(tok_rows, 1, HD), own_pos)[:, 0, :], kv_lin
    ).astype(jnp.bfloat16)
    kv_other = lax.ppermute(kv_mine, "mp", [(m, m ^ 1) for m in range(mp_count)])
    key_own = jnp.where(core == 0, kv_mine, kv_other)
    value_own = jnp.where(core == 0, kv_other, kv_mine)
    kv_own = jnp.concatenate([key_own, value_own], axis=1)

    back = min((WINDOW - 1 + tok_rows - 1) // tok_rows, seq_count - 1)
    half = (back + 1) // 2
    fetched = []
    for j in range(half):
        pairs = []
        for s in range(seq_count):
            for m in range(mp_count):
                k = 2 * j + 1 + m % 2
                if s + k < seq_count:
                    pairs.append((s * mp_count + m, (s + k) * mp_count + m))
        fetched.append(lax.ppermute(kv_own, ("seq", "mp"), pairs))
    fetched = jnp.stack(fetched)
    partner = lax.ppermute(
        fetched, "mp", [(m, m ^ 1) for m in range(mp_count)]
    )
    odd = jnp.where(core == 0, fetched, partner)
    even = jnp.where(core == 0, partner, fetched)
    offsets = jnp.concatenate(
        [
            2 * jnp.arange(half, dtype=jnp.int32) + 1,
            2 * jnp.arange(half, dtype=jnp.int32) + 2,
            jnp.zeros((1,), jnp.int32),
        ]
    )
    kv_win = jnp.concatenate(
        [odd.reshape(-1, 2 * HD), even.reshape(-1, 2 * HD), kv_own], axis=0
    )
    key_rows = kv_win[:, :HD]
    value_rows = kv_win[:, HD:].astype(jnp.float32)
    key_index = (
        (seq_index - offsets)[:, None] * tok_rows + jnp.arange(tok_rows, dtype=jnp.int32)[None, :]
    ).reshape(-1)
    key_index = jnp.where(
        jnp.repeat(offsets, tok_rows) <= back, key_index, -1
    )

    scores = jnp.einsum(
        "hqd,kd->hqk", queries, key_rows, preferred_element_type=jnp.float32
    ) * HD ** (-0.5)
    query_prompt, _ = prompt_ids(own_index, lengths)
    key_prompt, _ = prompt_ids(key_index, lengths)
    spacing = own_index[:, None] - key_index[None, :]
    allowed = (
        (query_prompt[:, None] == key_prompt[None, :])
        & (spacing >= 0)
        & (spacing < WINDOW)
        & (key_index[None, :] >= 0)
    )[None]
    masked = jnp.where(allowed, scores, -1e30)
    peak = jnp.max(masked, axis=-1)
    probs = jnp.where(allowed, jnp.exp(masked - peak[..., None]), 0.0)
    total = jnp.sum(probs, axis=-1)
    accum = jnp.einsum("hqk,kd->hqd", probs, value_rows)
    attended = (
        (accum / total[..., None])
        .transpose(1, 0, 2)
        .reshape(tok_rows, q_cols)
        .astype(jnp.bfloat16)
    )
    attended_rows = lax.all_gather(attended, "mp", axis=1, tiled=True)
    attn_mine = lax.dot_general(
        attended_rows, wo_cols, (((1,), (1,)), ((), ())), preferred_element_type=jnp.float32
    )
    residual = (hidden_in.astype(jnp.float32) + attn_mine).astype(jnp.bfloat16)
    residual_f = residual.astype(jnp.float32)

    local_experts = expert_gate.shape[0]
    experts = seq_count * local_experts
    top_count = routes.shape[1]
    capacity = 2 * tok_rows * top_count // experts
    part_cap = capacity // mp_count
    pair_count = tok_rows * top_count
    flat_ids = routes.reshape(-1)
    one_hot = (flat_ids[:, None] == jnp.arange(experts, dtype=jnp.int32)[None, :]).astype(jnp.int32)
    before = (
        jnp.arange(pair_count, dtype=jnp.int32)[:, None]
        > jnp.arange(pair_count, dtype=jnp.int32)[None, :]
    ).astype(jnp.bfloat16)
    earlier_all = jnp.dot(before, one_hot.astype(jnp.bfloat16), preferred_element_type=jnp.float32)
    earlier_count = jnp.sum(earlier_all.astype(jnp.int32) * one_hot, axis=1)
    slot_index = flat_ids * capacity + earlier_count
    slots = jnp.arange(experts * capacity, dtype=jnp.int32)
    pick = (slot_index[None, :] == slots[:, None]).reshape(experts * capacity, tok_rows, top_count)
    select = jnp.sum(pick.astype(jnp.bfloat16), axis=2)
    buffer = jnp.dot(select, residual, preferred_element_type=jnp.float32).astype(jnp.bfloat16)
    arrived = lax.all_to_all(buffer, ("seq", "mp"), 0, 0, tiled=True)
    feat = D // mp_count
    arrived_rows = (
        arrived.reshape(seq_count, mp_count, part_cap, feat)
        .transpose(0, 2, 1, 3)
        .reshape(seq_count * part_cap, D)
        .astype(jnp.float32)
    )
    moe_in = (
        arrived_rows
        * lax.rsqrt(jnp.sum(arrived_rows * arrived_rows, axis=-1, keepdims=True) / D + EPSILON)
    ).astype(jnp.bfloat16)
    w_gate = expert_all[0]
    w_up = expert_all[1]
    w_down = expert_all[2]
    gate_act = lax.dot_general(
        moe_in, w_gate, (((1,), (1,)), ((), ())), preferred_element_type=jnp.float32
    )
    up_act = lax.dot_general(
        moe_in, w_up, (((1,), (1,)), ((), ())), preferred_element_type=jnp.float32
    )
    active = (jnp.maximum(gate_act, 0.0) * up_act).astype(jnp.bfloat16)
    result = jnp.dot(active, w_down, preferred_element_type=jnp.float32).astype(jnp.bfloat16)
    outgoing = (
        result.reshape(seq_count, part_cap, mp_count, feat)
        .transpose(0, 2, 1, 3)
        .reshape(seq_count * mp_count * part_cap, feat)
    )
    returned = lax.all_to_all(outgoing, ("seq", "mp"), 0, 0, tiled=True)

    gate_weights = jax.nn.softmax(gate_logits, axis=-1)
    combine = jnp.sum(
        jnp.where(
            slot_index[:, None] == slots[None, :], gate_weights.reshape(-1)[:, None], 0.0
        ).reshape(tok_rows, top_count, experts * capacity),
        axis=1,
    )
    moe_total = jnp.dot(
        combine,
        returned.astype(jnp.float32),
        precision=lax.Precision.HIGHEST,
        preferred_element_type=jnp.float32,
    )
    return (residual_f + moe_total).astype(jnp.bfloat16)


def solution(mesh):
    return jax.shard_map(
        local,
        mesh=mesh,
        in_specs=(
            P("seq", "mp"),
            P("seq", "mp"),
            P("seq", None),
            P("mp", "seq"),
            P(),
            P("seq", None),
            P("seq", None),
            P("seq", "mp", None),
            P("seq", "mp", None),
            P("seq", "mp", None),
        ),
        out_specs=P("seq", "mp"),
        check_vma=False,
    )
```

```python
import math

import jax
import jax.numpy as jnp
from jax import lax
from jax.sharding import PartitionSpec as P
from jax.experimental import pallas as pl
from jax.experimental.pallas import tpu as pltpu

D = 1536
HQ = 12
KVH = 2
HD = 128
WINDOW = 4096


ROPE_BASE = 1500000.0
EPSILON = 1e-06


def prompt_ids(index, lengths):
    first_end = lengths[0]
    second_end = lengths[0] + lengths[1]
    prompt = (index >= first_end).astype(jnp.int32) + (index >= second_end).astype(jnp.int32)
    begin = jnp.where(index >= second_end, second_end, jnp.where(index >= first_end, first_end, 0))
    return (prompt, index - begin)


def rotary(values, position):
    half_dim = values.shape[-1] // 2
    freqs = jnp.exp(
        jnp.arange(half_dim, dtype=jnp.float32) * (-2.0 * math.log(ROPE_BASE) / values.shape[-1])
    )
    angles = position.astype(jnp.float32)[:, None] * freqs[None, :]
    cosine = jnp.cos(angles)[:, None, :]
    sine = jnp.sin(angles)[:, None, :]
    front = values[..., :half_dim]
    latter = values[..., half_dim:]
    return jnp.concatenate(
        [front * cosine - latter * sine, latter * cosine + front * sine], axis=-1
    )


def attention_kernel(q_ref, k_ref, v_ref, qi_ref, qp_ref, ki_ref, kp_ref, o_ref, m_sc, l_sc, acc_sc):
    step = pl.program_id(0)

    @pl.when(step == 0)
    def _():
        m_sc[...] = jnp.full(m_sc.shape, -1e30, jnp.float32)
        l_sc[...] = jnp.zeros(l_sc.shape, jnp.float32)
        acc_sc[...] = jnp.zeros(acc_sc.shape, jnp.float32)

    scores = lax.dot_general(
        q_ref[...], k_ref[...], (((1,), (1,)), ((), ())), preferred_element_type=jnp.float32
    ) * HD ** (-0.5)
    key_at = ki_ref[...]
    spacing = qi_ref[...] - key_at
    allowed = (qp_ref[...] == kp_ref[...]) & (spacing >= 0) & (spacing < WINDOW) & (key_at >= 0)
    masked = jnp.where(allowed, scores, -1e30)
    m_old = m_sc[...]
    m_new = jnp.maximum(m_old, jnp.max(masked, axis=1, keepdims=True))
    alpha = jnp.exp(m_old - m_new)
    probs = jnp.where(allowed, jnp.exp(masked - m_new), 0.0)
    l_sc[...] = alpha * l_sc[...] + jnp.sum(probs, axis=1, keepdims=True)
    probs_hi = probs.astype(jnp.bfloat16)
    probs_lo = (probs - probs_hi.astype(jnp.float32)).astype(jnp.bfloat16)
    values = v_ref[...]
    mixed = jnp.dot(probs_hi, values, preferred_element_type=jnp.float32) + jnp.dot(
        probs_lo, values, preferred_element_type=jnp.float32
    )
    acc_sc[...] = alpha * acc_sc[...] + mixed
    m_sc[...] = m_new

    @pl.when(step == pl.num_programs(0) - 1)
    def _():
        o_ref[...] = (acc_sc[...] / l_sc[...]).astype(o_ref.dtype)


def attention(queries, keys, values, query_at, query_prompt, key_at, key_prompt, chunk):
    rows = queries.shape[0]
    steps = keys.shape[0] // chunk
    full = lambda shape: pl.BlockSpec(shape, lambda j: (0, 0))
    return pl.pallas_call(
        attention_kernel,
        grid=(steps,),
        in_specs=[
            full((rows, HD)),
            pl.BlockSpec((chunk, HD), lambda j: (j, 0)),
            pl.BlockSpec((chunk, HD), lambda j: (j, 0)),
            full((rows, 1)),
            full((rows, 1)),
            pl.BlockSpec((1, chunk), lambda j: (0, j)),
            pl.BlockSpec((1, chunk), lambda j: (0, j)),
        ],
        out_specs=full((rows, HD)),
        out_shape=jax.ShapeDtypeStruct((rows, HD), jnp.bfloat16),
        scratch_shapes=[
            pltpu.VMEM((rows, 1), jnp.float32),
            pltpu.VMEM((rows, 1), jnp.float32),
            pltpu.VMEM((rows, HD), jnp.float32),
        ],
    )(queries, keys, values, query_at, query_prompt, key_at, key_prompt)


def gather_seq(piece, count):
    rows = piece.shape[0]
    spread = jnp.broadcast_to(piece[None], (count,) + piece.shape).reshape(
        count * rows, piece.shape[1]
    )
    return lax.all_to_all(spread, "seq", 0, 0, tiled=True)


def local(
    hidden_in, wq, wkv, wo, lengths, routes, gate_logits, expert_gate, expert_up, expert_down
):
    tok_rows = hidden_in.shape[0]
    seq_index = lax.axis_index("seq")
    mp_index = lax.axis_index("mp")
    seq_count = lax.axis_size("seq")
    mp_count = lax.axis_size("mp")
    heads_here = wq.shape[1] // HD
    q_cols = heads_here * HD
    kv_group = mp_index * heads_here // (HQ // KVH)

    expert_all = lax.all_gather(
        jnp.concatenate([expert_gate, expert_up, expert_down], axis=0), "mp", axis=1, tiled=True
    )

    core = mp_index % 2
    kv_col = jnp.where(core == 0, kv_group * HD, KVH * HD + kv_group * HD)
    kv_cols = lax.dynamic_slice_in_dim(wkv, kv_col, HD, 1)
    w_qkv = gather_seq(jnp.concatenate([wq, kv_cols], axis=1), seq_count)

    whole = lax.all_gather(hidden_in, "mp", axis=1, tiled=True)
    whole_f = whole.astype(jnp.float32)
    normed = (
        whole_f * lax.rsqrt(jnp.sum(whole_f * whole_f, axis=-1, keepdims=True) / D + EPSILON)
    ).astype(jnp.bfloat16)
    lin = jnp.dot(normed, w_qkv, preferred_element_type=jnp.float32)
    wo_piece, lin = lax.optimization_barrier((wo.T, lin))
    wo_rows = gather_seq(wo_piece, seq_count)
    own_index = seq_index * tok_rows + jnp.arange(tok_rows, dtype=jnp.int32)
    _, own_pos = prompt_ids(own_index, lengths)
    queries = (
        rotary(lin[:, :q_cols].reshape(tok_rows, heads_here, HD), own_pos)
        .astype(jnp.bfloat16)
        .transpose(1, 0, 2)
    )
    kv_lin = lin[:, q_cols:]
    kv_mine = jnp.where(
        core == 0, rotary(kv_lin.reshape(tok_rows, 1, HD), own_pos)[:, 0, :], kv_lin
    ).astype(jnp.bfloat16)
    kv_other = lax.ppermute(kv_mine, "mp", [(m, m ^ 1) for m in range(mp_count)])
    key_own = jnp.where(core == 0, kv_mine, kv_other)
    value_own = jnp.where(core == 0, kv_other, kv_mine)
    kv_own = jnp.concatenate([key_own, value_own], axis=1)

    back = min((WINDOW - 1 + tok_rows - 1) // tok_rows, seq_count - 1)
    half = (back + 1) // 2
    fetched = []
    for j in range(half):
        pairs = []
        for s in range(seq_count):
            for m in range(mp_count):
                k = 2 * j + 1 + m % 2
                if s + k < seq_count:
                    pairs.append((s * mp_count + m, (s + k) * mp_count + m))
        fetched.append(lax.ppermute(kv_own, ("seq", "mp"), pairs))
    fetched = jnp.stack(fetched)
    partner = lax.ppermute(
        fetched, "mp", [(m, m ^ 1) for m in range(mp_count)]
    )
    odd = jnp.where(core == 0, fetched, partner)
    even = jnp.where(core == 0, partner, fetched)
    offsets = jnp.concatenate(
        [
            2 * jnp.arange(half, dtype=jnp.int32) + 1,
            2 * jnp.arange(half, dtype=jnp.int32) + 2,
            jnp.zeros((1,), jnp.int32),
        ]
    )
    kv_win = jnp.concatenate(
        [
            odd.reshape(-1, 2 * HD),
            even.reshape(-1, 2 * HD),
            kv_own,
            jnp.zeros((tok_rows, 2 * HD), jnp.bfloat16),
        ],
        axis=0,
    )
    key_index = (
        (seq_index - offsets)[:, None] * tok_rows + jnp.arange(tok_rows, dtype=jnp.int32)[None, :]
    ).reshape(-1)
    key_index = jnp.where(jnp.repeat(offsets, tok_rows) <= back, key_index, -1)
    key_index = jnp.concatenate([key_index, jnp.full((tok_rows,), -1, jnp.int32)])
    query_prompt, _ = prompt_ids(own_index, lengths)
    key_prompt, _ = prompt_ids(key_index, lengths)
    mixed = attention(
        queries.reshape(heads_here * tok_rows, HD),
        kv_win[:, :HD],
        kv_win[:, HD:],
        jnp.tile(own_index, heads_here)[:, None],
        jnp.tile(query_prompt, heads_here)[:, None],
        key_index[None, :],
        key_prompt[None, :],
        3 * tok_rows,
    )
    attended = (
        mixed.reshape(heads_here, tok_rows, HD).transpose(1, 0, 2).reshape(tok_rows, q_cols)
    )
    partial_out = lax.dot_general(
        attended, wo_rows, (((1,), (1,)), ((), ())), preferred_element_type=jnp.float32
    )
    swapped_out = lax.all_to_all(partial_out.astype(jnp.bfloat16), "mp", 1, 0, tiled=True)
    attn_mine = jnp.sum(
        swapped_out.reshape(mp_count, tok_rows, D // mp_count).astype(jnp.float32), axis=0
    )
    residual = (hidden_in.astype(jnp.float32) + attn_mine).astype(jnp.bfloat16)
    residual_f = residual.astype(jnp.float32)

    local_experts = expert_gate.shape[0]
    experts = seq_count * local_experts
    top_count = routes.shape[1]
    capacity = 2 * tok_rows * top_count // experts
    part_cap = capacity // mp_count
    pair_count = tok_rows * top_count
    flat_ids = routes.reshape(-1)
    one_hot = (flat_ids[:, None] == jnp.arange(experts, dtype=jnp.int32)[None, :]).astype(jnp.int32)
    before = (
        jnp.arange(pair_count, dtype=jnp.int32)[:, None]
        > jnp.arange(pair_count, dtype=jnp.int32)[None, :]
    ).astype(jnp.bfloat16)
    earlier_all = jnp.dot(before, one_hot.astype(jnp.bfloat16), preferred_element_type=jnp.float32)
    earlier_count = jnp.sum(earlier_all.astype(jnp.int32) * one_hot, axis=1)
    slot_index = flat_ids * capacity + earlier_count
    slots = jnp.arange(experts * capacity, dtype=jnp.int32)
    pick = (slot_index[None, :] == slots[:, None]).reshape(experts * capacity, tok_rows, top_count)
    select = jnp.sum(pick.astype(jnp.bfloat16), axis=2)
    buffer = jnp.dot(select, residual, preferred_element_type=jnp.float32).astype(jnp.bfloat16)
    arrived = lax.all_to_all(buffer, ("seq", "mp"), 0, 0, tiled=True)
    feat = D // mp_count
    arrived_rows = (
        arrived.reshape(seq_count, mp_count, part_cap, feat)
        .transpose(0, 2, 1, 3)
        .reshape(seq_count * part_cap, D)
        .astype(jnp.float32)
    )
    moe_in = (
        arrived_rows
        * lax.rsqrt(jnp.sum(arrived_rows * arrived_rows, axis=-1, keepdims=True) / D + EPSILON)
    ).astype(jnp.bfloat16)
    w_gate = expert_all[0]
    w_up = expert_all[1]
    w_down = expert_all[2]
    gate_act = lax.dot_general(
        moe_in, w_gate, (((1,), (1,)), ((), ())), preferred_element_type=jnp.float32
    )
    up_act = lax.dot_general(
        moe_in, w_up, (((1,), (1,)), ((), ())), preferred_element_type=jnp.float32
    )
    active = (jnp.maximum(gate_act, 0.0) * up_act).astype(jnp.bfloat16)
    result = jnp.dot(active, w_down, preferred_element_type=jnp.float32).astype(jnp.bfloat16)
    outgoing = (
        result.reshape(seq_count, part_cap, mp_count, feat)
        .transpose(0, 2, 1, 3)
        .reshape(seq_count * mp_count * part_cap, feat)
    )
    returned = lax.all_to_all(outgoing, ("seq", "mp"), 0, 0, tiled=True)

    gate_weights = jax.nn.softmax(gate_logits, axis=-1)
    combine = jnp.sum(
        jnp.where(
            slot_index[:, None] == slots[None, :], gate_weights.reshape(-1)[:, None], 0.0
        ).reshape(tok_rows, top_count, experts * capacity),
        axis=1,
    )
    moe_total = jnp.dot(
        combine,
        returned.astype(jnp.float32),
        precision=lax.Precision.HIGHEST,
        preferred_element_type=jnp.float32,
    )
    return (residual_f + moe_total).astype(jnp.bfloat16)


def solution(mesh):
    return jax.shard_map(
        local,
        mesh=mesh,
        in_specs=(
            P("seq", "mp"),
            P("seq", "mp"),
            P("seq", None),
            P("mp", "seq"),
            P(),
            P("seq", None),
            P("seq", None),
            P("seq", "mp", None),
            P("seq", "mp", None),
            P("seq", "mp", None),
        ),
        out_specs=P("seq", "mp"),
        check_vma=False,
    )
```

```python
import functools
import math

import jax
import jax.numpy as jnp
from jax import lax
from jax.sharding import PartitionSpec as P
from jax.experimental import pallas as pl
from jax.experimental.pallas import tpu as pltpu

D = 1536
HQ = 12
KVH = 2
HD = 128
WINDOW = 4096


ROPE_BASE = 1500000.0
EPSILON = 1e-06


def prompt_ids(index, lengths):
    first_end = lengths[0]
    second_end = lengths[0] + lengths[1]
    prompt = (index >= first_end).astype(jnp.int32) + (index >= second_end).astype(jnp.int32)
    begin = jnp.where(index >= second_end, second_end, jnp.where(index >= first_end, first_end, 0))
    return (prompt, index - begin)


def rotary(values, position):
    half_dim = values.shape[-1] // 2
    freqs = jnp.exp(
        jnp.arange(half_dim, dtype=jnp.float32) * (-2.0 * math.log(ROPE_BASE) / values.shape[-1])
    )
    angles = position.astype(jnp.float32)[:, None] * freqs[None, :]
    cosine = jnp.cos(angles)[:, None, :]
    sine = jnp.sin(angles)[:, None, :]
    front = values[..., :half_dim]
    latter = values[..., half_dim:]
    return jnp.concatenate(
        [front * cosine - latter * sine, latter * cosine + front * sine], axis=-1
    )


def attention_kernel(
    half, q_ref, fetched_ref, partner_ref, own_ref, qi_ref, qp_ref, ki_ref, kp_ref, o_ref, m_sc, l_sc,
    acc_sc
):
    step = pl.program_id(0)

    @pl.when(step == 0)
    def _():
        m_sc[...] = jnp.full(m_sc.shape, -1e30, jnp.float32)
        l_sc[...] = jnp.zeros(l_sc.shape, jnp.float32)
        acc_sc[...] = jnp.zeros(acc_sc.shape, jnp.float32)

    heads, rows, _ = q_ref.shape
    key_at = ki_ref[0]
    spacing = qi_ref[...] - key_at
    allowed = (qp_ref[...] == kp_ref[0]) & (spacing >= 0) & (spacing < WINDOW) & (key_at >= 0)

    def update(block):
        keys = block[:, :HD]
        values = block[:, HD:]
        scores = lax.dot_general(
            q_ref[...].reshape(heads * rows, HD), keys, (((1,), (1,)), ((), ())),
            preferred_element_type=jnp.float32,
        ).reshape(heads, rows, -1) * HD ** (-0.5)
        masked = jnp.where(allowed[None], scores, -1e30)
        m_old = m_sc[...]
        m_new = jnp.maximum(m_old, jnp.max(masked, axis=2, keepdims=True))
        alpha = jnp.exp(m_old - m_new)
        probs = jnp.where(allowed[None], jnp.exp(masked - m_new), 0.0)
        l_sc[...] = alpha * l_sc[...] + jnp.sum(probs, axis=2, keepdims=True)
        mixed = jnp.dot(
            probs.reshape(heads * rows, -1).astype(jnp.bfloat16), values,
            preferred_element_type=jnp.float32,
        ).reshape(heads, rows, HD)
        acc_sc[...] = alpha * acc_sc[...] + mixed
        m_sc[...] = m_new

    @pl.when(step < half)
    def _():
        update(fetched_ref[0])

    @pl.when((step >= half) & (step < 2 * half))
    def _():
        update(partner_ref[0])

    @pl.when(step == 2 * half)
    def _():
        update(own_ref[...])

    @pl.when(step == pl.num_programs(0) - 1)
    def _():
        o_ref[...] = (acc_sc[...] / l_sc[...]).astype(o_ref.dtype)


def attention(queries, fetched, partner, own, query_at, query_prompt, key_at, key_prompt):
    heads, rows, _ = queries.shape
    half, block, width = fetched.shape
    last = half - 1
    return pl.pallas_call(
        functools.partial(attention_kernel, half),
        grid=(2 * half + 1,),
        in_specs=[
            pl.BlockSpec((heads, rows, HD), lambda j: (0, 0, 0)),
            pl.BlockSpec((1, block, width), lambda j: (jnp.minimum(j, last), 0, 0)),
            pl.BlockSpec(
                (1, block, width), lambda j: (jnp.minimum(jnp.maximum(j - half, 0), last), 0, 0)
            ),
            pl.BlockSpec((block, width), lambda j: (0, 0)),
            pl.BlockSpec((rows, 1), lambda j: (0, 0)),
            pl.BlockSpec((rows, 1), lambda j: (0, 0)),
            pl.BlockSpec((1, 1, block), lambda j: (j, 0, 0)),
            pl.BlockSpec((1, 1, block), lambda j: (j, 0, 0)),
        ],
        out_specs=pl.BlockSpec((heads, rows, HD), lambda j: (0, 0, 0)),
        out_shape=jax.ShapeDtypeStruct((heads, rows, HD), jnp.bfloat16),
        scratch_shapes=[
            pltpu.VMEM((heads, rows, 1), jnp.float32),
            pltpu.VMEM((heads, rows, 1), jnp.float32),
            pltpu.VMEM((heads, rows, HD), jnp.float32),
        ],
    )(queries, fetched, partner, own, query_at, query_prompt, key_at, key_prompt)


def gather_seq(piece, count):
    rows = piece.shape[0]
    spread = jnp.broadcast_to(piece[None], (count,) + piece.shape).reshape(
        count * rows, piece.shape[1]
    )
    return lax.all_to_all(spread, "seq", 0, 0, tiled=True)


def local(
    hidden_in, wq, wkv, wo, lengths, routes, gate_logits, expert_gate, expert_up, expert_down
):
    tok_rows = hidden_in.shape[0]
    seq_index = lax.axis_index("seq")
    mp_index = lax.axis_index("mp")
    seq_count = lax.axis_size("seq")
    mp_count = lax.axis_size("mp")
    heads_here = wq.shape[1] // HD
    q_cols = heads_here * HD
    kv_group = mp_index * heads_here // (HQ // KVH)

    expert_all = lax.all_gather(
        jnp.concatenate([expert_gate, expert_up, expert_down], axis=0), "mp", axis=1, tiled=True
    )

    core = mp_index % 2
    kv_col = jnp.where(core == 0, kv_group * HD, KVH * HD + kv_group * HD)
    kv_cols = lax.dynamic_slice_in_dim(wkv, kv_col, HD, 1)
    w_qkv = gather_seq(jnp.concatenate([wq, kv_cols], axis=1), seq_count)

    whole = lax.all_gather(hidden_in, "mp", axis=1, tiled=True)
    whole_f = whole.astype(jnp.float32)
    normed = (
        whole_f * lax.rsqrt(jnp.sum(whole_f * whole_f, axis=-1, keepdims=True) / D + EPSILON)
    ).astype(jnp.bfloat16)
    lin = jnp.dot(normed, w_qkv, preferred_element_type=jnp.float32)
    wo_piece, lin = lax.optimization_barrier((wo.T, lin))
    wo_rows = gather_seq(wo_piece, seq_count)
    own_index = seq_index * tok_rows + jnp.arange(tok_rows, dtype=jnp.int32)
    _, own_pos = prompt_ids(own_index, lengths)
    queries = (
        rotary(lin[:, :q_cols].reshape(tok_rows, heads_here, HD), own_pos)
        .astype(jnp.bfloat16)
        .transpose(1, 0, 2)
    )
    kv_lin = lin[:, q_cols:]
    kv_mine = jnp.where(
        core == 0, rotary(kv_lin.reshape(tok_rows, 1, HD), own_pos)[:, 0, :], kv_lin
    ).astype(jnp.bfloat16)
    kv_other = lax.ppermute(kv_mine, "mp", [(m, m ^ 1) for m in range(mp_count)])
    key_own = jnp.where(core == 0, kv_mine, kv_other)
    value_own = jnp.where(core == 0, kv_other, kv_mine)
    kv_own = jnp.concatenate([key_own, value_own], axis=1)

    back = min((WINDOW - 1 + tok_rows - 1) // tok_rows, seq_count - 1)
    half = (back + 1) // 2
    fetched = []
    for j in range(half):
        pairs = []
        for s in range(seq_count):
            for m in range(mp_count):
                k = 2 * j + 1 + m % 2
                if s + k < seq_count:
                    pairs.append((s * mp_count + m, (s + k) * mp_count + m))
        fetched.append(lax.ppermute(kv_own, ("seq", "mp"), pairs))
    fetched = jnp.stack(fetched)
    partner = lax.ppermute(
        fetched, "mp", [(m, m ^ 1) for m in range(mp_count)]
    )
    fetch_offsets = 2 * jnp.arange(half, dtype=jnp.int32) + 1 + core
    partner_offsets = 2 * jnp.arange(half, dtype=jnp.int32) + 2 - core
    offsets = jnp.concatenate([fetch_offsets, partner_offsets, jnp.zeros((1,), jnp.int32)])
    key_index = (
        (seq_index - offsets)[:, None] * tok_rows + jnp.arange(tok_rows, dtype=jnp.int32)[None, :]
    )
    key_index = jnp.where((offsets <= back)[:, None], key_index, -1)
    query_prompt, _ = prompt_ids(own_index, lengths)
    key_prompt, _ = prompt_ids(key_index, lengths)
    mixed = attention(
        queries,
        fetched,
        partner,
        kv_own,
        own_index[:, None],
        query_prompt[:, None],
        key_index[:, None, :],
        key_prompt[:, None, :],
    )
    attended = mixed.transpose(1, 0, 2).reshape(tok_rows, q_cols)
    partial_out = lax.dot_general(
        attended, wo_rows, (((1,), (1,)), ((), ())), preferred_element_type=jnp.float32
    )
    swapped_out = lax.all_to_all(partial_out.astype(jnp.bfloat16), "mp", 1, 0, tiled=True)
    attn_mine = jnp.sum(
        swapped_out.reshape(mp_count, tok_rows, D // mp_count).astype(jnp.float32), axis=0
    )
    residual = (hidden_in.astype(jnp.float32) + attn_mine).astype(jnp.bfloat16)
    residual_f = residual.astype(jnp.float32)

    local_experts = expert_gate.shape[0]
    experts = seq_count * local_experts
    top_count = routes.shape[1]
    capacity = 2 * tok_rows * top_count // experts
    part_cap = capacity // mp_count
    pair_count = tok_rows * top_count
    flat_ids = routes.reshape(-1)
    one_hot = (flat_ids[:, None] == jnp.arange(experts, dtype=jnp.int32)[None, :]).astype(jnp.int32)
    before = (
        jnp.arange(pair_count, dtype=jnp.int32)[:, None]
        > jnp.arange(pair_count, dtype=jnp.int32)[None, :]
    ).astype(jnp.bfloat16)
    earlier_all = jnp.dot(before, one_hot.astype(jnp.bfloat16), preferred_element_type=jnp.float32)
    earlier_count = jnp.sum(earlier_all.astype(jnp.int32) * one_hot, axis=1)
    slot_index = flat_ids * capacity + earlier_count
    slots = jnp.arange(experts * capacity, dtype=jnp.int32)
    pick = (slot_index[None, :] == slots[:, None]).reshape(experts * capacity, tok_rows, top_count)
    select = jnp.sum(pick.astype(jnp.bfloat16), axis=2)
    buffer = jnp.dot(select, residual, preferred_element_type=jnp.float32).astype(jnp.bfloat16)
    arrived = lax.all_to_all(buffer, ("seq", "mp"), 0, 0, tiled=True)
    feat = D // mp_count
    arrived_rows = (
        arrived.reshape(seq_count, mp_count, part_cap, feat)
        .transpose(0, 2, 1, 3)
        .reshape(seq_count * part_cap, D)
        .astype(jnp.float32)
    )
    moe_in = (
        arrived_rows
        * lax.rsqrt(jnp.sum(arrived_rows * arrived_rows, axis=-1, keepdims=True) / D + EPSILON)
    ).astype(jnp.bfloat16)
    w_gate = expert_all[0]
    w_up = expert_all[1]
    w_down = expert_all[2]
    gate_act = lax.dot_general(
        moe_in, w_gate, (((1,), (1,)), ((), ())), preferred_element_type=jnp.float32
    )
    up_act = lax.dot_general(
        moe_in, w_up, (((1,), (1,)), ((), ())), preferred_element_type=jnp.float32
    )
    active = (jnp.maximum(gate_act, 0.0) * up_act).astype(jnp.bfloat16)
    result = jnp.dot(active, w_down, preferred_element_type=jnp.float32).astype(jnp.bfloat16)
    outgoing = (
        result.reshape(seq_count, part_cap, mp_count, feat)
        .transpose(0, 2, 1, 3)
        .reshape(seq_count * mp_count * part_cap, feat)
    )
    returned = lax.all_to_all(outgoing, ("seq", "mp"), 0, 0, tiled=True)

    gate_weights = jax.nn.softmax(gate_logits, axis=-1)
    combine = jnp.sum(
        jnp.where(
            slot_index[:, None] == slots[None, :], gate_weights.reshape(-1)[:, None], 0.0
        ).reshape(tok_rows, top_count, experts * capacity),
        axis=1,
    )
    moe_total = jnp.dot(
        combine,
        returned.astype(jnp.float32),
        precision=lax.Precision.HIGHEST,
        preferred_element_type=jnp.float32,
    )
    return (residual_f + moe_total).astype(jnp.bfloat16)


def solution(mesh):
    return jax.shard_map(
        local,
        mesh=mesh,
        in_specs=(
            P("seq", "mp"),
            P("seq", "mp"),
            P("seq", None),
            P("mp", "seq"),
            P(),
            P("seq", None),
            P("seq", None),
            P("seq", "mp", None),
            P("seq", "mp", None),
            P("seq", "mp", None),
        ),
        out_specs=P("seq", "mp"),
        check_vma=False,
    )
```

```python
import functools
import math

import jax
import jax.numpy as jnp
from jax import lax
from jax.sharding import PartitionSpec as P
from jax.experimental import pallas as pl
from jax.experimental.pallas import tpu as pltpu

D = 1536
HQ = 12
KVH = 2
HD = 128
WINDOW = 4096


ROPE_BASE = 1500000.0
EPSILON = 1e-06


def prompt_ids(index, lengths):
    first_end = lengths[0]
    second_end = lengths[0] + lengths[1]
    prompt = (index >= first_end).astype(jnp.int32) + (index >= second_end).astype(jnp.int32)
    begin = jnp.where(index >= second_end, second_end, jnp.where(index >= first_end, first_end, 0))
    return (prompt, index - begin)


def rotary(values, position):
    half_dim = values.shape[-1] // 2
    freqs = jnp.exp(
        jnp.arange(half_dim, dtype=jnp.float32) * (-2.0 * math.log(ROPE_BASE) / values.shape[-1])
    )
    angles = position.astype(jnp.float32)[:, None] * freqs[None, :]
    cosine = jnp.cos(angles)[:, None, :]
    sine = jnp.sin(angles)[:, None, :]
    front = values[..., :half_dim]
    latter = values[..., half_dim:]
    return jnp.concatenate(
        [front * cosine - latter * sine, latter * cosine + front * sine], axis=-1
    )


def attention_kernel(
    pairs, heads, q_ref, fetched_ref, partner_ref, own_ref, qi_ref, qp_ref, ki_ref, kp_ref, o_ref,
    m_sc, l_sc, acc_sc
):
    step = pl.program_id(0)

    @pl.when(step == 0)
    def _():
        m_sc[...] = jnp.full(m_sc.shape, -1e29, jnp.float32)
        l_sc[...] = jnp.zeros(l_sc.shape, jnp.float32)
        acc_sc[...] = jnp.zeros(acc_sc.shape, jnp.float32)

    rows = qi_ref.shape[0]
    key_at = ki_ref[0]
    spacing = qi_ref[...] - key_at
    allowed = (qp_ref[...] == kp_ref[0]) & (spacing >= 0) & (spacing < WINDOW) & (key_at >= 0)

    def update(block, allowed):
        keys = block[:, :HD]
        values = block[:, HD:]
        scores = lax.dot_general(
            q_ref[...], keys, (((1,), (1,)), ((), ())), preferred_element_type=jnp.float32
        ) * HD ** (-0.5)
        masked = jnp.concatenate(
            [jnp.where(allowed, scores[h * rows : (h + 1) * rows], -1e30) for h in range(heads)],
            axis=0,
        )
        m_old = m_sc[...]
        m_new = jnp.maximum(m_old, jnp.max(masked, axis=1, keepdims=True))
        alpha = jnp.exp(m_old - m_new)
        probs = jnp.exp(masked - m_new)
        l_sc[...] = alpha * l_sc[...] + jnp.sum(probs, axis=1, keepdims=True)
        mixed = jnp.dot(probs.astype(jnp.bfloat16), values, preferred_element_type=jnp.float32)
        acc_sc[...] = alpha * acc_sc[...] + mixed
        m_sc[...] = m_new

    width = fetched_ref.shape[2]

    @pl.when(step < pairs)
    def _():
        update(fetched_ref[...].reshape(-1, width), allowed)

    @pl.when((step >= pairs) & (step < 2 * pairs))
    def _():
        update(partner_ref[...].reshape(-1, width), allowed)

    @pl.when(step == 2 * pairs)
    def _():
        update(own_ref[...], allowed[:, : own_ref.shape[0]])

    @pl.when(step == pl.num_programs(0) - 1)
    def _():
        o_ref[...] = (acc_sc[...] / l_sc[...]).astype(o_ref.dtype)


def attention(queries, fetched, partner, own, query_at, query_prompt, key_at, key_prompt):
    heads, rows, _ = queries.shape
    half, block, width = fetched.shape
    pairs = half // 2
    last = pairs - 1
    return pl.pallas_call(
        functools.partial(attention_kernel, pairs, heads),
        grid=(2 * pairs + 1,),
        in_specs=[
            pl.BlockSpec((heads * rows, HD), lambda j: (0, 0)),
            pl.BlockSpec((2, block, width), lambda j: (jnp.minimum(j, last), 0, 0)),
            pl.BlockSpec(
                (2, block, width), lambda j: (jnp.minimum(jnp.maximum(j - pairs, 0), last), 0, 0)
            ),
            pl.BlockSpec((block, width), lambda j: (0, 0)),
            pl.BlockSpec((rows, 1), lambda j: (0, 0)),
            pl.BlockSpec((rows, 1), lambda j: (0, 0)),
            pl.BlockSpec((1, 1, 2 * block), lambda j: (j, 0, 0)),
            pl.BlockSpec((1, 1, 2 * block), lambda j: (j, 0, 0)),
        ],
        out_specs=pl.BlockSpec((heads * rows, HD), lambda j: (0, 0)),
        out_shape=jax.ShapeDtypeStruct((heads * rows, HD), jnp.bfloat16),
        scratch_shapes=[
            pltpu.VMEM((heads * rows, 1), jnp.float32),
            pltpu.VMEM((heads * rows, 1), jnp.float32),
            pltpu.VMEM((heads * rows, HD), jnp.float32),
        ],
    )(
        queries.reshape(heads * rows, HD), fetched, partner, own, query_at, query_prompt, key_at,
        key_prompt,
    ).reshape(heads, rows, HD)


def gather_seq(piece, count):
    rows = piece.shape[0]
    spread = jnp.broadcast_to(piece[None], (count,) + piece.shape).reshape(
        count * rows, piece.shape[1]
    )
    return lax.all_to_all(spread, "seq", 0, 0, tiled=True)


def local(
    hidden_in, wq, wkv, wo, lengths, routes, gate_logits, expert_gate, expert_up, expert_down
):
    tok_rows = hidden_in.shape[0]
    seq_index = lax.axis_index("seq")
    mp_index = lax.axis_index("mp")
    seq_count = lax.axis_size("seq")
    mp_count = lax.axis_size("mp")
    heads_here = wq.shape[1] // HD
    q_cols = heads_here * HD
    kv_group = mp_index * heads_here // (HQ // KVH)

    expert_all = lax.all_gather(
        jnp.concatenate([expert_gate, expert_up, expert_down], axis=0), "mp", axis=1, tiled=True
    )

    core = mp_index % 2
    kv_col = jnp.where(core == 0, kv_group * HD, KVH * HD + kv_group * HD)
    kv_cols = lax.dynamic_slice_in_dim(wkv, kv_col, HD, 1)
    w_qkv = gather_seq(jnp.concatenate([wq, kv_cols], axis=1), seq_count)

    whole = lax.all_gather(hidden_in, "mp", axis=1, tiled=True)
    whole_f = whole.astype(jnp.float32)
    normed = (
        whole_f * lax.rsqrt(jnp.sum(whole_f * whole_f, axis=-1, keepdims=True) / D + EPSILON)
    ).astype(jnp.bfloat16)
    lin = jnp.dot(normed, w_qkv, preferred_element_type=jnp.float32)
    wo_piece, lin = lax.optimization_barrier((wo.T, lin))
    wo_rows = gather_seq(wo_piece, seq_count)
    own_index = seq_index * tok_rows + jnp.arange(tok_rows, dtype=jnp.int32)
    _, own_pos = prompt_ids(own_index, lengths)
    queries = (
        rotary(lin[:, :q_cols].reshape(tok_rows, heads_here, HD), own_pos)
        .astype(jnp.bfloat16)
        .transpose(1, 0, 2)
    )
    kv_lin = lin[:, q_cols:]
    kv_mine = jnp.where(
        core == 0, rotary(kv_lin.reshape(tok_rows, 1, HD), own_pos)[:, 0, :], kv_lin
    ).astype(jnp.bfloat16)
    kv_other = lax.ppermute(kv_mine, "mp", [(m, m ^ 1) for m in range(mp_count)])
    key_own = jnp.where(core == 0, kv_mine, kv_other)
    value_own = jnp.where(core == 0, kv_other, kv_mine)
    kv_own = jnp.concatenate([key_own, value_own], axis=1)

    back = min((WINDOW - 1 + tok_rows - 1) // tok_rows, seq_count - 1)
    half = (back + 1) // 2
    fetched = []
    for j in range(half):
        pairs = []
        for s in range(seq_count):
            for m in range(mp_count):
                k = 2 * j + 1 + m % 2
                if s + k < seq_count:
                    pairs.append((s * mp_count + m, (s + k) * mp_count + m))
        fetched.append(lax.ppermute(kv_own, ("seq", "mp"), pairs))
    fetched = jnp.stack(fetched)
    partner = lax.ppermute(
        fetched, "mp", [(m, m ^ 1) for m in range(mp_count)]
    )
    fetch_offsets = 2 * jnp.arange(half, dtype=jnp.int32) + 1 + core
    partner_offsets = 2 * jnp.arange(half, dtype=jnp.int32) + 2 - core
    offsets = jnp.concatenate([fetch_offsets, partner_offsets, jnp.zeros((1,), jnp.int32)])
    key_index = (
        (seq_index - offsets)[:, None] * tok_rows + jnp.arange(tok_rows, dtype=jnp.int32)[None, :]
    )
    key_index = jnp.where((offsets <= back)[:, None], key_index, -1)
    key_index = jnp.concatenate(
        [key_index, jnp.full((1, tok_rows), -1, jnp.int32)], axis=0
    ).reshape(half + 1, 1, 2 * tok_rows)
    query_prompt, _ = prompt_ids(own_index, lengths)
    key_prompt, _ = prompt_ids(key_index, lengths)
    mixed = attention(
        queries,
        fetched,
        partner,
        kv_own,
        own_index[:, None],
        query_prompt[:, None],
        key_index,
        key_prompt,
    )
    attended = mixed.transpose(1, 0, 2).reshape(tok_rows, q_cols)
    partial_out = lax.dot_general(
        attended, wo_rows, (((1,), (1,)), ((), ())), preferred_element_type=jnp.float32
    )
    swapped_out = lax.all_to_all(partial_out.astype(jnp.bfloat16), "mp", 1, 0, tiled=True)
    attn_mine = jnp.sum(
        swapped_out.reshape(mp_count, tok_rows, D // mp_count).astype(jnp.float32), axis=0
    )
    residual = (hidden_in.astype(jnp.float32) + attn_mine).astype(jnp.bfloat16)
    residual_f = residual.astype(jnp.float32)

    local_experts = expert_gate.shape[0]
    experts = seq_count * local_experts
    top_count = routes.shape[1]
    capacity = 2 * tok_rows * top_count // experts
    part_cap = capacity // mp_count
    pair_count = tok_rows * top_count
    flat_ids = routes.reshape(-1)
    one_hot = (flat_ids[:, None] == jnp.arange(experts, dtype=jnp.int32)[None, :]).astype(jnp.int32)
    before = (
        jnp.arange(pair_count, dtype=jnp.int32)[:, None]
        > jnp.arange(pair_count, dtype=jnp.int32)[None, :]
    ).astype(jnp.bfloat16)
    earlier_all = jnp.dot(before, one_hot.astype(jnp.bfloat16), preferred_element_type=jnp.float32)
    earlier_count = jnp.sum(earlier_all.astype(jnp.int32) * one_hot, axis=1)
    slot_index = flat_ids * capacity + earlier_count
    slots = jnp.arange(experts * capacity, dtype=jnp.int32)
    pick = (slot_index[None, :] == slots[:, None]).reshape(experts * capacity, tok_rows, top_count)
    select = jnp.sum(pick.astype(jnp.bfloat16), axis=2)
    buffer = jnp.dot(select, residual, preferred_element_type=jnp.float32).astype(jnp.bfloat16)
    arrived = lax.all_to_all(buffer, ("seq", "mp"), 0, 0, tiled=True)
    feat = D // mp_count
    arrived_rows = (
        arrived.reshape(seq_count, mp_count, part_cap, feat)
        .transpose(0, 2, 1, 3)
        .reshape(seq_count * part_cap, D)
        .astype(jnp.float32)
    )
    moe_in = (
        arrived_rows
        * lax.rsqrt(jnp.sum(arrived_rows * arrived_rows, axis=-1, keepdims=True) / D + EPSILON)
    ).astype(jnp.bfloat16)
    w_gate = expert_all[0]
    w_up = expert_all[1]
    w_down = expert_all[2]
    gate_act = lax.dot_general(
        moe_in, w_gate, (((1,), (1,)), ((), ())), preferred_element_type=jnp.float32
    )
    up_act = lax.dot_general(
        moe_in, w_up, (((1,), (1,)), ((), ())), preferred_element_type=jnp.float32
    )
    active = (jnp.maximum(gate_act, 0.0) * up_act).astype(jnp.bfloat16)
    result = jnp.dot(active, w_down, preferred_element_type=jnp.float32).astype(jnp.bfloat16)
    outgoing = (
        result.reshape(seq_count, part_cap, mp_count, feat)
        .transpose(0, 2, 1, 3)
        .reshape(seq_count * mp_count * part_cap, feat)
    )
    returned = lax.all_to_all(outgoing, ("seq", "mp"), 0, 0, tiled=True)

    gate_weights = jax.nn.softmax(gate_logits, axis=-1)
    combine = jnp.sum(
        jnp.where(
            slot_index[:, None] == slots[None, :], gate_weights.reshape(-1)[:, None], 0.0
        ).reshape(tok_rows, top_count, experts * capacity),
        axis=1,
    )
    moe_total = jnp.dot(
        combine,
        returned.astype(jnp.float32),
        precision=lax.Precision.HIGHEST,
        preferred_element_type=jnp.float32,
    )
    return (residual_f + moe_total).astype(jnp.bfloat16)


def solution(mesh):
    return jax.shard_map(
        local,
        mesh=mesh,
        in_specs=(
            P("seq", "mp"),
            P("seq", "mp"),
            P("seq", None),
            P("mp", "seq"),
            P(),
            P("seq", None),
            P("seq", None),
            P("seq", "mp", None),
            P("seq", "mp", None),
            P("seq", "mp", None),
        ),
        out_specs=P("seq", "mp"),
        check_vma=False,
    )
```

```python
import math

import jax
import jax.numpy as jnp
from jax import lax
from jax.sharding import PartitionSpec as P

D = 1536
HQ = 12
KVH = 2
HD = 128
WINDOW = 4096


ROPE_BASE = 1500000.0
EPSILON = 1e-06


def prompt_ids(index, lengths):
    first_end = lengths[0]
    second_end = lengths[0] + lengths[1]
    prompt = (index >= first_end).astype(jnp.int32) + (index >= second_end).astype(jnp.int32)
    begin = jnp.where(index >= second_end, second_end, jnp.where(index >= first_end, first_end, 0))
    return (prompt, index - begin)


def rotary(values, position):
    half_dim = values.shape[-1] // 2
    freqs = jnp.exp(
        jnp.arange(half_dim, dtype=jnp.float32) * (-2.0 * math.log(ROPE_BASE) / values.shape[-1])
    )
    angles = position.astype(jnp.float32)[:, None] * freqs[None, :]
    cosine = jnp.cos(angles)[:, None, :]
    sine = jnp.sin(angles)[:, None, :]
    front = values[..., :half_dim]
    latter = values[..., half_dim:]
    return jnp.concatenate(
        [front * cosine - latter * sine, latter * cosine + front * sine], axis=-1
    )


def gather_seq(piece, count):
    rows = piece.shape[0]
    spread = jnp.broadcast_to(piece[None], (count,) + piece.shape).reshape(
        count * rows, piece.shape[1]
    )
    return lax.all_to_all(spread, "seq", 0, 0, tiled=True)


def local(
    hidden_in, wq, wkv, wo, lengths, routes, gate_logits, expert_gate, expert_up, expert_down
):
    tok_rows = hidden_in.shape[0]
    seq_index = lax.axis_index("seq")
    mp_index = lax.axis_index("mp")
    seq_count = lax.axis_size("seq")
    mp_count = lax.axis_size("mp")
    heads_here = wq.shape[1] // HD
    q_cols = heads_here * HD
    kv_group = mp_index * heads_here // (HQ // KVH)

    expert_all = lax.all_gather(
        jnp.concatenate([expert_gate, expert_up, expert_down], axis=0), "mp", axis=1, tiled=True
    )

    core = mp_index % 2
    kv_col = jnp.where(core == 0, kv_group * HD, KVH * HD + kv_group * HD)
    kv_cols = lax.dynamic_slice_in_dim(wkv, kv_col, HD, 1)
    w_qkv = gather_seq(jnp.concatenate([wq, kv_cols], axis=1), seq_count)

    whole = lax.all_gather(hidden_in, "mp", axis=1, tiled=True)
    whole_f = whole.astype(jnp.float32)
    normed = (
        whole_f * lax.rsqrt(jnp.sum(whole_f * whole_f, axis=-1, keepdims=True) / D + EPSILON)
    ).astype(jnp.bfloat16)
    lin = jnp.dot(normed, w_qkv, preferred_element_type=jnp.float32)
    wo_rows = lax.all_gather(wo.T, "seq", axis=0, tiled=True)
    own_index = seq_index * tok_rows + jnp.arange(tok_rows, dtype=jnp.int32)
    _, own_pos = prompt_ids(own_index, lengths)
    queries = (
        rotary(lin[:, :q_cols].reshape(tok_rows, heads_here, HD), own_pos)
        .astype(jnp.bfloat16)
        .transpose(1, 0, 2)
    )
    kv_lin = lin[:, q_cols:]
    kv_mine = jnp.where(
        core == 0, rotary(kv_lin.reshape(tok_rows, 1, HD), own_pos)[:, 0, :], kv_lin
    ).astype(jnp.bfloat16)
    kv_other = lax.ppermute(kv_mine, "mp", [(m, m ^ 1) for m in range(mp_count)])
    key_own = jnp.where(core == 0, kv_mine, kv_other)
    value_own = jnp.where(core == 0, kv_other, kv_mine)
    kv_own = jnp.concatenate([key_own, value_own], axis=1)

    back = min((WINDOW - 1 + tok_rows - 1) // tok_rows, seq_count - 1)
    half = (back + 1) // 2
    fetched = []
    for j in range(half):
        pairs = []
        for s in range(seq_count):
            for m in range(mp_count):
                k = 2 * j + 1 + m % 2
                if s + k < seq_count:
                    pairs.append((s * mp_count + m, (s + k) * mp_count + m))
        fetched.append(lax.ppermute(kv_own, ("seq", "mp"), pairs))
    fetched = jnp.stack(fetched)
    partner = lax.ppermute(
        fetched, "mp", [(m, m ^ 1) for m in range(mp_count)]
    )
    odd = jnp.where(core == 0, fetched, partner)
    even = jnp.where(core == 0, partner, fetched)
    offsets = jnp.concatenate(
        [
            2 * jnp.arange(half, dtype=jnp.int32) + 1,
            2 * jnp.arange(half, dtype=jnp.int32) + 2,
            jnp.zeros((1,), jnp.int32),
        ]
    )
    kv_win = jnp.concatenate(
        [odd.reshape(-1, 2 * HD), even.reshape(-1, 2 * HD), kv_own], axis=0
    )
    key_rows = kv_win[:, :HD]
    value_rows = kv_win[:, HD:].astype(jnp.float32)
    key_index = (
        (seq_index - offsets)[:, None] * tok_rows + jnp.arange(tok_rows, dtype=jnp.int32)[None, :]
    ).reshape(-1)
    key_index = jnp.where(
        jnp.repeat(offsets, tok_rows) <= back, key_index, -1
    )

    scores = jnp.einsum(
        "hqd,kd->hqk", queries, key_rows, preferred_element_type=jnp.float32
    ) * HD ** (-0.5)
    query_prompt, _ = prompt_ids(own_index, lengths)
    key_prompt, _ = prompt_ids(key_index, lengths)
    spacing = own_index[:, None] - key_index[None, :]
    allowed = (
        (query_prompt[:, None] == key_prompt[None, :])
        & (spacing >= 0)
        & (spacing < WINDOW)
        & (key_index[None, :] >= 0)
    )[None]
    masked = jnp.where(allowed, scores, -1e30)
    peak = jnp.max(masked, axis=-1)
    probs = jnp.where(allowed, jnp.exp(masked - peak[..., None]), 0.0)
    total = jnp.sum(probs, axis=-1)
    accum = jnp.einsum("hqk,kd->hqd", probs, value_rows)
    attended = (
        (accum / total[..., None])
        .transpose(1, 0, 2)
        .reshape(tok_rows, q_cols)
        .astype(jnp.bfloat16)
    )
    partial_out = lax.dot_general(
        attended, wo_rows, (((1,), (1,)), ((), ())), preferred_element_type=jnp.float32
    )
    swapped_out = lax.all_to_all(partial_out.astype(jnp.bfloat16), "mp", 1, 0, tiled=True)
    attn_mine = jnp.sum(
        swapped_out.reshape(mp_count, tok_rows, D // mp_count).astype(jnp.float32), axis=0
    )
    residual = (hidden_in.astype(jnp.float32) + attn_mine).astype(jnp.bfloat16)
    residual_f = residual.astype(jnp.float32)

    local_experts = expert_gate.shape[0]
    experts = seq_count * local_experts
    top_count = routes.shape[1]
    capacity = 2 * tok_rows * top_count // experts
    part_cap = capacity // mp_count
    pair_count = tok_rows * top_count
    flat_ids = routes.reshape(-1)
    one_hot = (flat_ids[:, None] == jnp.arange(experts, dtype=jnp.int32)[None, :]).astype(jnp.int32)
    before = (
        jnp.arange(pair_count, dtype=jnp.int32)[:, None]
        > jnp.arange(pair_count, dtype=jnp.int32)[None, :]
    ).astype(jnp.bfloat16)
    earlier_all = jnp.dot(before, one_hot.astype(jnp.bfloat16), preferred_element_type=jnp.float32)
    earlier_count = jnp.sum(earlier_all.astype(jnp.int32) * one_hot, axis=1)
    slot_index = flat_ids * capacity + earlier_count
    slots = jnp.arange(experts * capacity, dtype=jnp.int32)
    pick = (slot_index[None, :] == slots[:, None]).reshape(experts * capacity, tok_rows, top_count)
    select = jnp.sum(pick.astype(jnp.bfloat16), axis=2)
    buffer = jnp.dot(select, residual, preferred_element_type=jnp.float32).astype(jnp.bfloat16)
    arrived = lax.all_to_all(buffer, ("seq", "mp"), 0, 0, tiled=True)
    feat = D // mp_count
    arrived_rows = (
        arrived.reshape(seq_count, mp_count, part_cap, feat)
        .transpose(0, 2, 1, 3)
        .reshape(seq_count * part_cap, D)
        .astype(jnp.float32)
    )
    moe_in = (
        arrived_rows
        * lax.rsqrt(jnp.sum(arrived_rows * arrived_rows, axis=-1, keepdims=True) / D + EPSILON)
    ).astype(jnp.bfloat16)
    w_gate = expert_all[0]
    w_up = expert_all[1]
    w_down = expert_all[2]
    gate_act = lax.dot_general(
        moe_in, w_gate, (((1,), (1,)), ((), ())), preferred_element_type=jnp.float32
    )
    up_act = lax.dot_general(
        moe_in, w_up, (((1,), (1,)), ((), ())), preferred_element_type=jnp.float32
    )
    active = (jnp.maximum(gate_act, 0.0) * up_act).astype(jnp.bfloat16)
    result = jnp.dot(active, w_down, preferred_element_type=jnp.float32).astype(jnp.bfloat16)
    outgoing = (
        result.reshape(seq_count, part_cap, mp_count, feat)
        .transpose(0, 2, 1, 3)
        .reshape(seq_count * mp_count * part_cap, feat)
    )
    returned = lax.all_to_all(outgoing, ("seq", "mp"), 0, 0, tiled=True)

    gate_weights = jax.nn.softmax(gate_logits, axis=-1)
    combine = jnp.sum(
        jnp.where(
            slot_index[:, None] == slots[None, :], gate_weights.reshape(-1)[:, None], 0.0
        ).reshape(tok_rows, top_count, experts * capacity),
        axis=1,
    )
    moe_total = jnp.dot(
        combine,
        returned.astype(jnp.float32),
        precision=lax.Precision.HIGHEST,
        preferred_element_type=jnp.float32,
    )
    return (residual_f + moe_total).astype(jnp.bfloat16)


def solution(mesh):
    return jax.shard_map(
        local,
        mesh=mesh,
        in_specs=(
            P("seq", "mp"),
            P("seq", "mp"),
            P("seq", None),
            P("mp", "seq"),
            P(),
            P("seq", None),
            P("seq", None),
            P("seq", "mp", None),
            P("seq", "mp", None),
            P("seq", "mp", None),
        ),
        out_specs=P("seq", "mp"),
        check_vma=False,
    )
```

```python
import math

import jax
import jax.numpy as jnp
from jax import lax
from jax.sharding import PartitionSpec as P

D = 1536
HQ = 12
KVH = 2
HD = 128
WINDOW = 4096


ROPE_BASE = 1500000.0
EPSILON = 1e-06


def prompt_ids(index, lengths):
    first_end = lengths[0]
    second_end = lengths[0] + lengths[1]
    prompt = (index >= first_end).astype(jnp.int32) + (index >= second_end).astype(jnp.int32)
    begin = jnp.where(index >= second_end, second_end, jnp.where(index >= first_end, first_end, 0))
    return (prompt, index - begin)


def rotary(values, position):
    half_dim = values.shape[-1] // 2
    freqs = jnp.exp(
        jnp.arange(half_dim, dtype=jnp.float32) * (-2.0 * math.log(ROPE_BASE) / values.shape[-1])
    )
    angles = position.astype(jnp.float32)[:, None] * freqs[None, :]
    cosine = jnp.cos(angles)[:, None, :]
    sine = jnp.sin(angles)[:, None, :]
    front = values[..., :half_dim]
    latter = values[..., half_dim:]
    return jnp.concatenate(
        [front * cosine - latter * sine, latter * cosine + front * sine], axis=-1
    )


def gather_seq(piece, count):
    rows = piece.shape[0]
    spread = jnp.broadcast_to(piece[None], (count,) + piece.shape).reshape(
        count * rows, piece.shape[1]
    )
    return lax.all_to_all(spread, "seq", 0, 0, tiled=True)


def local(
    hidden_in, wq, wkv, wo, lengths, routes, gate_logits, expert_gate, expert_up, expert_down
):
    tok_rows = hidden_in.shape[0]
    seq_index = lax.axis_index("seq")
    mp_index = lax.axis_index("mp")
    seq_count = lax.axis_size("seq")
    mp_count = lax.axis_size("mp")
    heads_here = wq.shape[1] // HD
    q_cols = heads_here * HD
    kv_group = mp_index * heads_here // (HQ // KVH)

    expert_own = jnp.concatenate([expert_gate, expert_up, expert_down], axis=0)
    across = lax.ppermute(expert_own, "mp", [(m, m ^ 2) for m in range(mp_count)])

    core = mp_index % 2
    kv_col = jnp.where(core == 0, kv_group * HD, KVH * HD + kv_group * HD)
    kv_cols = lax.dynamic_slice_in_dim(wkv, kv_col, HD, 1)
    w_qkv = gather_seq(jnp.concatenate([wq, kv_cols], axis=1), seq_count)

    whole = lax.all_gather(hidden_in, "mp", axis=1, tiled=True)
    whole_f = whole.astype(jnp.float32)
    normed = (
        whole_f * lax.rsqrt(jnp.sum(whole_f * whole_f, axis=-1, keepdims=True) / D + EPSILON)
    ).astype(jnp.bfloat16)
    lin = jnp.dot(normed, w_qkv, preferred_element_type=jnp.float32)
    across, lin = lax.optimization_barrier((across, lin))
    beside = lax.ppermute(
        jnp.stack([expert_own, across]), "mp", [(m, m ^ 1) for m in range(mp_count)]
    )
    expert_pieces = [expert_own, across, beside[0], beside[1]]
    wo_rows = lax.all_gather(wo.T, "seq", axis=0, tiled=True)
    own_index = seq_index * tok_rows + jnp.arange(tok_rows, dtype=jnp.int32)
    _, own_pos = prompt_ids(own_index, lengths)
    queries = (
        rotary(lin[:, :q_cols].reshape(tok_rows, heads_here, HD), own_pos)
        .astype(jnp.bfloat16)
        .transpose(1, 0, 2)
    )
    kv_lin = lin[:, q_cols:]
    kv_mine = jnp.where(
        core == 0, rotary(kv_lin.reshape(tok_rows, 1, HD), own_pos)[:, 0, :], kv_lin
    ).astype(jnp.bfloat16)
    kv_other = lax.ppermute(kv_mine, "mp", [(m, m ^ 1) for m in range(mp_count)])
    key_own = jnp.where(core == 0, kv_mine, kv_other)
    value_own = jnp.where(core == 0, kv_other, kv_mine)
    kv_own = jnp.concatenate([key_own, value_own], axis=1)

    back = min((WINDOW - 1 + tok_rows - 1) // tok_rows, seq_count - 1)
    half = (back + 1) // 2
    fetched = []
    for j in range(half):
        pairs = []
        for s in range(seq_count):
            for m in range(mp_count):
                k = 2 * j + 1 + m % 2
                if s + k < seq_count:
                    pairs.append((s * mp_count + m, (s + k) * mp_count + m))
        fetched.append(lax.ppermute(kv_own, ("seq", "mp"), pairs))
    fetched = jnp.stack(fetched)
    partner = lax.ppermute(
        fetched, "mp", [(m, m ^ 1) for m in range(mp_count)]
    )
    odd = jnp.where(core == 0, fetched, partner)
    even = jnp.where(core == 0, partner, fetched)
    offsets = jnp.concatenate(
        [
            2 * jnp.arange(half, dtype=jnp.int32) + 1,
            2 * jnp.arange(half, dtype=jnp.int32) + 2,
            jnp.zeros((1,), jnp.int32),
        ]
    )
    kv_win = jnp.concatenate(
        [odd.reshape(-1, 2 * HD), even.reshape(-1, 2 * HD), kv_own], axis=0
    )
    key_rows = kv_win[:, :HD]
    value_rows = kv_win[:, HD:].astype(jnp.float32)
    key_index = (
        (seq_index - offsets)[:, None] * tok_rows + jnp.arange(tok_rows, dtype=jnp.int32)[None, :]
    ).reshape(-1)
    key_index = jnp.where(
        jnp.repeat(offsets, tok_rows) <= back, key_index, -1
    )

    scores = jnp.einsum(
        "hqd,kd->hqk", queries, key_rows, preferred_element_type=jnp.float32
    ) * HD ** (-0.5)
    query_prompt, _ = prompt_ids(own_index, lengths)
    key_prompt, _ = prompt_ids(key_index, lengths)
    spacing = own_index[:, None] - key_index[None, :]
    allowed = (
        (query_prompt[:, None] == key_prompt[None, :])
        & (spacing >= 0)
        & (spacing < WINDOW)
        & (key_index[None, :] >= 0)
    )[None]
    masked = jnp.where(allowed, scores, -1e30)
    peak = jnp.max(masked, axis=-1)
    probs = jnp.where(allowed, jnp.exp(masked - peak[..., None]), 0.0)
    total = jnp.sum(probs, axis=-1)
    accum = jnp.einsum("hqk,kd->hqd", probs, value_rows)
    attended = (
        (accum / total[..., None])
        .transpose(1, 0, 2)
        .reshape(tok_rows, q_cols)
        .astype(jnp.bfloat16)
    )
    partial_out = lax.dot_general(
        attended, wo_rows, (((1,), (1,)), ((), ())), preferred_element_type=jnp.float32
    )
    swapped_out = lax.all_to_all(partial_out.astype(jnp.bfloat16), "mp", 1, 0, tiled=True)
    attn_mine = jnp.sum(
        swapped_out.reshape(mp_count, tok_rows, D // mp_count).astype(jnp.float32), axis=0
    )
    residual = (hidden_in.astype(jnp.float32) + attn_mine).astype(jnp.bfloat16)
    residual_f = residual.astype(jnp.float32)

    local_experts = expert_gate.shape[0]
    experts = seq_count * local_experts
    top_count = routes.shape[1]
    capacity = 2 * tok_rows * top_count // experts
    part_cap = capacity // mp_count
    pair_count = tok_rows * top_count
    flat_ids = routes.reshape(-1)
    one_hot = (flat_ids[:, None] == jnp.arange(experts, dtype=jnp.int32)[None, :]).astype(jnp.int32)
    before = (
        jnp.arange(pair_count, dtype=jnp.int32)[:, None]
        > jnp.arange(pair_count, dtype=jnp.int32)[None, :]
    ).astype(jnp.bfloat16)
    earlier_all = jnp.dot(before, one_hot.astype(jnp.bfloat16), preferred_element_type=jnp.float32)
    earlier_count = jnp.sum(earlier_all.astype(jnp.int32) * one_hot, axis=1)
    slot_index = flat_ids * capacity + earlier_count
    slots = jnp.arange(experts * capacity, dtype=jnp.int32)
    pick = (slot_index[None, :] == slots[:, None]).reshape(experts * capacity, tok_rows, top_count)
    select = jnp.sum(pick.astype(jnp.bfloat16), axis=2)
    buffer = jnp.dot(select, residual, preferred_element_type=jnp.float32).astype(jnp.bfloat16)
    arrived = lax.all_to_all(buffer, ("seq", "mp"), 0, 0, tiled=True)
    feat = D // mp_count
    arrived_rows = (
        arrived.reshape(seq_count, mp_count, part_cap, feat)
        .transpose(0, 2, 1, 3)
        .reshape(seq_count * part_cap, D)
        .astype(jnp.float32)
    )
    moe_in = (
        arrived_rows
        * lax.rsqrt(jnp.sum(arrived_rows * arrived_rows, axis=-1, keepdims=True) / D + EPSILON)
    ).astype(jnp.bfloat16)
    result_f = None
    for piece in expert_pieces:
        gate_act = lax.dot_general(
            moe_in, piece[0], (((1,), (1,)), ((), ())), preferred_element_type=jnp.float32
        )
        up_act = lax.dot_general(
            moe_in, piece[1], (((1,), (1,)), ((), ())), preferred_element_type=jnp.float32
        )
        active = (jnp.maximum(gate_act, 0.0) * up_act).astype(jnp.bfloat16)
        part = jnp.dot(active, piece[2], preferred_element_type=jnp.float32)
        result_f = part if result_f is None else result_f + part
    result = result_f.astype(jnp.bfloat16)
    outgoing = (
        result.reshape(seq_count, part_cap, mp_count, feat)
        .transpose(0, 2, 1, 3)
        .reshape(seq_count * mp_count * part_cap, feat)
    )
    returned = lax.all_to_all(outgoing, ("seq", "mp"), 0, 0, tiled=True)

    gate_weights = jax.nn.softmax(gate_logits, axis=-1)
    combine = jnp.sum(
        jnp.where(
            slot_index[:, None] == slots[None, :], gate_weights.reshape(-1)[:, None], 0.0
        ).reshape(tok_rows, top_count, experts * capacity),
        axis=1,
    )
    moe_total = jnp.dot(
        combine,
        returned.astype(jnp.float32),
        precision=lax.Precision.HIGHEST,
        preferred_element_type=jnp.float32,
    )
    return (residual_f + moe_total).astype(jnp.bfloat16)


def solution(mesh):
    return jax.shard_map(
        local,
        mesh=mesh,
        in_specs=(
            P("seq", "mp"),
            P("seq", "mp"),
            P("seq", None),
            P("mp", "seq"),
            P(),
            P("seq", None),
            P("seq", None),
            P("seq", "mp", None),
            P("seq", "mp", None),
            P("seq", "mp", None),
        ),
        out_specs=P("seq", "mp"),
        check_vma=False,
    )
```

```python
import functools
import math

import jax
import jax.numpy as jnp
from jax import lax
from jax.sharding import PartitionSpec as P
from jax.experimental import pallas as pl
from jax.experimental.pallas import tpu as pltpu

D = 1536
HQ = 12
KVH = 2
HD = 128
WINDOW = 4096


ROPE_BASE = 1500000.0
EPSILON = 1e-06


def prompt_ids(index, lengths):
    first_end = lengths[0]
    second_end = lengths[0] + lengths[1]
    prompt = (index >= first_end).astype(jnp.int32) + (index >= second_end).astype(jnp.int32)
    begin = jnp.where(index >= second_end, second_end, jnp.where(index >= first_end, first_end, 0))
    return (prompt, index - begin)


def rotary(values, position):
    half_dim = values.shape[-1] // 2
    freqs = jnp.exp(
        jnp.arange(half_dim, dtype=jnp.float32) * (-2.0 * math.log(ROPE_BASE) / values.shape[-1])
    )
    angles = position.astype(jnp.float32)[:, None] * freqs[None, :]
    cosine = jnp.cos(angles)[:, None, :]
    sine = jnp.sin(angles)[:, None, :]
    front = values[..., :half_dim]
    latter = values[..., half_dim:]
    return jnp.concatenate(
        [front * cosine - latter * sine, latter * cosine + front * sine], axis=-1
    )


def attention_kernel(
    pairs, q_ref, fetched_ref, partner_ref, own_ref, qi_ref, qp_ref, ki_ref, kp_ref, o_ref,
    m_sc, l_sc, acc_sc
):
    step = pl.program_id(0)

    @pl.when(step == 0)
    def _():
        m_sc[...] = jnp.full(m_sc.shape, -1e29, jnp.float32)
        l_sc[...] = jnp.zeros(l_sc.shape, jnp.float32)
        acc_sc[...] = jnp.zeros(acc_sc.shape, jnp.float32)

    key_at = ki_ref[...]
    spacing = qi_ref[...] - key_at
    allowed = (qp_ref[...] == kp_ref[...]) & (spacing >= 0) & (spacing < WINDOW) & (key_at >= 0)

    def update(block, allowed):
        keys = block[:, :HD]
        values = block[:, HD:]
        scores = lax.dot_general(
            keys, q_ref[...], (((1,), (1,)), ((), ())), preferred_element_type=jnp.float32
        ) * HD ** (-0.5)
        masked = jnp.where(allowed, scores, -1e30)
        m_old = m_sc[...]
        m_new = jnp.maximum(m_old, jnp.max(masked, axis=0, keepdims=True))
        alpha = jnp.exp(m_old - m_new)
        probs = jnp.exp(masked - m_new)
        l_sc[...] = alpha * l_sc[...] + jnp.sum(probs, axis=0, keepdims=True)
        mixed = lax.dot_general(
            values, probs.astype(jnp.bfloat16), (((0,), (0,)), ((), ())),
            preferred_element_type=jnp.float32,
        )
        acc_sc[...] = alpha * acc_sc[...] + mixed
        m_sc[...] = m_new

    width = fetched_ref.shape[2]

    @pl.when(step < pairs)
    def _():
        update(fetched_ref[...].reshape(-1, width), allowed)

    @pl.when((step >= pairs) & (step < 2 * pairs))
    def _():
        update(partner_ref[...].reshape(-1, width), allowed)

    @pl.when(step == 2 * pairs)
    def _():
        update(own_ref[...], allowed[: own_ref.shape[0]])

    @pl.when(step == pl.num_programs(0) - 1)
    def _():
        o_ref[...] = (acc_sc[...] / l_sc[...]).astype(o_ref.dtype)


def attention(queries, fetched, partner, own, query_at, query_prompt, key_at, key_prompt):
    heads, rows, _ = queries.shape
    half, block, width = fetched.shape
    pairs = half // 2
    last = pairs - 1
    cols = heads * rows
    out_t = pl.pallas_call(
        functools.partial(attention_kernel, pairs),
        grid=(2 * pairs + 1,),
        in_specs=[
            pl.BlockSpec((cols, HD), lambda j: (0, 0)),
            pl.BlockSpec((2, block, width), lambda j: (jnp.minimum(j, last), 0, 0)),
            pl.BlockSpec(
                (2, block, width), lambda j: (jnp.minimum(jnp.maximum(j - pairs, 0), last), 0, 0)
            ),
            pl.BlockSpec((block, width), lambda j: (0, 0)),
            pl.BlockSpec((1, cols), lambda j: (0, 0)),
            pl.BlockSpec((1, cols), lambda j: (0, 0)),
            pl.BlockSpec((2 * block, 1), lambda j: (j, 0)),
            pl.BlockSpec((2 * block, 1), lambda j: (j, 0)),
        ],
        out_specs=pl.BlockSpec((HD, cols), lambda j: (0, 0)),
        out_shape=jax.ShapeDtypeStruct((HD, cols), jnp.bfloat16),
        scratch_shapes=[
            pltpu.VMEM((1, cols), jnp.float32),
            pltpu.VMEM((1, cols), jnp.float32),
            pltpu.VMEM((HD, cols), jnp.float32),
        ],
    )(
        queries.reshape(cols, HD), fetched, partner, own,
        jnp.tile(query_at, heads)[None, :], jnp.tile(query_prompt, heads)[None, :],
        key_at.reshape(-1, 1), key_prompt.reshape(-1, 1),
    )
    return out_t.T.reshape(heads, rows, HD)


def gather_seq(piece, count):
    rows = piece.shape[0]
    spread = jnp.broadcast_to(piece[None], (count,) + piece.shape).reshape(
        count * rows, piece.shape[1]
    )
    return lax.all_to_all(spread, "seq", 0, 0, tiled=True)


def local(
    hidden_in, wq, wkv, wo, lengths, routes, gate_logits, expert_gate, expert_up, expert_down
):
    tok_rows = hidden_in.shape[0]
    seq_index = lax.axis_index("seq")
    mp_index = lax.axis_index("mp")
    seq_count = lax.axis_size("seq")
    mp_count = lax.axis_size("mp")
    heads_here = wq.shape[1] // HD
    q_cols = heads_here * HD
    kv_group = mp_index * heads_here // (HQ // KVH)

    expert_all = lax.all_gather(
        jnp.concatenate([expert_gate, expert_up, expert_down], axis=0), "mp", axis=1, tiled=True
    )

    core = mp_index % 2
    kv_col = jnp.where(core == 0, kv_group * HD, KVH * HD + kv_group * HD)
    kv_cols = lax.dynamic_slice_in_dim(wkv, kv_col, HD, 1)
    w_qkv = gather_seq(jnp.concatenate([wq, kv_cols], axis=1), seq_count)

    whole = lax.all_gather(hidden_in, "mp", axis=1, tiled=True)
    whole_f = whole.astype(jnp.float32)
    normed = (
        whole_f * lax.rsqrt(jnp.sum(whole_f * whole_f, axis=-1, keepdims=True) / D + EPSILON)
    ).astype(jnp.bfloat16)
    lin = jnp.dot(normed, w_qkv, preferred_element_type=jnp.float32)
    wo_piece, lin = lax.optimization_barrier((wo.T, lin))
    wo_rows = gather_seq(wo_piece, seq_count)
    own_index = seq_index * tok_rows + jnp.arange(tok_rows, dtype=jnp.int32)
    _, own_pos = prompt_ids(own_index, lengths)
    queries = (
        rotary(lin[:, :q_cols].reshape(tok_rows, heads_here, HD), own_pos)
        .astype(jnp.bfloat16)
        .transpose(1, 0, 2)
    )
    kv_lin = lin[:, q_cols:]
    kv_mine = jnp.where(
        core == 0, rotary(kv_lin.reshape(tok_rows, 1, HD), own_pos)[:, 0, :], kv_lin
    ).astype(jnp.bfloat16)
    kv_other = lax.ppermute(kv_mine, "mp", [(m, m ^ 1) for m in range(mp_count)])
    key_own = jnp.where(core == 0, kv_mine, kv_other)
    value_own = jnp.where(core == 0, kv_other, kv_mine)
    kv_own = jnp.concatenate([key_own, value_own], axis=1)

    back = min((WINDOW - 1 + tok_rows - 1) // tok_rows, seq_count - 1)
    half = (back + 1) // 2
    fetched = []
    for j in range(half):
        pairs = []
        for s in range(seq_count):
            for m in range(mp_count):
                k = 2 * j + 1 + m % 2
                if s + k < seq_count:
                    pairs.append((s * mp_count + m, (s + k) * mp_count + m))
        fetched.append(lax.ppermute(kv_own, ("seq", "mp"), pairs))
    fetched = jnp.stack(fetched)
    partner = lax.ppermute(
        fetched, "mp", [(m, m ^ 1) for m in range(mp_count)]
    )
    fetch_offsets = 2 * jnp.arange(half, dtype=jnp.int32) + 1 + core
    partner_offsets = 2 * jnp.arange(half, dtype=jnp.int32) + 2 - core
    offsets = jnp.concatenate([fetch_offsets, partner_offsets, jnp.zeros((1,), jnp.int32)])
    key_index = (
        (seq_index - offsets)[:, None] * tok_rows + jnp.arange(tok_rows, dtype=jnp.int32)[None, :]
    )
    key_index = jnp.where((offsets <= back)[:, None], key_index, -1)
    key_index = jnp.concatenate(
        [key_index, jnp.full((1, tok_rows), -1, jnp.int32)], axis=0
    ).reshape(half + 1, 1, 2 * tok_rows)
    query_prompt, _ = prompt_ids(own_index, lengths)
    key_prompt, _ = prompt_ids(key_index, lengths)
    mixed = attention(
        queries,
        fetched,
        partner,
        kv_own,
        own_index,
        query_prompt,
        key_index,
        key_prompt,
    )
    attended = mixed.transpose(1, 0, 2).reshape(tok_rows, q_cols)
    partial_out = lax.dot_general(
        attended, wo_rows, (((1,), (1,)), ((), ())), preferred_element_type=jnp.float32
    )
    swapped_out = lax.all_to_all(partial_out.astype(jnp.bfloat16), "mp", 1, 0, tiled=True)
    attn_mine = jnp.sum(
        swapped_out.reshape(mp_count, tok_rows, D // mp_count).astype(jnp.float32), axis=0
    )
    residual = (hidden_in.astype(jnp.float32) + attn_mine).astype(jnp.bfloat16)
    residual_f = residual.astype(jnp.float32)

    local_experts = expert_gate.shape[0]
    experts = seq_count * local_experts
    top_count = routes.shape[1]
    capacity = 2 * tok_rows * top_count // experts
    part_cap = capacity // mp_count
    pair_count = tok_rows * top_count
    flat_ids = routes.reshape(-1)
    one_hot = (flat_ids[:, None] == jnp.arange(experts, dtype=jnp.int32)[None, :]).astype(jnp.int32)
    before = (
        jnp.arange(pair_count, dtype=jnp.int32)[:, None]
        > jnp.arange(pair_count, dtype=jnp.int32)[None, :]
    ).astype(jnp.bfloat16)
    earlier_all = jnp.dot(before, one_hot.astype(jnp.bfloat16), preferred_element_type=jnp.float32)
    earlier_count = jnp.sum(earlier_all.astype(jnp.int32) * one_hot, axis=1)
    slot_index = flat_ids * capacity + earlier_count
    slots = jnp.arange(experts * capacity, dtype=jnp.int32)
    pick = (slot_index[None, :] == slots[:, None]).reshape(experts * capacity, tok_rows, top_count)
    select = jnp.sum(pick.astype(jnp.bfloat16), axis=2)
    buffer = jnp.dot(select, residual, preferred_element_type=jnp.float32).astype(jnp.bfloat16)
    arrived = lax.all_to_all(buffer, ("seq", "mp"), 0, 0, tiled=True)
    feat = D // mp_count
    arrived_rows = (
        arrived.reshape(seq_count, mp_count, part_cap, feat)
        .transpose(0, 2, 1, 3)
        .reshape(seq_count * part_cap, D)
        .astype(jnp.float32)
    )
    moe_in = (
        arrived_rows
        * lax.rsqrt(jnp.sum(arrived_rows * arrived_rows, axis=-1, keepdims=True) / D + EPSILON)
    ).astype(jnp.bfloat16)
    w_gate = expert_all[0]
    w_up = expert_all[1]
    w_down = expert_all[2]
    gate_act = lax.dot_general(
        moe_in, w_gate, (((1,), (1,)), ((), ())), preferred_element_type=jnp.float32
    )
    up_act = lax.dot_general(
        moe_in, w_up, (((1,), (1,)), ((), ())), preferred_element_type=jnp.float32
    )
    active = (jnp.maximum(gate_act, 0.0) * up_act).astype(jnp.bfloat16)
    result = jnp.dot(active, w_down, preferred_element_type=jnp.float32).astype(jnp.bfloat16)
    outgoing = (
        result.reshape(seq_count, part_cap, mp_count, feat)
        .transpose(0, 2, 1, 3)
        .reshape(seq_count * mp_count * part_cap, feat)
    )
    returned = lax.all_to_all(outgoing, ("seq", "mp"), 0, 0, tiled=True)

    gate_weights = jax.nn.softmax(gate_logits, axis=-1)
    combine = jnp.sum(
        jnp.where(
            slot_index[:, None] == slots[None, :], gate_weights.reshape(-1)[:, None], 0.0
        ).reshape(tok_rows, top_count, experts * capacity),
        axis=1,
    )
    moe_total = jnp.dot(
        combine,
        returned.astype(jnp.float32),
        precision=lax.Precision.HIGHEST,
        preferred_element_type=jnp.float32,
    )
    return (residual_f + moe_total).astype(jnp.bfloat16)


def solution(mesh):
    return jax.shard_map(
        local,
        mesh=mesh,
        in_specs=(
            P("seq", "mp"),
            P("seq", "mp"),
            P("seq", None),
            P("mp", "seq"),
            P(),
            P("seq", None),
            P("seq", None),
            P("seq", "mp", None),
            P("seq", "mp", None),
            P("seq", "mp", None),
        ),
        out_specs=P("seq", "mp"),
        check_vma=False,
    )
```

```python
import math

import jax
import jax.numpy as jnp
from jax import lax
from jax.sharding import PartitionSpec as P

D = 1536
HQ = 12
KVH = 2
HD = 128
WINDOW = 4096


ROPE_BASE = 1500000.0
EPSILON = 1e-06


def prompt_ids(index, lengths):
    first_end = lengths[0]
    second_end = lengths[0] + lengths[1]
    prompt = (index >= first_end).astype(jnp.int32) + (index >= second_end).astype(jnp.int32)
    begin = jnp.where(index >= second_end, second_end, jnp.where(index >= first_end, first_end, 0))
    return (prompt, index - begin)


def rotary(values, position):
    half_dim = values.shape[-1] // 2
    freqs = jnp.exp(
        jnp.arange(half_dim, dtype=jnp.float32) * (-2.0 * math.log(ROPE_BASE) / values.shape[-1])
    )
    angles = position.astype(jnp.float32)[:, None] * freqs[None, :]
    cosine = jnp.cos(angles)[:, None, :]
    sine = jnp.sin(angles)[:, None, :]
    front = values[..., :half_dim]
    latter = values[..., half_dim:]
    return jnp.concatenate(
        [front * cosine - latter * sine, latter * cosine + front * sine], axis=-1
    )


def gather_seq(piece, count):
    rows = piece.shape[0]
    spread = jnp.broadcast_to(piece[None], (count,) + piece.shape).reshape(
        count * rows, piece.shape[1]
    )
    return lax.all_to_all(spread, "seq", 0, 0, tiled=True)


def local(
    hidden_in, wq, wkv, wo, lengths, routes, gate_logits, expert_gate, expert_up, expert_down
):
    tok_rows = hidden_in.shape[0]
    seq_index = lax.axis_index("seq")
    mp_index = lax.axis_index("mp")
    seq_count = lax.axis_size("seq")
    mp_count = lax.axis_size("mp")
    heads_here = wq.shape[1] // HD
    q_cols = heads_here * HD
    kv_group = mp_index * heads_here // (HQ // KVH)

    expert_all = lax.all_gather(
        jnp.concatenate([expert_gate, expert_up, expert_down], axis=0), "mp", axis=1, tiled=True
    )

    core = mp_index % 2
    kv_col = jnp.where(core == 0, kv_group * HD, KVH * HD + kv_group * HD)
    kv_cols = lax.dynamic_slice_in_dim(wkv, kv_col, HD, 1)
    w_qkv = gather_seq(jnp.concatenate([wq, kv_cols], axis=1), seq_count)

    whole = lax.all_gather(hidden_in, "mp", axis=1, tiled=True)
    whole_f = whole.astype(jnp.float32)
    normed = (
        whole_f * lax.rsqrt(jnp.sum(whole_f * whole_f, axis=-1, keepdims=True) / D + EPSILON)
    ).astype(jnp.bfloat16)
    lin = jnp.dot(normed, w_qkv, preferred_element_type=jnp.float32)
    wo_piece, lin = lax.optimization_barrier((wo.T, lin))
    wo_rows = gather_seq(wo_piece, seq_count)
    own_index = seq_index * tok_rows + jnp.arange(tok_rows, dtype=jnp.int32)
    _, own_pos = prompt_ids(own_index, lengths)
    queries = (
        rotary(lin[:, :q_cols].reshape(tok_rows, heads_here, HD), own_pos)
        .astype(jnp.bfloat16)
        .transpose(1, 0, 2)
    )
    kv_lin = lin[:, q_cols:]
    kv_mine = jnp.where(
        core == 0, rotary(kv_lin.reshape(tok_rows, 1, HD), own_pos)[:, 0, :], kv_lin
    ).astype(jnp.bfloat16)
    kv_other = lax.ppermute(kv_mine, "mp", [(m, m ^ 1) for m in range(mp_count)])
    key_own = jnp.where(core == 0, kv_mine, kv_other)
    value_own = jnp.where(core == 0, kv_other, kv_mine)
    kv_own = jnp.concatenate([key_own, value_own], axis=1)

    back = min((WINDOW - 1 + tok_rows - 1) // tok_rows, seq_count - 1)
    half = (back + 1) // 2
    fetched = []
    for j in range(half):
        pairs = []
        for s in range(seq_count):
            for m in range(mp_count):
                k = 2 * j + 1 + m % 2
                if s + k < seq_count:
                    pairs.append((s * mp_count + m, (s + k) * mp_count + m))
        fetched.append(lax.ppermute(kv_own, ("seq", "mp"), pairs))
    fetched = jnp.stack(fetched)
    partner = lax.ppermute(
        fetched, "mp", [(m, m ^ 1) for m in range(mp_count)]
    )
    odd = jnp.where(core == 0, fetched, partner)
    even = jnp.where(core == 0, partner, fetched)
    offsets = jnp.concatenate(
        [
            2 * jnp.arange(half, dtype=jnp.int32) + 1,
            2 * jnp.arange(half, dtype=jnp.int32) + 2,
            jnp.zeros((1,), jnp.int32),
        ]
    )
    kv_win = jnp.concatenate(
        [odd.reshape(-1, 2 * HD), even.reshape(-1, 2 * HD), kv_own], axis=0
    )
    key_rows = kv_win[:, :HD]
    value_rows = kv_win[:, HD:].astype(jnp.float32)
    key_index = (
        (seq_index - offsets)[:, None] * tok_rows + jnp.arange(tok_rows, dtype=jnp.int32)[None, :]
    ).reshape(-1)
    key_index = jnp.where(
        jnp.repeat(offsets, tok_rows) <= back, key_index, -1
    )

    scores = jnp.einsum(
        "hqd,kd->hqk", queries, key_rows, preferred_element_type=jnp.float32
    ) * HD ** (-0.5)
    query_prompt, _ = prompt_ids(own_index, lengths)
    key_prompt, _ = prompt_ids(key_index, lengths)
    spacing = own_index[:, None] - key_index[None, :]
    allowed = (
        (query_prompt[:, None] == key_prompt[None, :])
        & (spacing >= 0)
        & (spacing < WINDOW)
        & (key_index[None, :] >= 0)
    )[None]
    masked = jnp.where(allowed, scores, -1e30)
    peak = jnp.max(masked, axis=-1)
    probs = jnp.exp(masked - peak[..., None])
    total = jnp.sum(probs, axis=-1)
    accum = jnp.einsum("hqk,kd->hqd", probs, value_rows)
    attended = (
        (accum / total[..., None])
        .transpose(1, 0, 2)
        .reshape(tok_rows, q_cols)
        .astype(jnp.bfloat16)
    )
    partial_out = lax.dot_general(
        attended, wo_rows, (((1,), (1,)), ((), ())), preferred_element_type=jnp.float32
    )
    swapped_out = lax.all_to_all(partial_out.astype(jnp.bfloat16), "mp", 1, 0, tiled=True)
    attn_mine = jnp.sum(
        swapped_out.reshape(mp_count, tok_rows, D // mp_count).astype(jnp.float32), axis=0
    )
    residual = (hidden_in.astype(jnp.float32) + attn_mine).astype(jnp.bfloat16)
    residual_f = residual.astype(jnp.float32)

    local_experts = expert_gate.shape[0]
    experts = seq_count * local_experts
    top_count = routes.shape[1]
    capacity = 2 * tok_rows * top_count // experts
    part_cap = capacity // mp_count
    pair_count = tok_rows * top_count
    flat_ids = routes.reshape(-1)
    one_hot = (flat_ids[:, None] == jnp.arange(experts, dtype=jnp.int32)[None, :]).astype(jnp.int32)
    before = (
        jnp.arange(pair_count, dtype=jnp.int32)[:, None]
        > jnp.arange(pair_count, dtype=jnp.int32)[None, :]
    ).astype(jnp.bfloat16)
    earlier_all = jnp.dot(before, one_hot.astype(jnp.bfloat16), preferred_element_type=jnp.float32)
    earlier_count = jnp.sum(earlier_all.astype(jnp.int32) * one_hot, axis=1)
    slot_index = flat_ids * capacity + earlier_count
    slots = jnp.arange(experts * capacity, dtype=jnp.int32)
    pick = (slot_index[None, :] == slots[:, None]).reshape(experts * capacity, tok_rows, top_count)
    select = jnp.sum(pick.astype(jnp.bfloat16), axis=2)
    buffer = jnp.dot(select, residual, preferred_element_type=jnp.float32).astype(jnp.bfloat16)
    arrived = lax.all_to_all(buffer, ("seq", "mp"), 0, 0, tiled=True)
    feat = D // mp_count
    arrived_rows = (
        arrived.reshape(seq_count, mp_count, part_cap, feat)
        .transpose(0, 2, 1, 3)
        .reshape(seq_count * part_cap, D)
        .astype(jnp.float32)
    )
    moe_in = (
        arrived_rows
        * lax.rsqrt(jnp.sum(arrived_rows * arrived_rows, axis=-1, keepdims=True) / D + EPSILON)
    ).astype(jnp.bfloat16)
    w_gate = expert_all[0]
    w_up = expert_all[1]
    w_down = expert_all[2]
    gate_act = lax.dot_general(
        moe_in, w_gate, (((1,), (1,)), ((), ())), preferred_element_type=jnp.float32
    )
    up_act = lax.dot_general(
        moe_in, w_up, (((1,), (1,)), ((), ())), preferred_element_type=jnp.float32
    )
    active = (jnp.maximum(gate_act, 0.0) * up_act).astype(jnp.bfloat16)
    result = jnp.dot(active, w_down, preferred_element_type=jnp.float32).astype(jnp.bfloat16)
    outgoing = (
        result.reshape(seq_count, part_cap, mp_count, feat)
        .transpose(0, 2, 1, 3)
        .reshape(seq_count * mp_count * part_cap, feat)
    )
    returned = lax.all_to_all(outgoing, ("seq", "mp"), 0, 0, tiled=True)

    gate_weights = jax.nn.softmax(gate_logits, axis=-1)
    combine = jnp.sum(
        jnp.where(
            slot_index[:, None] == slots[None, :], gate_weights.reshape(-1)[:, None], 0.0
        ).reshape(tok_rows, top_count, experts * capacity),
        axis=1,
    )
    moe_total = jnp.dot(
        combine,
        returned.astype(jnp.float32),
        precision=lax.Precision.HIGHEST,
        preferred_element_type=jnp.float32,
    )
    return (residual_f + moe_total).astype(jnp.bfloat16)


def solution(mesh):
    return jax.shard_map(
        local,
        mesh=mesh,
        in_specs=(
            P("seq", "mp"),
            P("seq", "mp"),
            P("seq", None),
            P("mp", "seq"),
            P(),
            P("seq", None),
            P("seq", None),
            P("seq", "mp", None),
            P("seq", "mp", None),
            P("seq", "mp", None),
        ),
        out_specs=P("seq", "mp"),
        check_vma=False,
    )
```

```python
import math

import jax
import jax.numpy as jnp
from jax import lax
from jax.sharding import PartitionSpec as P

D = 1536
HQ = 12
KVH = 2
HD = 128
WINDOW = 4096


ROPE_BASE = 1500000.0
EPSILON = 1e-06


def prompt_ids(index, lengths):
    first_end = lengths[0]
    second_end = lengths[0] + lengths[1]
    prompt = (index >= first_end).astype(jnp.int32) + (index >= second_end).astype(jnp.int32)
    begin = jnp.where(index >= second_end, second_end, jnp.where(index >= first_end, first_end, 0))
    return (prompt, index - begin)


def rotary(values, position):
    half_dim = values.shape[-1] // 2
    freqs = jnp.exp(
        jnp.arange(half_dim, dtype=jnp.float32) * (-2.0 * math.log(ROPE_BASE) / values.shape[-1])
    )
    angles = position.astype(jnp.float32)[:, None] * freqs[None, :]
    cosine = jnp.cos(angles)[:, None, :]
    sine = jnp.sin(angles)[:, None, :]
    front = values[..., :half_dim]
    latter = values[..., half_dim:]
    return jnp.concatenate(
        [front * cosine - latter * sine, latter * cosine + front * sine], axis=-1
    )


def gather_seq(piece, count):
    rows = piece.shape[0]
    spread = jnp.broadcast_to(piece[None], (count,) + piece.shape).reshape(
        count * rows, piece.shape[1]
    )
    return lax.all_to_all(spread, "seq", 0, 0, tiled=True)


def local(
    hidden_in, wq, wkv, wo, lengths, routes, gate_logits, expert_gate, expert_up, expert_down
):
    tok_rows = hidden_in.shape[0]
    seq_index = lax.axis_index("seq")
    mp_index = lax.axis_index("mp")
    seq_count = lax.axis_size("seq")
    mp_count = lax.axis_size("mp")
    heads_here = wq.shape[1] // HD
    q_cols = heads_here * HD
    kv_group = mp_index * heads_here // (HQ // KVH)


    core = mp_index % 2
    kv_col = jnp.where(core == 0, kv_group * HD, KVH * HD + kv_group * HD)
    kv_cols = lax.dynamic_slice_in_dim(wkv, kv_col, HD, 1)
    w_qkv = gather_seq(jnp.concatenate([wq, kv_cols], axis=1), seq_count)

    whole = lax.all_gather(hidden_in, "mp", axis=1, tiled=True)
    whole_f = whole.astype(jnp.float32)
    normed = (
        whole_f * lax.rsqrt(jnp.sum(whole_f * whole_f, axis=-1, keepdims=True) / D + EPSILON)
    ).astype(jnp.bfloat16)
    lin = jnp.dot(normed, w_qkv, preferred_element_type=jnp.float32)
    expert_own = jnp.concatenate([expert_gate, expert_up, expert_down], axis=0)
    wo_piece, expert_own, lin = lax.optimization_barrier((wo.T, expert_own, lin))
    expert_quarters = lax.all_to_all(
        jnp.broadcast_to(expert_own[None], (mp_count,) + expert_own.shape),
        "mp", 0, 0, tiled=True,
    )
    wo_rows = gather_seq(wo_piece, seq_count)
    own_index = seq_index * tok_rows + jnp.arange(tok_rows, dtype=jnp.int32)
    _, own_pos = prompt_ids(own_index, lengths)
    queries = (
        rotary(lin[:, :q_cols].reshape(tok_rows, heads_here, HD), own_pos)
        .astype(jnp.bfloat16)
        .transpose(1, 0, 2)
    )
    kv_lin = lin[:, q_cols:]
    kv_mine = jnp.where(
        core == 0, rotary(kv_lin.reshape(tok_rows, 1, HD), own_pos)[:, 0, :], kv_lin
    ).astype(jnp.bfloat16)
    kv_other = lax.ppermute(kv_mine, "mp", [(m, m ^ 1) for m in range(mp_count)])
    key_own = jnp.where(core == 0, kv_mine, kv_other)
    value_own = jnp.where(core == 0, kv_other, kv_mine)
    kv_own = jnp.concatenate([key_own, value_own], axis=1)

    back = min((WINDOW - 1 + tok_rows - 1) // tok_rows, seq_count - 1)
    half = (back + 1) // 2
    fetched = []
    for j in range(half):
        pairs = []
        for s in range(seq_count):
            for m in range(mp_count):
                k = 2 * j + 1 + m % 2
                if s + k < seq_count:
                    pairs.append((s * mp_count + m, (s + k) * mp_count + m))
        fetched.append(lax.ppermute(kv_own, ("seq", "mp"), pairs))
    fetched = jnp.stack(fetched)
    partner = lax.ppermute(
        fetched, "mp", [(m, m ^ 1) for m in range(mp_count)]
    )
    odd = jnp.where(core == 0, fetched, partner)
    even = jnp.where(core == 0, partner, fetched)
    offsets = jnp.concatenate(
        [
            2 * jnp.arange(half, dtype=jnp.int32) + 1,
            2 * jnp.arange(half, dtype=jnp.int32) + 2,
            jnp.zeros((1,), jnp.int32),
        ]
    )
    kv_win = jnp.concatenate(
        [odd.reshape(-1, 2 * HD), even.reshape(-1, 2 * HD), kv_own], axis=0
    )
    expert_quarters, kv_win = lax.optimization_barrier((expert_quarters, kv_win))
    key_rows = kv_win[:, :HD]
    value_rows = kv_win[:, HD:].astype(jnp.float32)
    key_index = (
        (seq_index - offsets)[:, None] * tok_rows + jnp.arange(tok_rows, dtype=jnp.int32)[None, :]
    ).reshape(-1)
    key_index = jnp.where(
        jnp.repeat(offsets, tok_rows) <= back, key_index, -1
    )

    scores = jnp.einsum(
        "hqd,kd->hqk", queries, key_rows, preferred_element_type=jnp.float32
    ) * HD ** (-0.5)
    query_prompt, _ = prompt_ids(own_index, lengths)
    key_prompt, _ = prompt_ids(key_index, lengths)
    spacing = own_index[:, None] - key_index[None, :]
    allowed = (
        (query_prompt[:, None] == key_prompt[None, :])
        & (spacing >= 0)
        & (spacing < WINDOW)
        & (key_index[None, :] >= 0)
    )[None]
    masked = jnp.where(allowed, scores, -1e30)
    peak = jnp.max(masked, axis=-1)
    probs = jnp.exp(masked - peak[..., None])
    total = jnp.sum(probs, axis=-1)
    accum = jnp.einsum("hqk,kd->hqd", probs, value_rows)
    attended = (
        (accum / total[..., None])
        .transpose(1, 0, 2)
        .reshape(tok_rows, q_cols)
        .astype(jnp.bfloat16)
    )
    partial_out = lax.dot_general(
        attended, wo_rows, (((1,), (1,)), ((), ())), preferred_element_type=jnp.float32
    )
    swapped_out = lax.all_to_all(partial_out.astype(jnp.bfloat16), "mp", 1, 0, tiled=True)
    attn_mine = jnp.sum(
        swapped_out.reshape(mp_count, tok_rows, D // mp_count).astype(jnp.float32), axis=0
    )
    residual = (hidden_in.astype(jnp.float32) + attn_mine).astype(jnp.bfloat16)
    residual_f = residual.astype(jnp.float32)

    local_experts = expert_gate.shape[0]
    experts = seq_count * local_experts
    top_count = routes.shape[1]
    capacity = 2 * tok_rows * top_count // experts
    part_cap = capacity // mp_count
    pair_count = tok_rows * top_count
    flat_ids = routes.reshape(-1)
    one_hot = (flat_ids[:, None] == jnp.arange(experts, dtype=jnp.int32)[None, :]).astype(jnp.int32)
    before = (
        jnp.arange(pair_count, dtype=jnp.int32)[:, None]
        > jnp.arange(pair_count, dtype=jnp.int32)[None, :]
    ).astype(jnp.bfloat16)
    earlier_all = jnp.dot(before, one_hot.astype(jnp.bfloat16), preferred_element_type=jnp.float32)
    earlier_count = jnp.sum(earlier_all.astype(jnp.int32) * one_hot, axis=1)
    slot_index = flat_ids * capacity + earlier_count
    slots = jnp.arange(experts * capacity, dtype=jnp.int32)
    pick = (slot_index[None, :] == slots[:, None]).reshape(experts * capacity, tok_rows, top_count)
    select = jnp.sum(pick.astype(jnp.bfloat16), axis=2)
    buffer = jnp.dot(select, residual, preferred_element_type=jnp.float32).astype(jnp.bfloat16)
    arrived = lax.all_to_all(buffer, ("seq", "mp"), 0, 0, tiled=True)
    feat = D // mp_count
    arrived_rows = (
        arrived.reshape(seq_count, mp_count, part_cap, feat)
        .transpose(0, 2, 1, 3)
        .reshape(seq_count * part_cap, D)
        .astype(jnp.float32)
    )
    moe_in = (
        arrived_rows
        * lax.rsqrt(jnp.sum(arrived_rows * arrived_rows, axis=-1, keepdims=True) / D + EPSILON)
    ).astype(jnp.bfloat16)
    result_f = None
    for quarter in range(mp_count):
        piece = expert_quarters[quarter]
        gate_act = lax.dot_general(
            moe_in, piece[0], (((1,), (1,)), ((), ())), preferred_element_type=jnp.float32
        )
        up_act = lax.dot_general(
            moe_in, piece[1], (((1,), (1,)), ((), ())), preferred_element_type=jnp.float32
        )
        active = (jnp.maximum(gate_act, 0.0) * up_act).astype(jnp.bfloat16)
        part = jnp.dot(active, piece[2], preferred_element_type=jnp.float32)
        result_f = part if result_f is None else result_f + part
    result = result_f.astype(jnp.bfloat16)
    outgoing = (
        result.reshape(seq_count, part_cap, mp_count, feat)
        .transpose(0, 2, 1, 3)
        .reshape(seq_count * mp_count * part_cap, feat)
    )
    returned = lax.all_to_all(outgoing, ("seq", "mp"), 0, 0, tiled=True)

    gate_weights = jax.nn.softmax(gate_logits, axis=-1)
    combine = jnp.sum(
        jnp.where(
            slot_index[:, None] == slots[None, :], gate_weights.reshape(-1)[:, None], 0.0
        ).reshape(tok_rows, top_count, experts * capacity),
        axis=1,
    )
    moe_total = jnp.dot(
        combine,
        returned.astype(jnp.float32),
        precision=lax.Precision.HIGHEST,
        preferred_element_type=jnp.float32,
    )
    return (residual_f + moe_total).astype(jnp.bfloat16)


def solution(mesh):
    return jax.shard_map(
        local,
        mesh=mesh,
        in_specs=(
            P("seq", "mp"),
            P("seq", "mp"),
            P("seq", None),
            P("mp", "seq"),
            P(),
            P("seq", None),
            P("seq", None),
            P("seq", "mp", None),
            P("seq", "mp", None),
            P("seq", "mp", None),
        ),
        out_specs=P("seq", "mp"),
        check_vma=False,
    )
```

```python
import math

import jax
import jax.numpy as jnp
from jax import lax
from jax.sharding import PartitionSpec as P

D = 1536
HQ = 12
KVH = 2
HD = 128
WINDOW = 4096


ROPE_BASE = 1500000.0
EPSILON = 1e-06


def prompt_ids(index, lengths):
    first_end = lengths[0]
    second_end = lengths[0] + lengths[1]
    prompt = (index >= first_end).astype(jnp.int32) + (index >= second_end).astype(jnp.int32)
    begin = jnp.where(index >= second_end, second_end, jnp.where(index >= first_end, first_end, 0))
    return (prompt, index - begin)


def rotary(values, position):
    half_dim = values.shape[-1] // 2
    freqs = jnp.exp(
        jnp.arange(half_dim, dtype=jnp.float32) * (-2.0 * math.log(ROPE_BASE) / values.shape[-1])
    )
    angles = position.astype(jnp.float32)[:, None] * freqs[None, :]
    cosine = jnp.cos(angles)[:, None, :]
    sine = jnp.sin(angles)[:, None, :]
    front = values[..., :half_dim]
    latter = values[..., half_dim:]
    return jnp.concatenate(
        [front * cosine - latter * sine, latter * cosine + front * sine], axis=-1
    )


def gather_seq(piece, count):
    rows = piece.shape[0]
    spread = jnp.broadcast_to(piece[None], (count,) + piece.shape).reshape(
        count * rows, piece.shape[1]
    )
    return lax.all_to_all(spread, "seq", 0, 0, tiled=True)


def local(
    hidden_in, wq, wkv, wo, lengths, routes, gate_logits, expert_gate, expert_up, expert_down
):
    tok_rows = hidden_in.shape[0]
    seq_index = lax.axis_index("seq")
    mp_index = lax.axis_index("mp")
    seq_count = lax.axis_size("seq")
    mp_count = lax.axis_size("mp")
    heads_here = wq.shape[1] // HD
    q_cols = heads_here * HD
    kv_group = mp_index * heads_here // (HQ // KVH)

    expert_all = lax.all_gather(
        jnp.concatenate([expert_gate, expert_up, expert_down], axis=0), "mp", axis=1, tiled=True
    )

    core = mp_index % 2
    kv_col = jnp.where(core == 0, kv_group * HD, KVH * HD + kv_group * HD)
    kv_cols = lax.dynamic_slice_in_dim(wkv, kv_col, HD, 1)
    w_qkv = gather_seq(jnp.concatenate([wq, kv_cols], axis=1), seq_count)

    whole = lax.all_gather(hidden_in, "mp", axis=1, tiled=True)
    whole_f = whole.astype(jnp.float32)
    normed = (
        whole_f * lax.rsqrt(jnp.sum(whole_f * whole_f, axis=-1, keepdims=True) / D + EPSILON)
    ).astype(jnp.bfloat16)
    lin = jnp.dot(normed, w_qkv, preferred_element_type=jnp.float32)
    wo_piece, lin = lax.optimization_barrier((wo.T, lin))
    wo_rows = gather_seq(wo_piece, seq_count)
    own_index = seq_index * tok_rows + jnp.arange(tok_rows, dtype=jnp.int32)
    _, own_pos = prompt_ids(own_index, lengths)
    queries = (
        rotary(lin[:, :q_cols].reshape(tok_rows, heads_here, HD), own_pos)
        .astype(jnp.bfloat16)
        .transpose(1, 0, 2)
    )
    kv_lin = lin[:, q_cols:]
    kv_mine = jnp.where(
        core == 0, rotary(kv_lin.reshape(tok_rows, 1, HD), own_pos)[:, 0, :], kv_lin
    ).astype(jnp.bfloat16)
    kv_other = lax.ppermute(kv_mine, "mp", [(m, m ^ 1) for m in range(mp_count)])
    key_own = jnp.where(core == 0, kv_mine, kv_other)
    value_own = jnp.where(core == 0, kv_other, kv_mine)
    kv_own = jnp.concatenate([key_own, value_own], axis=1)

    back = min((WINDOW - 1 + tok_rows - 1) // tok_rows, seq_count - 1)
    half = (back + 1) // 2
    fetched = []
    for j in range(half):
        pairs = []
        for s in range(seq_count):
            for m in range(mp_count):
                k = 2 * j + 1 + m % 2
                if s + k < seq_count:
                    pairs.append((s * mp_count + m, (s + k) * mp_count + m))
        fetched.append(lax.ppermute(kv_own, ("seq", "mp"), pairs))
    fetched = jnp.stack(fetched)
    partner = lax.ppermute(
        fetched, "mp", [(m, m ^ 1) for m in range(mp_count)]
    )
    odd = jnp.where(core == 0, fetched, partner)
    even = jnp.where(core == 0, partner, fetched)
    offsets = jnp.concatenate(
        [
            2 * jnp.arange(half, dtype=jnp.int32) + 1,
            2 * jnp.arange(half, dtype=jnp.int32) + 2,
            jnp.zeros((1,), jnp.int32),
        ]
    )
    kv_win = jnp.concatenate(
        [odd.reshape(-1, 2 * HD), even.reshape(-1, 2 * HD), kv_own], axis=0
    )
    key_rows = kv_win[:, :HD]
    value_rows = kv_win[:, HD:].astype(jnp.float32)
    key_index = (
        (seq_index - offsets)[:, None] * tok_rows + jnp.arange(tok_rows, dtype=jnp.int32)[None, :]
    ).reshape(-1)
    key_index = jnp.where(
        jnp.repeat(offsets, tok_rows) <= back, key_index, -1
    )

    scores = jnp.einsum(
        "hqd,kd->hqk", queries, key_rows, preferred_element_type=jnp.float32
    ) * HD ** (-0.5)
    query_prompt, _ = prompt_ids(own_index, lengths)
    key_prompt, _ = prompt_ids(key_index, lengths)
    spacing = own_index[:, None] - key_index[None, :]
    allowed = (
        (query_prompt[:, None] == key_prompt[None, :])
        & (spacing >= 0)
        & (spacing < WINDOW)
        & (key_index[None, :] >= 0)
    )[None]
    masked = jnp.where(allowed, scores, -1e30)
    peak = jnp.max(masked, axis=-1)
    probs = jnp.exp(masked - peak[..., None])
    total = jnp.sum(probs, axis=-1)
    accum = jnp.einsum("hqk,kd->hqd", probs, value_rows)
    attended = (
        (accum / total[..., None])
        .transpose(1, 0, 2)
        .reshape(tok_rows, q_cols)
        .astype(jnp.bfloat16)
    )
    partial_out = lax.dot_general(
        attended, wo_rows, (((1,), (1,)), ((), ())), preferred_element_type=jnp.float32
    )
    swapped_out = lax.all_to_all(partial_out.astype(jnp.bfloat16), "mp", 1, 0, tiled=True)
    attn_mine = jnp.sum(
        swapped_out.reshape(mp_count, tok_rows, D // mp_count).astype(jnp.float32), axis=0
    )
    residual = (hidden_in.astype(jnp.float32) + attn_mine).astype(jnp.bfloat16)
    residual_f = residual.astype(jnp.float32)

    local_experts = expert_gate.shape[0]
    experts = seq_count * local_experts
    top_count = routes.shape[1]
    capacity = 2 * tok_rows * top_count // experts
    part_cap = capacity // mp_count
    pair_count = tok_rows * top_count
    flat_ids = routes.reshape(-1)
    one_hot = (flat_ids[:, None] == jnp.arange(experts, dtype=jnp.int32)[None, :]).astype(jnp.int32)
    before = (
        jnp.arange(pair_count, dtype=jnp.int32)[:, None]
        > jnp.arange(pair_count, dtype=jnp.int32)[None, :]
    ).astype(jnp.bfloat16)
    earlier_all = jnp.dot(before, one_hot.astype(jnp.bfloat16), preferred_element_type=jnp.float32)
    earlier_count = jnp.sum(earlier_all.astype(jnp.int32) * one_hot, axis=1)
    slot_index = flat_ids * capacity + earlier_count
    slots = jnp.arange(experts * capacity, dtype=jnp.int32)
    pick = (slot_index[None, :] == slots[:, None]).reshape(experts * capacity, tok_rows, top_count)
    select = jnp.sum(pick.astype(jnp.bfloat16), axis=2)
    buffer = jnp.dot(select, residual, preferred_element_type=jnp.float32).astype(jnp.bfloat16)
    arrived = lax.all_to_all(buffer, ("seq", "mp"), 0, 0, tiled=True)
    feat = D // mp_count
    arrived_rows = (
        arrived.reshape(seq_count, mp_count, part_cap, feat)
        .transpose(0, 2, 1, 3)
        .reshape(seq_count * part_cap, D)
        .astype(jnp.float32)
    )
    moe_in = (
        arrived_rows
        * lax.rsqrt(jnp.sum(arrived_rows * arrived_rows, axis=-1, keepdims=True) / D + EPSILON)
    ).astype(jnp.bfloat16)
    w_gate = expert_all[0]
    w_up = expert_all[1]
    w_down = expert_all[2]
    gate_act = lax.dot_general(
        moe_in, w_gate, (((1,), (1,)), ((), ())), preferred_element_type=jnp.float32
    )
    up_act = lax.dot_general(
        moe_in, w_up, (((1,), (1,)), ((), ())), preferred_element_type=jnp.float32
    )
    active = (jnp.maximum(gate_act, 0.0) * up_act).astype(jnp.bfloat16)
    result = jnp.dot(active, w_down, preferred_element_type=jnp.float32).astype(jnp.bfloat16)
    outgoing = (
        result.reshape(seq_count, part_cap, mp_count, feat)
        .transpose(0, 2, 1, 3)
        .reshape(seq_count * mp_count * part_cap, feat)
    )
    returned = lax.all_to_all(outgoing, ("seq", "mp"), 0, 0, tiled=True)

    gate_weights = jax.nn.softmax(gate_logits, axis=-1)
    combine = jnp.sum(
        jnp.where(
            slot_index[:, None] == slots[None, :], gate_weights.reshape(-1)[:, None], 0.0
        ).reshape(tok_rows, top_count, experts * capacity),
        axis=1,
    )
    combine_hi = combine.astype(jnp.bfloat16)
    combine_lo = (combine - combine_hi.astype(jnp.float32)).astype(jnp.bfloat16)
    moe_total = jnp.dot(combine_hi, returned, preferred_element_type=jnp.float32) + jnp.dot(
        combine_lo, returned, preferred_element_type=jnp.float32
    )
    return (residual_f + moe_total).astype(jnp.bfloat16)


def solution(mesh):
    return jax.shard_map(
        local,
        mesh=mesh,
        in_specs=(
            P("seq", "mp"),
            P("seq", "mp"),
            P("seq", None),
            P("mp", "seq"),
            P(),
            P("seq", None),
            P("seq", None),
            P("seq", "mp", None),
            P("seq", "mp", None),
            P("seq", "mp", None),
        ),
        out_specs=P("seq", "mp"),
        check_vma=False,
    )
```

```python
import math

import jax
import jax.numpy as jnp
from jax import lax
from jax.sharding import PartitionSpec as P

D = 1536
HQ = 12
KVH = 2
HD = 128
WINDOW = 4096


ROPE_BASE = 1500000.0
EPSILON = 1e-06


def prompt_ids(index, lengths):
    first_end = lengths[0]
    second_end = lengths[0] + lengths[1]
    prompt = (index >= first_end).astype(jnp.int32) + (index >= second_end).astype(jnp.int32)
    begin = jnp.where(index >= second_end, second_end, jnp.where(index >= first_end, first_end, 0))
    return (prompt, index - begin)


def rotary(values, position):
    half_dim = values.shape[-1] // 2
    freqs = jnp.exp(
        jnp.arange(half_dim, dtype=jnp.float32) * (-2.0 * math.log(ROPE_BASE) / values.shape[-1])
    )
    angles = position.astype(jnp.float32)[:, None] * freqs[None, :]
    cosine = jnp.cos(angles)[:, None, :]
    sine = jnp.sin(angles)[:, None, :]
    front = values[..., :half_dim]
    latter = values[..., half_dim:]
    return jnp.concatenate(
        [front * cosine - latter * sine, latter * cosine + front * sine], axis=-1
    )


def gather_seq(piece, count):
    rows = piece.shape[0]
    spread = jnp.broadcast_to(piece[None], (count,) + piece.shape).reshape(
        count * rows, piece.shape[1]
    )
    return lax.all_to_all(spread, "seq", 0, 0, tiled=True)


def local(
    hidden_in, wq, wkv, wo, lengths, routes, gate_logits, expert_gate, expert_up, expert_down
):
    tok_rows = hidden_in.shape[0]
    seq_index = lax.axis_index("seq")
    mp_index = lax.axis_index("mp")
    seq_count = lax.axis_size("seq")
    mp_count = lax.axis_size("mp")
    heads_here = wq.shape[1] // HD
    q_cols = heads_here * HD
    kv_group = mp_index * heads_here // (HQ // KVH)


    core = mp_index % 2
    kv_col = jnp.where(core == 0, kv_group * HD, KVH * HD + kv_group * HD)
    kv_cols = lax.dynamic_slice_in_dim(wkv, kv_col, HD, 1)
    w_qkv = gather_seq(jnp.concatenate([wq, kv_cols], axis=1), seq_count)

    whole = lax.all_gather(hidden_in, "mp", axis=1, tiled=True)
    expert_own, whole = lax.optimization_barrier(
        (jnp.concatenate([expert_gate, expert_up, expert_down], axis=0), whole)
    )
    expert_all = lax.all_gather(expert_own, "mp", axis=1, tiled=True)
    whole_f = whole.astype(jnp.float32)
    normed = (
        whole_f * lax.rsqrt(jnp.sum(whole_f * whole_f, axis=-1, keepdims=True) / D + EPSILON)
    ).astype(jnp.bfloat16)
    lin = jnp.dot(normed, w_qkv, preferred_element_type=jnp.float32)
    wo_piece, lin = lax.optimization_barrier((wo.T, lin))
    wo_rows = gather_seq(wo_piece, seq_count)
    own_index = seq_index * tok_rows + jnp.arange(tok_rows, dtype=jnp.int32)
    _, own_pos = prompt_ids(own_index, lengths)
    queries = (
        rotary(lin[:, :q_cols].reshape(tok_rows, heads_here, HD), own_pos)
        .astype(jnp.bfloat16)
        .transpose(1, 0, 2)
    )
    kv_lin = lin[:, q_cols:]
    kv_mine = jnp.where(
        core == 0, rotary(kv_lin.reshape(tok_rows, 1, HD), own_pos)[:, 0, :], kv_lin
    ).astype(jnp.bfloat16)
    kv_other = lax.ppermute(kv_mine, "mp", [(m, m ^ 1) for m in range(mp_count)])
    key_own = jnp.where(core == 0, kv_mine, kv_other)
    value_own = jnp.where(core == 0, kv_other, kv_mine)
    kv_own = jnp.concatenate([key_own, value_own], axis=1)

    back = min((WINDOW - 1 + tok_rows - 1) // tok_rows, seq_count - 1)
    half = (back + 1) // 2
    fetched = []
    for j in range(half):
        pairs = []
        for s in range(seq_count):
            for m in range(mp_count):
                k = 2 * j + 1 + m % 2
                if s + k < seq_count:
                    pairs.append((s * mp_count + m, (s + k) * mp_count + m))
        fetched.append(lax.ppermute(kv_own, ("seq", "mp"), pairs))
    fetched = jnp.stack(fetched)
    partner = lax.ppermute(
        fetched, "mp", [(m, m ^ 1) for m in range(mp_count)]
    )
    odd = jnp.where(core == 0, fetched, partner)
    even = jnp.where(core == 0, partner, fetched)
    offsets = jnp.concatenate(
        [
            2 * jnp.arange(half, dtype=jnp.int32) + 1,
            2 * jnp.arange(half, dtype=jnp.int32) + 2,
            jnp.zeros((1,), jnp.int32),
        ]
    )
    kv_win = jnp.concatenate(
        [odd.reshape(-1, 2 * HD), even.reshape(-1, 2 * HD), kv_own], axis=0
    )
    key_rows = kv_win[:, :HD]
    value_rows = kv_win[:, HD:].astype(jnp.float32)
    key_index = (
        (seq_index - offsets)[:, None] * tok_rows + jnp.arange(tok_rows, dtype=jnp.int32)[None, :]
    ).reshape(-1)
    key_index = jnp.where(
        jnp.repeat(offsets, tok_rows) <= back, key_index, -1
    )

    scores = jnp.einsum(
        "hqd,kd->hqk", queries, key_rows, preferred_element_type=jnp.float32
    ) * HD ** (-0.5)
    query_prompt, _ = prompt_ids(own_index, lengths)
    key_prompt, _ = prompt_ids(key_index, lengths)
    spacing = own_index[:, None] - key_index[None, :]
    allowed = (
        (query_prompt[:, None] == key_prompt[None, :])
        & (spacing >= 0)
        & (spacing < WINDOW)
        & (key_index[None, :] >= 0)
    )[None]
    masked = jnp.where(allowed, scores, -1e30)
    peak = jnp.max(masked, axis=-1)
    probs = jnp.where(allowed, jnp.exp(masked - peak[..., None]), 0.0)
    total = jnp.sum(probs, axis=-1)
    accum = jnp.einsum("hqk,kd->hqd", probs, value_rows)
    attended = (
        (accum / total[..., None])
        .transpose(1, 0, 2)
        .reshape(tok_rows, q_cols)
        .astype(jnp.bfloat16)
    )
    partial_out = lax.dot_general(
        attended, wo_rows, (((1,), (1,)), ((), ())), preferred_element_type=jnp.float32
    )
    swapped_out = lax.all_to_all(partial_out.astype(jnp.bfloat16), "mp", 1, 0, tiled=True)
    attn_mine = jnp.sum(
        swapped_out.reshape(mp_count, tok_rows, D // mp_count).astype(jnp.float32), axis=0
    )
    residual = (hidden_in.astype(jnp.float32) + attn_mine).astype(jnp.bfloat16)
    residual_f = residual.astype(jnp.float32)

    local_experts = expert_gate.shape[0]
    experts = seq_count * local_experts
    top_count = routes.shape[1]
    capacity = 2 * tok_rows * top_count // experts
    part_cap = capacity // mp_count
    pair_count = tok_rows * top_count
    flat_ids = routes.reshape(-1)
    one_hot = (flat_ids[:, None] == jnp.arange(experts, dtype=jnp.int32)[None, :]).astype(jnp.int32)
    before = (
        jnp.arange(pair_count, dtype=jnp.int32)[:, None]
        > jnp.arange(pair_count, dtype=jnp.int32)[None, :]
    ).astype(jnp.bfloat16)
    earlier_all = jnp.dot(before, one_hot.astype(jnp.bfloat16), preferred_element_type=jnp.float32)
    earlier_count = jnp.sum(earlier_all.astype(jnp.int32) * one_hot, axis=1)
    slot_index = flat_ids * capacity + earlier_count
    slots = jnp.arange(experts * capacity, dtype=jnp.int32)
    pick = (slot_index[None, :] == slots[:, None]).reshape(experts * capacity, tok_rows, top_count)
    select = jnp.sum(pick.astype(jnp.bfloat16), axis=2)
    buffer = jnp.dot(select, residual, preferred_element_type=jnp.float32).astype(jnp.bfloat16)
    arrived = lax.all_to_all(buffer, ("seq", "mp"), 0, 0, tiled=True)
    feat = D // mp_count
    arrived_rows = (
        arrived.reshape(seq_count, mp_count, part_cap, feat)
        .transpose(0, 2, 1, 3)
        .reshape(seq_count * part_cap, D)
        .astype(jnp.float32)
    )
    moe_in = (
        arrived_rows
        * lax.rsqrt(jnp.sum(arrived_rows * arrived_rows, axis=-1, keepdims=True) / D + EPSILON)
    ).astype(jnp.bfloat16)
    w_gate = expert_all[0]
    w_up = expert_all[1]
    w_down = expert_all[2]
    gate_act = lax.dot_general(
        moe_in, w_gate, (((1,), (1,)), ((), ())), preferred_element_type=jnp.float32
    )
    up_act = lax.dot_general(
        moe_in, w_up, (((1,), (1,)), ((), ())), preferred_element_type=jnp.float32
    )
    active = (jnp.maximum(gate_act, 0.0) * up_act).astype(jnp.bfloat16)
    result = jnp.dot(active, w_down, preferred_element_type=jnp.float32).astype(jnp.bfloat16)
    outgoing = (
        result.reshape(seq_count, part_cap, mp_count, feat)
        .transpose(0, 2, 1, 3)
        .reshape(seq_count * mp_count * part_cap, feat)
    )
    returned = lax.all_to_all(outgoing, ("seq", "mp"), 0, 0, tiled=True)

    gate_weights = jax.nn.softmax(gate_logits, axis=-1)
    combine = jnp.sum(
        jnp.where(
            slot_index[:, None] == slots[None, :], gate_weights.reshape(-1)[:, None], 0.0
        ).reshape(tok_rows, top_count, experts * capacity),
        axis=1,
    )
    moe_total = jnp.dot(
        combine,
        returned.astype(jnp.float32),
        precision=lax.Precision.HIGHEST,
        preferred_element_type=jnp.float32,
    )
    return (residual_f + moe_total).astype(jnp.bfloat16)


def solution(mesh):
    return jax.shard_map(
        local,
        mesh=mesh,
        in_specs=(
            P("seq", "mp"),
            P("seq", "mp"),
            P("seq", None),
            P("mp", "seq"),
            P(),
            P("seq", None),
            P("seq", None),
            P("seq", "mp", None),
            P("seq", "mp", None),
            P("seq", "mp", None),
        ),
        out_specs=P("seq", "mp"),
        check_vma=False,
    )
```

```python
import math

import jax
import jax.numpy as jnp
from jax import lax
from jax.sharding import PartitionSpec as P

D = 1536
HQ = 12
KVH = 2
HD = 128
WINDOW = 4096


ROPE_BASE = 1500000.0
EPSILON = 1e-06


def prompt_ids(index, lengths):
    first_end = lengths[0]
    second_end = lengths[0] + lengths[1]
    prompt = (index >= first_end).astype(jnp.int32) + (index >= second_end).astype(jnp.int32)
    begin = jnp.where(index >= second_end, second_end, jnp.where(index >= first_end, first_end, 0))
    return (prompt, index - begin)


def rotary(values, position):
    half_dim = values.shape[-1] // 2
    freqs = jnp.exp(
        jnp.arange(half_dim, dtype=jnp.float32) * (-2.0 * math.log(ROPE_BASE) / values.shape[-1])
    )
    angles = position.astype(jnp.float32)[:, None] * freqs[None, :]
    cosine = jnp.cos(angles)[:, None, :]
    sine = jnp.sin(angles)[:, None, :]
    front = values[..., :half_dim]
    latter = values[..., half_dim:]
    return jnp.concatenate(
        [front * cosine - latter * sine, latter * cosine + front * sine], axis=-1
    )


def gather_seq(piece, count):
    rows = piece.shape[0]
    spread = jnp.broadcast_to(piece[None], (count,) + piece.shape).reshape(
        count * rows, piece.shape[1]
    )
    return lax.all_to_all(spread, "seq", 0, 0, tiled=True)


def local(
    hidden_in, wq, wkv, wo, lengths, routes, gate_logits, expert_gate, expert_up, expert_down
):
    tok_rows = hidden_in.shape[0]
    seq_index = lax.axis_index("seq")
    mp_index = lax.axis_index("mp")
    seq_count = lax.axis_size("seq")
    mp_count = lax.axis_size("mp")
    heads_here = wq.shape[1] // HD
    q_cols = heads_here * HD
    kv_group = mp_index * heads_here // (HQ // KVH)

    expert_all = lax.all_gather(
        jnp.concatenate([expert_gate, expert_up, expert_down], axis=0), "mp", axis=1, tiled=True
    )

    core = mp_index % 2
    kv_col = jnp.where(core == 0, kv_group * HD, KVH * HD + kv_group * HD)
    kv_cols = lax.dynamic_slice_in_dim(wkv, kv_col, HD, 1)
    w_qkv = gather_seq(jnp.concatenate([wq, kv_cols], axis=1), seq_count)

    whole = lax.all_gather(hidden_in, "mp", axis=1, tiled=True)
    whole_f = whole.astype(jnp.float32)
    normed = (
        whole_f * lax.rsqrt(jnp.sum(whole_f * whole_f, axis=-1, keepdims=True) / D + EPSILON)
    ).astype(jnp.bfloat16)
    lin = jnp.dot(normed, w_qkv, preferred_element_type=jnp.float32)
    wo_piece, lin = lax.optimization_barrier((wo.T, lin))
    wo_rows = gather_seq(wo_piece, seq_count)
    own_index = seq_index * tok_rows + jnp.arange(tok_rows, dtype=jnp.int32)
    _, own_pos = prompt_ids(own_index, lengths)
    queries = (
        rotary(lin[:, :q_cols].reshape(tok_rows, heads_here, HD), own_pos)
        .astype(jnp.bfloat16)
        .transpose(1, 0, 2)
    )
    kv_lin = lin[:, q_cols:]
    kv_mine = jnp.where(
        core == 0, rotary(kv_lin.reshape(tok_rows, 1, HD), own_pos)[:, 0, :], kv_lin
    ).astype(jnp.bfloat16)
    kv_other = lax.ppermute(kv_mine, "mp", [(m, m ^ 1) for m in range(mp_count)])
    key_own = jnp.where(core == 0, kv_mine, kv_other)
    value_own = jnp.where(core == 0, kv_other, kv_mine)
    kv_own = jnp.concatenate([key_own, value_own], axis=1)

    back = min((WINDOW - 1 + tok_rows - 1) // tok_rows, seq_count - 1)
    half = (back + 1) // 2
    fetched = []
    for j in range(half):
        pairs = []
        for s in range(seq_count):
            for m in range(mp_count):
                k = 2 * j + 1 + m % 2
                if s + k < seq_count:
                    pairs.append((s * mp_count + m, (s + k) * mp_count + m))
        fetched.append(lax.ppermute(kv_own, ("seq", "mp"), pairs))
    fetched = jnp.stack(fetched)
    partner = lax.ppermute(
        fetched, "mp", [(m, m ^ 1) for m in range(mp_count)]
    )
    odd = jnp.where(core == 0, fetched, partner)
    even = jnp.where(core == 0, partner, fetched)
    offsets = jnp.concatenate(
        [
            2 * jnp.arange(half, dtype=jnp.int32) + 1,
            2 * jnp.arange(half, dtype=jnp.int32) + 2,
            jnp.zeros((1,), jnp.int32),
        ]
    )
    kv_win = jnp.concatenate(
        [odd.reshape(-1, 2 * HD), even.reshape(-1, 2 * HD), kv_own], axis=0
    )
    key_rows = kv_win[:, :HD]
    value_rows = kv_win[:, HD:].astype(jnp.float32)
    key_index = (
        (seq_index - offsets)[:, None] * tok_rows + jnp.arange(tok_rows, dtype=jnp.int32)[None, :]
    ).reshape(-1)
    key_index = jnp.where(
        jnp.repeat(offsets, tok_rows) <= back, key_index, -1
    )

    scores = jnp.einsum(
        "hqd,kd->hqk", queries, key_rows, preferred_element_type=jnp.float32
    ) * HD ** (-0.5)
    query_prompt, _ = prompt_ids(own_index, lengths)
    key_prompt, _ = prompt_ids(key_index, lengths)
    spacing = own_index[:, None] - key_index[None, :]
    allowed = (
        (query_prompt[:, None] == key_prompt[None, :])
        & (spacing >= 0)
        & (spacing < WINDOW)
        & (key_index[None, :] >= 0)
    )[None]
    masked = jnp.where(allowed, scores, -1e30)
    peak = jnp.max(masked, axis=-1)
    probs = jnp.where(allowed, jnp.exp(masked - peak[..., None]), 0.0)
    total = jnp.sum(probs, axis=-1)
    accum = jnp.einsum("hqk,kd->hqd", probs, value_rows)
    attended = (
        (accum / total[..., None])
        .transpose(1, 0, 2)
        .reshape(tok_rows, q_cols)
        .astype(jnp.bfloat16)
    )
    partial_out = lax.dot_general(
        attended, wo_rows, (((1,), (1,)), ((), ())), preferred_element_type=jnp.float32
    )
    swapped_out = lax.all_to_all(partial_out.astype(jnp.bfloat16), "mp", 1, 0, tiled=True)
    attn_mine = jnp.sum(
        swapped_out.reshape(mp_count, tok_rows, D // mp_count).astype(jnp.float32), axis=0
    )
    residual = (hidden_in.astype(jnp.float32) + attn_mine).astype(jnp.bfloat16)
    residual_f = residual.astype(jnp.float32)

    local_experts = expert_gate.shape[0]
    experts = seq_count * local_experts
    top_count = routes.shape[1]
    capacity = 2 * tok_rows * top_count // experts
    part_cap = capacity // mp_count
    pair_count = tok_rows * top_count
    flat_ids = routes.reshape(-1)
    one_hot = (flat_ids[:, None] == jnp.arange(experts, dtype=jnp.int32)[None, :]).astype(jnp.int32)
    before = (
        jnp.arange(pair_count, dtype=jnp.int32)[:, None]
        > jnp.arange(pair_count, dtype=jnp.int32)[None, :]
    ).astype(jnp.bfloat16)
    earlier_all = jnp.dot(before, one_hot.astype(jnp.bfloat16), preferred_element_type=jnp.float32)
    earlier_count = jnp.sum(earlier_all.astype(jnp.int32) * one_hot, axis=1)
    slot_index = (
        (earlier_count // part_cap) * (experts * part_cap)
        + flat_ids * part_cap
        + earlier_count % part_cap
    )
    slots = jnp.arange(experts * capacity, dtype=jnp.int32)
    pick = (slot_index[None, :] == slots[:, None]).reshape(experts * capacity, tok_rows, top_count)
    select = jnp.sum(pick.astype(jnp.bfloat16), axis=2)
    buffer = jnp.dot(select, residual, preferred_element_type=jnp.float32).astype(jnp.bfloat16)
    arrived = lax.all_to_all(buffer, ("mp", "seq"), 0, 0, tiled=True)
    feat = D // mp_count
    arrived_q = arrived.reshape(mp_count, seq_count * part_cap, feat).astype(jnp.float32)
    square_sum = jnp.sum(jnp.sum(arrived_q * arrived_q, axis=2), axis=0)
    moe_in = (arrived_q * lax.rsqrt(square_sum / D + EPSILON)[None, :, None]).astype(jnp.bfloat16)
    w_gate = expert_all[0]
    w_up = expert_all[1]
    w_down = expert_all[2]
    gate_act = None
    up_act = None
    for q in range(mp_count):
        g = lax.dot_general(
            moe_in[q], w_gate[:, q * feat : (q + 1) * feat], (((1,), (1,)), ((), ())),
            preferred_element_type=jnp.float32,
        )
        u = lax.dot_general(
            moe_in[q], w_up[:, q * feat : (q + 1) * feat], (((1,), (1,)), ((), ())),
            preferred_element_type=jnp.float32,
        )
        gate_act = g if gate_act is None else gate_act + g
        up_act = u if up_act is None else up_act + u
    active = (jnp.maximum(gate_act, 0.0) * up_act).astype(jnp.bfloat16)
    outgoing = jnp.stack(
        [
            jnp.dot(
                active, w_down[:, q * feat : (q + 1) * feat], preferred_element_type=jnp.float32
            ).astype(jnp.bfloat16)
            for q in range(mp_count)
        ]
    ).reshape(mp_count * seq_count * part_cap, feat)
    returned = lax.all_to_all(outgoing, ("mp", "seq"), 0, 0, tiled=True)

    gate_weights = jax.nn.softmax(gate_logits, axis=-1)
    combine = jnp.sum(
        jnp.where(
            slot_index[:, None] == slots[None, :], gate_weights.reshape(-1)[:, None], 0.0
        ).reshape(tok_rows, top_count, experts * capacity),
        axis=1,
    )
    moe_total = jnp.dot(
        combine,
        returned.astype(jnp.float32),
        precision=lax.Precision.HIGHEST,
        preferred_element_type=jnp.float32,
    )
    return (residual_f + moe_total).astype(jnp.bfloat16)


def solution(mesh):
    return jax.shard_map(
        local,
        mesh=mesh,
        in_specs=(
            P("seq", "mp"),
            P("seq", "mp"),
            P("seq", None),
            P("mp", "seq"),
            P(),
            P("seq", None),
            P("seq", None),
            P("seq", "mp", None),
            P("seq", "mp", None),
            P("seq", "mp", None),
        ),
        out_specs=P("seq", "mp"),
        check_vma=False,
    )
```

```python
import math

import jax
import jax.numpy as jnp
from jax import lax
from jax.sharding import PartitionSpec as P

D = 1536
HQ = 12
KVH = 2
HD = 128
WINDOW = 4096


ROPE_BASE = 1500000.0
EPSILON = 1e-06


def prompt_ids(index, lengths):
    first_end = lengths[0]
    second_end = lengths[0] + lengths[1]
    prompt = (index >= first_end).astype(jnp.int32) + (index >= second_end).astype(jnp.int32)
    begin = jnp.where(index >= second_end, second_end, jnp.where(index >= first_end, first_end, 0))
    return (prompt, index - begin)


def rotary(values, position):
    half_dim = values.shape[-1] // 2
    freqs = jnp.exp(
        jnp.arange(half_dim, dtype=jnp.float32) * (-2.0 * math.log(ROPE_BASE) / values.shape[-1])
    )
    angles = position.astype(jnp.float32)[:, None] * freqs[None, :]
    cosine = jnp.cos(angles)[:, None, :]
    sine = jnp.sin(angles)[:, None, :]
    front = values[..., :half_dim]
    latter = values[..., half_dim:]
    return jnp.concatenate(
        [front * cosine - latter * sine, latter * cosine + front * sine], axis=-1
    )


def gather_seq(piece, count):
    rows = piece.shape[0]
    spread = jnp.broadcast_to(piece[None], (count,) + piece.shape).reshape(
        count * rows, piece.shape[1]
    )
    return lax.all_to_all(spread, "seq", 0, 0, tiled=True)


def local(
    hidden_in, wq, wkv, wo, lengths, routes, gate_logits, expert_gate, expert_up, expert_down
):
    tok_rows = hidden_in.shape[0]
    seq_index = lax.axis_index("seq")
    mp_index = lax.axis_index("mp")
    seq_count = lax.axis_size("seq")
    mp_count = lax.axis_size("mp")
    heads_here = wq.shape[1] // HD
    q_cols = heads_here * HD
    kv_group = mp_index * heads_here // (HQ // KVH)

    expert_all = lax.all_gather(
        jnp.concatenate([expert_gate, expert_up, expert_down], axis=0), "mp", axis=1, tiled=True
    )

    core = mp_index % 2
    kv_col = jnp.where(core == 0, kv_group * HD, KVH * HD + kv_group * HD)
    kv_cols = lax.dynamic_slice_in_dim(wkv, kv_col, HD, 1)
    w_qkv = gather_seq(jnp.concatenate([wq, kv_cols], axis=1), seq_count)

    whole = lax.all_gather(hidden_in, "mp", axis=1, tiled=True)
    whole_f = whole.astype(jnp.float32)
    normed = (
        whole_f * lax.rsqrt(jnp.sum(whole_f * whole_f, axis=-1, keepdims=True) / D + EPSILON)
    ).astype(jnp.bfloat16)
    lin = jnp.dot(normed, w_qkv, preferred_element_type=jnp.float32)
    wo_piece, lin = lax.optimization_barrier((wo.T, lin))
    wo_rows = gather_seq(wo_piece, seq_count)
    own_index = seq_index * tok_rows + jnp.arange(tok_rows, dtype=jnp.int32)
    _, own_pos = prompt_ids(own_index, lengths)
    queries = (
        rotary(lin[:, :q_cols].reshape(tok_rows, heads_here, HD), own_pos)
        .astype(jnp.bfloat16)
        .transpose(1, 0, 2)
    )
    kv_lin = lin[:, q_cols:]
    kv_mine = jnp.where(
        core == 0, rotary(kv_lin.reshape(tok_rows, 1, HD), own_pos)[:, 0, :], kv_lin
    ).astype(jnp.bfloat16)
    kv_other = lax.ppermute(kv_mine, "mp", [(m, m ^ 1) for m in range(mp_count)])
    key_own = jnp.where(core == 0, kv_mine, kv_other)
    value_own = jnp.where(core == 0, kv_other, kv_mine)
    kv_own = jnp.concatenate([key_own, value_own], axis=1)

    back = min((WINDOW - 1 + tok_rows - 1) // tok_rows, seq_count - 1)
    half = (back + 1) // 2
    fetched = []
    for j in range(half):
        pairs = []
        for s in range(seq_count):
            for m in range(mp_count):
                k = 2 * j + 1 + m % 2
                if s + k < seq_count:
                    pairs.append((s * mp_count + m, (s + k) * mp_count + m))
        fetched.append(lax.ppermute(kv_own, ("seq", "mp"), pairs))
    fetched = jnp.stack(fetched)
    partner = lax.ppermute(
        fetched, "mp", [(m, m ^ 1) for m in range(mp_count)]
    )
    odd = jnp.where(core == 0, fetched, partner)
    even = jnp.where(core == 0, partner, fetched)
    offsets = jnp.concatenate(
        [
            2 * jnp.arange(half, dtype=jnp.int32) + 1,
            2 * jnp.arange(half, dtype=jnp.int32) + 2,
            jnp.zeros((1,), jnp.int32),
        ]
    )
    kv_win = jnp.concatenate(
        [odd.reshape(-1, 2 * HD), even.reshape(-1, 2 * HD), kv_own], axis=0
    )
    key_rows = kv_win[:, :HD]
    value_rows = kv_win[:, HD:].astype(jnp.float32)
    key_index = (
        (seq_index - offsets)[:, None] * tok_rows + jnp.arange(tok_rows, dtype=jnp.int32)[None, :]
    ).reshape(-1)
    key_index = jnp.where(
        jnp.repeat(offsets, tok_rows) <= back, key_index, -1
    )

    scores = jnp.einsum(
        "hqd,kd->hqk", queries, key_rows, preferred_element_type=jnp.float32
    ) * HD ** (-0.5)
    query_prompt, _ = prompt_ids(own_index, lengths)
    key_prompt, _ = prompt_ids(key_index, lengths)
    spacing = own_index[:, None] - key_index[None, :]
    allowed = (
        (query_prompt[:, None] == key_prompt[None, :])
        & (spacing >= 0)
        & (spacing < WINDOW)
        & (key_index[None, :] >= 0)
    )[None]
    masked = jnp.where(allowed, scores, -1e30)
    peak = jnp.max(masked, axis=-1)
    probs = jnp.exp(masked - peak[..., None])
    total = jnp.sum(probs, axis=-1)
    accum = jnp.einsum("hqk,kd->hqd", probs, value_rows)
    attended = (
        (accum / total[..., None])
        .transpose(1, 0, 2)
        .reshape(tok_rows, q_cols)
        .astype(jnp.bfloat16)
    )
    partial_out = lax.dot_general(
        attended, wo_rows, (((1,), (1,)), ((), ())), preferred_element_type=jnp.float32
    )
    swapped_out = lax.all_to_all(partial_out.astype(jnp.bfloat16), "mp", 1, 0, tiled=True)
    attn_mine = jnp.sum(
        swapped_out.reshape(mp_count, tok_rows, D // mp_count).astype(jnp.float32), axis=0
    )
    residual = (hidden_in.astype(jnp.float32) + attn_mine).astype(jnp.bfloat16)
    residual_f = residual.astype(jnp.float32)

    local_experts = expert_gate.shape[0]
    experts = seq_count * local_experts
    top_count = routes.shape[1]
    capacity = 2 * tok_rows * top_count // experts
    part_cap = capacity // mp_count
    pair_count = tok_rows * top_count
    flat_ids = routes.reshape(-1)
    one_hot = (flat_ids[:, None] == jnp.arange(experts, dtype=jnp.int32)[None, :]).astype(jnp.int32)
    before = (
        jnp.arange(pair_count, dtype=jnp.int32)[:, None]
        > jnp.arange(pair_count, dtype=jnp.int32)[None, :]
    ).astype(jnp.bfloat16)
    earlier_all = jnp.dot(before, one_hot.astype(jnp.bfloat16), preferred_element_type=jnp.float32)
    earlier_count = jnp.sum(earlier_all.astype(jnp.int32) * one_hot, axis=1)
    slot_index = (
        (earlier_count // part_cap) * (experts * part_cap)
        + flat_ids * part_cap
        + earlier_count % part_cap
    )
    slots = jnp.arange(experts * capacity, dtype=jnp.int32)
    pick = (slot_index[None, :] == slots[:, None]).reshape(experts * capacity, tok_rows, top_count)
    select = jnp.sum(pick.astype(jnp.bfloat16), axis=2)
    buffer = jnp.dot(select, residual, preferred_element_type=jnp.float32).astype(jnp.bfloat16)
    arrived = lax.all_to_all(buffer, ("mp", "seq"), 0, 0, tiled=True)
    feat = D // mp_count
    arrived_q = arrived.reshape(mp_count, seq_count * part_cap, feat).astype(jnp.float32)
    square_sum = jnp.sum(jnp.sum(arrived_q * arrived_q, axis=2), axis=0)
    moe_in = (arrived_q * lax.rsqrt(square_sum / D + EPSILON)[None, :, None]).astype(jnp.bfloat16)
    w_gate = expert_all[0]
    w_up = expert_all[1]
    w_down = expert_all[2]
    gate_act = None
    up_act = None
    for q in range(mp_count):
        g = lax.dot_general(
            moe_in[q], w_gate[:, q * feat : (q + 1) * feat], (((1,), (1,)), ((), ())),
            preferred_element_type=jnp.float32,
        )
        u = lax.dot_general(
            moe_in[q], w_up[:, q * feat : (q + 1) * feat], (((1,), (1,)), ((), ())),
            preferred_element_type=jnp.float32,
        )
        gate_act = g if gate_act is None else gate_act + g
        up_act = u if up_act is None else up_act + u
    active = (jnp.maximum(gate_act, 0.0) * up_act).astype(jnp.bfloat16)
    outgoing = jnp.stack(
        [
            jnp.dot(
                active, w_down[:, q * feat : (q + 1) * feat], preferred_element_type=jnp.float32
            ).astype(jnp.bfloat16)
            for q in range(mp_count)
        ]
    ).reshape(mp_count * seq_count * part_cap, feat)
    returned = lax.all_to_all(outgoing, ("mp", "seq"), 0, 0, tiled=True)

    gate_weights = jax.nn.softmax(gate_logits, axis=-1)
    combine = jnp.sum(
        jnp.where(
            slot_index[:, None] == slots[None, :], gate_weights.reshape(-1)[:, None], 0.0
        ).reshape(tok_rows, top_count, experts * capacity),
        axis=1,
    )
    combine_hi = combine.astype(jnp.bfloat16)
    combine_lo = (combine - combine_hi.astype(jnp.float32)).astype(jnp.bfloat16)
    moe_total = jnp.dot(combine_hi, returned, preferred_element_type=jnp.float32) + jnp.dot(
        combine_lo, returned, preferred_element_type=jnp.float32
    )
    return (residual_f + moe_total).astype(jnp.bfloat16)


def solution(mesh):
    return jax.shard_map(
        local,
        mesh=mesh,
        in_specs=(
            P("seq", "mp"),
            P("seq", "mp"),
            P("seq", None),
            P("mp", "seq"),
            P(),
            P("seq", None),
            P("seq", None),
            P("seq", "mp", None),
            P("seq", "mp", None),
            P("seq", "mp", None),
        ),
        out_specs=P("seq", "mp"),
        check_vma=False,
    )
```

```python
import math

import jax
import jax.numpy as jnp
from jax import lax
from jax.sharding import PartitionSpec as P

D = 1536
HQ = 12
KVH = 2
HD = 128
WINDOW = 4096


ROPE_BASE = 1500000.0
EPSILON = 1e-06


def prompt_ids(index, lengths):
    first_end = lengths[0]
    second_end = lengths[0] + lengths[1]
    prompt = (index >= first_end).astype(jnp.int32) + (index >= second_end).astype(jnp.int32)
    begin = jnp.where(index >= second_end, second_end, jnp.where(index >= first_end, first_end, 0))
    return (prompt, index - begin)


def rotary(values, position):
    half_dim = values.shape[-1] // 2
    freqs = jnp.exp(
        jnp.arange(half_dim, dtype=jnp.float32) * (-2.0 * math.log(ROPE_BASE) / values.shape[-1])
    )
    angles = position.astype(jnp.float32)[:, None] * freqs[None, :]
    cosine = jnp.cos(angles)[:, None, :]
    sine = jnp.sin(angles)[:, None, :]
    front = values[..., :half_dim]
    latter = values[..., half_dim:]
    return jnp.concatenate(
        [front * cosine - latter * sine, latter * cosine + front * sine], axis=-1
    )


def gather_seq(piece, count):
    rows = piece.shape[0]
    spread = jnp.broadcast_to(piece[None], (count,) + piece.shape).reshape(
        count * rows, piece.shape[1]
    )
    return lax.all_to_all(spread, "seq", 0, 0, tiled=True)


def local(
    hidden_in, wq, wkv, wo, lengths, routes, gate_logits, expert_gate, expert_up, expert_down
):
    tok_rows = hidden_in.shape[0]
    seq_index = lax.axis_index("seq")
    mp_index = lax.axis_index("mp")
    seq_count = lax.axis_size("seq")
    mp_count = lax.axis_size("mp")
    heads_here = wq.shape[1] // HD
    q_cols = heads_here * HD
    kv_group = mp_index * heads_here // (HQ // KVH)

    expert_all = lax.all_gather(
        jnp.concatenate([expert_gate, expert_up, expert_down], axis=0), "mp", axis=1, tiled=True
    )

    core = mp_index % 2
    kv_col = jnp.where(core == 0, kv_group * HD, KVH * HD + kv_group * HD)
    kv_cols = lax.dynamic_slice_in_dim(wkv, kv_col, HD, 1)
    w_qkv = gather_seq(jnp.concatenate([wq, kv_cols], axis=1), seq_count)

    whole = lax.all_gather(hidden_in, "mp", axis=1, tiled=True)
    whole_f = whole.astype(jnp.float32)
    normed = (
        whole_f * lax.rsqrt(jnp.sum(whole_f * whole_f, axis=-1, keepdims=True) / D + EPSILON)
    ).astype(jnp.bfloat16)
    lin = jnp.dot(normed, w_qkv, preferred_element_type=jnp.float32)
    wo_piece, lin = lax.optimization_barrier((wo.T, lin))
    wo_rows = gather_seq(wo_piece, seq_count)
    own_index = seq_index * tok_rows + jnp.arange(tok_rows, dtype=jnp.int32)
    _, own_pos = prompt_ids(own_index, lengths)
    queries = (
        rotary(lin[:, :q_cols].reshape(tok_rows, heads_here, HD), own_pos)
        .astype(jnp.bfloat16)
        .transpose(1, 0, 2)
    )
    kv_lin = lin[:, q_cols:]
    kv_mine = jnp.where(
        core == 0, rotary(kv_lin.reshape(tok_rows, 1, HD), own_pos)[:, 0, :], kv_lin
    ).astype(jnp.bfloat16)
    kv_other = lax.ppermute(kv_mine, "mp", [(m, m ^ 1) for m in range(mp_count)])
    key_own = jnp.where(core == 0, kv_mine, kv_other)
    value_own = jnp.where(core == 0, kv_other, kv_mine)
    kv_own = jnp.concatenate([key_own, value_own], axis=1)

    back = min((WINDOW - 1 + tok_rows - 1) // tok_rows, seq_count - 1)
    half = (back + 1) // 2
    fetched = []
    for j in range(half):
        pairs = []
        for s in range(seq_count):
            for m in range(mp_count):
                k = 2 * j + 1 + m % 2
                if s + k < seq_count:
                    pairs.append((s * mp_count + m, (s + k) * mp_count + m))
        fetched.append(lax.ppermute(kv_own, ("seq", "mp"), pairs))
    fetched = jnp.stack(fetched)
    partner = lax.ppermute(
        fetched, "mp", [(m, m ^ 1) for m in range(mp_count)]
    )
    odd = jnp.where(core == 0, fetched, partner)
    even = jnp.where(core == 0, partner, fetched)
    offsets = jnp.concatenate(
        [
            2 * jnp.arange(half, dtype=jnp.int32) + 1,
            2 * jnp.arange(half, dtype=jnp.int32) + 2,
            jnp.zeros((1,), jnp.int32),
        ]
    )
    kv_win = jnp.concatenate(
        [odd.reshape(-1, 2 * HD), even.reshape(-1, 2 * HD), kv_own], axis=0
    )
    key_rows = kv_win[:, :HD]
    value_rows = kv_win[:, HD:].astype(jnp.float32)
    key_index = (
        (seq_index - offsets)[:, None] * tok_rows + jnp.arange(tok_rows, dtype=jnp.int32)[None, :]
    ).reshape(-1)
    key_index = jnp.where(
        jnp.repeat(offsets, tok_rows) <= back, key_index, -1
    )

    scores = jnp.einsum(
        "hqd,kd->hqk", queries, key_rows, preferred_element_type=jnp.float32
    ) * HD ** (-0.5)
    query_prompt, _ = prompt_ids(own_index, lengths)
    key_prompt, _ = prompt_ids(key_index, lengths)
    spacing = own_index[:, None] - key_index[None, :]
    allowed = (
        (query_prompt[:, None] == key_prompt[None, :])
        & (spacing >= 0)
        & (spacing < WINDOW)
        & (key_index[None, :] >= 0)
    )[None]
    masked = jnp.where(allowed, scores, -1e30)
    peak = jnp.max(masked, axis=-1)
    probs = jnp.where(allowed, jnp.exp(masked - peak[..., None]), 0.0)
    total = jnp.sum(probs, axis=-1)
    accum = jnp.einsum("hqk,kd->hqd", probs, value_rows)
    attended = (
        (accum / total[..., None])
        .transpose(1, 0, 2)
        .reshape(tok_rows, q_cols)
        .astype(jnp.bfloat16)
    )
    partial_out = lax.dot_general(
        attended, wo_rows, (((1,), (1,)), ((), ())), preferred_element_type=jnp.float32
    )
    swapped_out = lax.all_to_all(partial_out.astype(jnp.bfloat16), "mp", 1, 0, tiled=True)
    attn_mine = jnp.sum(
        swapped_out.reshape(mp_count, tok_rows, D // mp_count).astype(jnp.float32), axis=0
    )
    residual = (hidden_in.astype(jnp.float32) + attn_mine).astype(jnp.bfloat16)
    residual_f = residual.astype(jnp.float32)

    local_experts = expert_gate.shape[0]
    experts = seq_count * local_experts
    top_count = routes.shape[1]
    capacity = 2 * tok_rows * top_count // experts
    part_cap = capacity // mp_count
    pair_count = tok_rows * top_count
    flat_ids = routes.reshape(-1)
    one_hot = (flat_ids[:, None] == jnp.arange(experts, dtype=jnp.int32)[None, :]).astype(jnp.int32)
    before = (
        jnp.arange(pair_count, dtype=jnp.int32)[:, None]
        > jnp.arange(pair_count, dtype=jnp.int32)[None, :]
    ).astype(jnp.bfloat16)
    earlier_all = jnp.dot(before, one_hot.astype(jnp.bfloat16), preferred_element_type=jnp.float32)
    earlier_count = jnp.sum(earlier_all.astype(jnp.int32) * one_hot, axis=1)
    slot_index = (
        (earlier_count // part_cap) * (experts * part_cap)
        + flat_ids * part_cap
        + earlier_count % part_cap
    )
    slots = jnp.arange(experts * capacity, dtype=jnp.int32)
    pick = (slot_index[None, :] == slots[:, None]).reshape(experts * capacity, tok_rows, top_count)
    select = jnp.sum(pick.astype(jnp.bfloat16), axis=2)
    buffer = jnp.dot(select, residual, preferred_element_type=jnp.float32).astype(jnp.bfloat16)
    arrived = lax.all_to_all(buffer, ("mp", "seq"), 0, 0, tiled=True)
    feat = D // mp_count
    arrived_q = arrived.reshape(mp_count, seq_count * part_cap, feat).astype(jnp.float32)
    square_sum = jnp.sum(jnp.sum(arrived_q * arrived_q, axis=2), axis=0)
    moe_in = (arrived_q * lax.rsqrt(square_sum / D + EPSILON)[None, :, None]).astype(jnp.bfloat16)
    w_gate = expert_all[0]
    w_up = expert_all[1]
    w_down = expert_all[2]
    hidden_units = w_gate.shape[0]
    w_gate_up = expert_all[:2].reshape(2 * hidden_units, D)
    both = None
    for q in range(mp_count):
        part = lax.dot_general(
            moe_in[q], w_gate_up[:, q * feat : (q + 1) * feat], (((1,), (1,)), ((), ())),
            preferred_element_type=jnp.float32,
        )
        both = part if both is None else both + part
    gate_act = both[:, :hidden_units]
    up_act = both[:, hidden_units:]
    active = (jnp.maximum(gate_act, 0.0) * up_act).astype(jnp.bfloat16)
    outgoing = jnp.stack(
        [
            jnp.dot(
                active, w_down[:, q * feat : (q + 1) * feat], preferred_element_type=jnp.float32
            ).astype(jnp.bfloat16)
            for q in range(mp_count)
        ]
    ).reshape(mp_count * seq_count * part_cap, feat)
    returned = lax.all_to_all(outgoing, ("mp", "seq"), 0, 0, tiled=True)

    gate_weights = jax.nn.softmax(gate_logits, axis=-1)
    combine = jnp.sum(
        jnp.where(
            slot_index[:, None] == slots[None, :], gate_weights.reshape(-1)[:, None], 0.0
        ).reshape(tok_rows, top_count, experts * capacity),
        axis=1,
    )
    moe_total = jnp.dot(
        combine,
        returned.astype(jnp.float32),
        precision=lax.Precision.HIGHEST,
        preferred_element_type=jnp.float32,
    )
    return (residual_f + moe_total).astype(jnp.bfloat16)


def solution(mesh):
    return jax.shard_map(
        local,
        mesh=mesh,
        in_specs=(
            P("seq", "mp"),
            P("seq", "mp"),
            P("seq", None),
            P("mp", "seq"),
            P(),
            P("seq", None),
            P("seq", None),
            P("seq", "mp", None),
            P("seq", "mp", None),
            P("seq", "mp", None),
        ),
        out_specs=P("seq", "mp"),
        check_vma=False,
    )
```

```python
import math

import jax
import jax.numpy as jnp
from jax import lax
from jax.sharding import PartitionSpec as P

D = 1536
HQ = 12
KVH = 2
HD = 128
WINDOW = 4096


ROPE_BASE = 1500000.0
EPSILON = 1e-06


def prompt_ids(index, lengths):
    first_end = lengths[0]
    second_end = lengths[0] + lengths[1]
    prompt = (index >= first_end).astype(jnp.int32) + (index >= second_end).astype(jnp.int32)
    begin = jnp.where(index >= second_end, second_end, jnp.where(index >= first_end, first_end, 0))
    return (prompt, index - begin)


def rotary(values, position):
    half_dim = values.shape[-1] // 2
    freqs = jnp.exp(
        jnp.arange(half_dim, dtype=jnp.float32) * (-2.0 * math.log(ROPE_BASE) / values.shape[-1])
    )
    angles = position.astype(jnp.float32)[:, None] * freqs[None, :]
    cosine = jnp.cos(angles)[:, None, :]
    sine = jnp.sin(angles)[:, None, :]
    front = values[..., :half_dim]
    latter = values[..., half_dim:]
    return jnp.concatenate(
        [front * cosine - latter * sine, latter * cosine + front * sine], axis=-1
    )


def gather_seq(piece, count):
    rows = piece.shape[0]
    spread = jnp.broadcast_to(piece[None], (count,) + piece.shape).reshape(
        count * rows, piece.shape[1]
    )
    return lax.all_to_all(spread, "seq", 0, 0, tiled=True)


def local(
    hidden_in, wq, wkv, wo, lengths, routes, gate_logits, expert_gate, expert_up, expert_down
):
    tok_rows = hidden_in.shape[0]
    seq_index = lax.axis_index("seq")
    mp_index = lax.axis_index("mp")
    seq_count = lax.axis_size("seq")
    mp_count = lax.axis_size("mp")
    heads_here = wq.shape[1] // HD
    q_cols = heads_here * HD
    kv_group = mp_index * heads_here // (HQ // KVH)

    expert_all = lax.all_gather(
        jnp.concatenate([expert_gate, expert_up, expert_down], axis=0), "mp", axis=1, tiled=True
    )

    core = mp_index % 2
    kv_col = jnp.where(core == 0, kv_group * HD, KVH * HD + kv_group * HD)
    kv_cols = lax.dynamic_slice_in_dim(wkv, kv_col, HD, 1)
    w_qkv = gather_seq(jnp.concatenate([wq, kv_cols], axis=1), seq_count)

    whole = lax.all_to_all(
        jnp.broadcast_to(hidden_in[None], (mp_count,) + hidden_in.shape), "mp", 0, 2, tiled=True
    ).reshape(tok_rows, D)
    whole_f = whole.astype(jnp.float32)
    normed = (
        whole_f * lax.rsqrt(jnp.sum(whole_f * whole_f, axis=-1, keepdims=True) / D + EPSILON)
    ).astype(jnp.bfloat16)
    lin = jnp.dot(normed, w_qkv, preferred_element_type=jnp.float32)
    wo_piece, lin = lax.optimization_barrier((wo.T, lin))
    wo_rows = gather_seq(wo_piece, seq_count)
    own_index = seq_index * tok_rows + jnp.arange(tok_rows, dtype=jnp.int32)
    _, own_pos = prompt_ids(own_index, lengths)
    queries = (
        rotary(lin[:, :q_cols].reshape(tok_rows, heads_here, HD), own_pos)
        .astype(jnp.bfloat16)
        .transpose(1, 0, 2)
    )
    kv_lin = lin[:, q_cols:]
    kv_mine = jnp.where(
        core == 0, rotary(kv_lin.reshape(tok_rows, 1, HD), own_pos)[:, 0, :], kv_lin
    ).astype(jnp.bfloat16)
    kv_other = lax.ppermute(kv_mine, "mp", [(m, m ^ 1) for m in range(mp_count)])
    key_own = jnp.where(core == 0, kv_mine, kv_other)
    value_own = jnp.where(core == 0, kv_other, kv_mine)
    kv_own = jnp.concatenate([key_own, value_own], axis=1)

    back = min((WINDOW - 1 + tok_rows - 1) // tok_rows, seq_count - 1)
    half = (back + 1) // 2
    fetched = []
    for j in range(half):
        pairs = []
        for s in range(seq_count):
            for m in range(mp_count):
                k = 2 * j + 1 + m % 2
                if s + k < seq_count:
                    pairs.append((s * mp_count + m, (s + k) * mp_count + m))
        fetched.append(lax.ppermute(kv_own, ("seq", "mp"), pairs))
    fetched = jnp.stack(fetched)
    partner = lax.ppermute(
        fetched, "mp", [(m, m ^ 1) for m in range(mp_count)]
    )
    odd = jnp.where(core == 0, fetched, partner)
    even = jnp.where(core == 0, partner, fetched)
    offsets = jnp.concatenate(
        [
            2 * jnp.arange(half, dtype=jnp.int32) + 1,
            2 * jnp.arange(half, dtype=jnp.int32) + 2,
            jnp.zeros((1,), jnp.int32),
        ]
    )
    kv_win = jnp.concatenate(
        [odd.reshape(-1, 2 * HD), even.reshape(-1, 2 * HD), kv_own], axis=0
    )
    key_rows = kv_win[:, :HD]
    value_rows = kv_win[:, HD:].astype(jnp.float32)
    key_index = (
        (seq_index - offsets)[:, None] * tok_rows + jnp.arange(tok_rows, dtype=jnp.int32)[None, :]
    ).reshape(-1)
    key_index = jnp.where(
        jnp.repeat(offsets, tok_rows) <= back, key_index, -1
    )

    scores = jnp.einsum(
        "hqd,kd->hqk", queries, key_rows, preferred_element_type=jnp.float32
    ) * HD ** (-0.5)
    query_prompt, _ = prompt_ids(own_index, lengths)
    key_prompt, _ = prompt_ids(key_index, lengths)
    spacing = own_index[:, None] - key_index[None, :]
    allowed = (
        (query_prompt[:, None] == key_prompt[None, :])
        & (spacing >= 0)
        & (spacing < WINDOW)
        & (key_index[None, :] >= 0)
    )[None]
    masked = jnp.where(allowed, scores, -1e30)
    peak = jnp.max(masked, axis=-1)
    probs = jnp.where(allowed, jnp.exp(masked - peak[..., None]), 0.0)
    total = jnp.sum(probs, axis=-1)
    accum = jnp.einsum("hqk,kd->hqd", probs, value_rows)
    attended = (
        (accum / total[..., None])
        .transpose(1, 0, 2)
        .reshape(tok_rows, q_cols)
        .astype(jnp.bfloat16)
    )
    partial_out = lax.dot_general(
        attended, wo_rows, (((1,), (1,)), ((), ())), preferred_element_type=jnp.float32
    )
    swapped_out = lax.all_to_all(partial_out.astype(jnp.bfloat16), "mp", 1, 0, tiled=True)
    attn_mine = jnp.sum(
        swapped_out.reshape(mp_count, tok_rows, D // mp_count).astype(jnp.float32), axis=0
    )
    residual = (hidden_in.astype(jnp.float32) + attn_mine).astype(jnp.bfloat16)
    residual_f = residual.astype(jnp.float32)

    local_experts = expert_gate.shape[0]
    experts = seq_count * local_experts
    top_count = routes.shape[1]
    capacity = 2 * tok_rows * top_count // experts
    part_cap = capacity // mp_count
    pair_count = tok_rows * top_count
    flat_ids = routes.reshape(-1)
    one_hot = (flat_ids[:, None] == jnp.arange(experts, dtype=jnp.int32)[None, :]).astype(jnp.int32)
    before = (
        jnp.arange(pair_count, dtype=jnp.int32)[:, None]
        > jnp.arange(pair_count, dtype=jnp.int32)[None, :]
    ).astype(jnp.bfloat16)
    earlier_all = jnp.dot(before, one_hot.astype(jnp.bfloat16), preferred_element_type=jnp.float32)
    earlier_count = jnp.sum(earlier_all.astype(jnp.int32) * one_hot, axis=1)
    slot_index = (
        (earlier_count // part_cap) * (experts * part_cap)
        + flat_ids * part_cap
        + earlier_count % part_cap
    )
    slots = jnp.arange(experts * capacity, dtype=jnp.int32)
    pick = (slot_index[None, :] == slots[:, None]).reshape(experts * capacity, tok_rows, top_count)
    select = jnp.sum(pick.astype(jnp.bfloat16), axis=2)
    buffer = jnp.dot(select, residual, preferred_element_type=jnp.float32).astype(jnp.bfloat16)
    arrived = lax.all_to_all(buffer, ("mp", "seq"), 0, 0, tiled=True)
    feat = D // mp_count
    arrived_q = arrived.reshape(mp_count, seq_count * part_cap, feat).astype(jnp.float32)
    square_sum = jnp.sum(jnp.sum(arrived_q * arrived_q, axis=2), axis=0)
    moe_in = (arrived_q * lax.rsqrt(square_sum / D + EPSILON)[None, :, None]).astype(jnp.bfloat16)
    w_gate = expert_all[0]
    w_up = expert_all[1]
    w_down = expert_all[2]
    gate_act = None
    up_act = None
    for q in range(mp_count):
        g = lax.dot_general(
            moe_in[q], w_gate[:, q * feat : (q + 1) * feat], (((1,), (1,)), ((), ())),
            preferred_element_type=jnp.float32,
        )
        u = lax.dot_general(
            moe_in[q], w_up[:, q * feat : (q + 1) * feat], (((1,), (1,)), ((), ())),
            preferred_element_type=jnp.float32,
        )
        gate_act = g if gate_act is None else gate_act + g
        up_act = u if up_act is None else up_act + u
    active = (jnp.maximum(gate_act, 0.0) * up_act).astype(jnp.bfloat16)
    outgoing = jnp.stack(
        [
            jnp.dot(
                active, w_down[:, q * feat : (q + 1) * feat], preferred_element_type=jnp.float32
            ).astype(jnp.bfloat16)
            for q in range(mp_count)
        ]
    ).reshape(mp_count * seq_count * part_cap, feat)
    returned = lax.all_to_all(outgoing, ("mp", "seq"), 0, 0, tiled=True)

    gate_weights = jax.nn.softmax(gate_logits, axis=-1)
    combine = jnp.sum(
        jnp.where(
            slot_index[:, None] == slots[None, :], gate_weights.reshape(-1)[:, None], 0.0
        ).reshape(tok_rows, top_count, experts * capacity),
        axis=1,
    )
    moe_total = jnp.dot(
        combine,
        returned.astype(jnp.float32),
        precision=lax.Precision.HIGHEST,
        preferred_element_type=jnp.float32,
    )
    return (residual_f + moe_total).astype(jnp.bfloat16)


def solution(mesh):
    return jax.shard_map(
        local,
        mesh=mesh,
        in_specs=(
            P("seq", "mp"),
            P("seq", "mp"),
            P("seq", None),
            P("mp", "seq"),
            P(),
            P("seq", None),
            P("seq", None),
            P("seq", "mp", None),
            P("seq", "mp", None),
            P("seq", "mp", None),
        ),
        out_specs=P("seq", "mp"),
        check_vma=False,
    )
```
